512 devices in a mesh: req: 4 (over x), exp: 8 (over z), shard: 16 (over y, core).
Axes of the slice: x: 4, y: 8, z: 8, core: 2. Of those that a mesh axis runs over, the one named last changes fastest.
Arguments:
- query_stretch: bfloat16 [8, 128, 2304], P('req', 'exp'), may hold values from -8 to 8
- resid_stretch: bfloat16 [8, 128, 2304], P('req', 'exp'), may hold values from -30 to 30
- route_ids: int32 [8, 128, 2], P('req', 'exp'), may hold values from 0 to 7, all different within a row; in each aligned block of 16 rows (0 to 15, 16 to 31, ..., all dimensions but the last counted through in order) at most 6 rows name the same one
- route_probs: bfloat16 [8, 128, 2], P('req', 'exp'), may hold values from 0.19921875 to 1
- request_order: int32 [8], replicated, may hold values from 0 to 7, each once
- prior_pages: int32 [4, 2], P('req'), may hold values from 63 to 189, as said below
- page_order: int32 [4, 256], P('req'), may hold values from 0 to 255, each once within a row
- key_pool: bfloat16 [4, 256, 64, 2304], P('req', ('exp', 'shard')), may hold values from -8 to 8
- value_pool: bfloat16 [4, 256, 64, 2304], P('req', ('exp', 'shard')), may hold values from -6 to 6
- norm_gain: float32 [2304], replicated, may hold values from 0.4 to 2.5
- out_proj: bfloat16 [2304, 2304], P('shard'), may hold values from -0.125 to 0.125
- gate_up: bfloat16 [8, 2, 2880, 2304], P('exp', None, 'shard'), may hold values from -0.125 to 0.125
- down_proj: bfloat16 [8, 2880, 2304], P('exp', 'shard'), may hold values from -0.109375 to 0.109375
Outputs:
- mixed_out: bfloat16 [8, 128, 2304], P('req', 'exp')
The draws below stay inside these ranges and needn't reach their ends.
Inputs may be any that keep to these rules, and one draw needn't show every extreme that they name: `route_ids`: each row names 2 different experts. In each aligned block of 16 rows (one request's tokens b * 16 to (b + 1) * 16 - 1) no expert is named by more than 6 rows, a bound that some block reaches. `request_order`: A permutation of the requests. `prior_pages`: in each group the 2 counts sum to 252, so that the pool is full; one member of every group has exactly 189. `page_order`: each row is a permutation of the group's pool pages.
All inputs are finite; a program needn't handle non-finite values.
Results may differ from the reference program's by a relative error of at most 0.02.
Values may be sent and summed in bfloat16 or wider, within the bound.
No kernel may reach another device: no remote copies, remote signals or barrier semaphores. Data moves between devices by JAX's collectives and lax.ppermute only.
A program may use at most 64 MiB of HBM per device.

```python
import math
import jax
import jax.numpy as jnp
import numpy as np
from jax import lax

D = 2304
H = 36
FF = 2880
TOPK = 2
STRETCH = 128
REQ_GRP = 2
PAGE = 64
HD = 64
EXPERTS = 8
GROUPS = 4
REQS = 8
TOK_EXP = 16
PAGES_POOL = 256
STRETCH_PAGES = 2
PRIOR_TOTAL = 252
PRIOR_MOST = 189
MOST = 6


def draw_query_stretch(key, part):
    row_count = REQS * STRETCH
    base_draw = 2.6 * jax.random.normal(jax.random.fold_in(key, 1), (row_count, D), jnp.float32)
    return jnp.clip(base_draw, -8.0, 8.0).reshape(REQS, STRETCH, D).astype(jnp.bfloat16)


def draw_key_pool(key, part):
    row_count = GROUPS * PAGES_POOL * PAGE
    base_draw = 1.25 * jax.random.normal(jax.random.fold_in(key, 2), (row_count, D), jnp.float32)
    return jnp.clip(base_draw, -8.0, 8.0).reshape(GROUPS, PAGES_POOL, PAGE, D).astype(jnp.bfloat16)


def draw_resid_stretch(key, part):
    row_count = REQS * STRETCH
    row_scale = jnp.exp(jax.random.uniform(jax.random.fold_in(key, 11), (row_count, 1), jnp.float32, math.log(0.08), math.log(0.8)))
    col_scale = jnp.exp(jax.random.uniform(jax.random.fold_in(key, 12), (1, D), jnp.float32, math.log(0.3), math.log(3.0)))
    noise_draw = jax.random.normal(jax.random.fold_in(key, 13), (row_count, D), jnp.float32)
    return jnp.clip(row_scale * col_scale * noise_draw, -30.0, 30.0).reshape(REQS, STRETCH, D).astype(jnp.bfloat16)


def draw_prior_pages(key, part):
    remain = PRIOR_TOTAL - PRIOR_MOST
    others = REQ_GRP - 1
    base_count = remain // others
    index_row = jnp.arange(REQ_GRP, dtype=jnp.int32)
    counts_row = jnp.where(index_row == 0, PRIOR_MOST, base_count)
    counts_row = jnp.where(index_row == REQ_GRP - 1, remain - base_count * (others - 1), counts_row)
    counts_row = jnp.where(index_row == 0, PRIOR_MOST, counts_row).astype(jnp.int32)
    group_keys = jax.random.split(jax.random.fold_in(key, 4242), GROUPS)
    placed = jax.vmap(lambda group_key: jax.random.permutation(group_key, counts_row))(group_keys)
    return placed.astype(jnp.int32)


def steps_of(stream_key, shape, pieces, least, top_value):
    factor_of, own = 1.0, jax.random.fold_in(stream_key, 6)
    for dim, parts in pieces:
        steps = jnp.exp(jax.random.uniform(jax.random.fold_in(own, dim), (parts,), jnp.float32, least / len(pieces), top_value / len(pieces)))
        factor_of = factor_of * jnp.repeat(steps, shape[dim] // parts).reshape([-1 if axis == dim else 1 for axis in range(len(shape))])
    return factor_of


def routed_block(own_key, own, number, rows, count, top, most, lean):
    order = jax.random.permutation(own_key, count)
    crowded, common = load_shares(count, rows * top, most, lean, True), load_shares(count, rows * top, most, lean, False)
    places = jnp.arange(count)

    def named(tallies, rotation):
        used = int((tallies > 0).sum())
        fixed = max(1, used // 4)
        passed = fixed + (places - fixed + rotation * (used - fixed)) % max(1, count - fixed)
        return jnp.zeros((count,), jnp.int32).at[order[jnp.where(places < fixed, places, passed)]].set(jnp.asarray(tallies, jnp.int32))

    tallies = jnp.where(number % 4 == 0, named(crowded, number // 4), named(common, number - number // 4 - 1))
    mixed = jax.random.permutation(jax.random.fold_in(own, 3), count)
    giver, sink = mixed[0:count // 2 * 2:2], mixed[1:count // 2 * 2:2]
    room = jnp.minimum(tallies[giver] - 1, most - tallies[sink]) // 2
    room = jnp.where((giver == order[0]) | (sink == order[0]) | (tallies[sink] == 0), 0, jnp.maximum(room, 0))
    passed = jax.random.randint(jax.random.fold_in(own, 4), (count // 2,), 0, 1 << 20) % (room + 1)
    tallies = tallies.at[giver].add(-passed).at[sink].add(passed)
    members = jnp.searchsorted(jnp.cumsum(tallies), jnp.arange(rows * top), side="right").astype(jnp.int32)
    listing = members.reshape(top, rows).T
    listing = listing[jax.random.permutation(jax.random.fold_in(own, 1), rows)]
    rotation = jax.random.randint(jax.random.fold_in(own, 2), (rows, 1), 0, top)
    return jnp.take_along_axis(listing, (jnp.arange(top)[None, :] + rotation) % top, axis=1)


def load_shares(number_of, total, most, skew, full):
    loads = [(1 << 20) // math.isqrt(grade ** skew) + 1 for grade in range(1, number_of + 1)]
    largest = most if full else min(most, max(-(-total // number_of), total * loads[0] // sum(loads)))
    least = 1 if total - largest >= number_of - 1 else 0
    holding, surplus = [largest] + [least] * (number_of - 1), total - largest - least * (number_of - 1)
    while surplus > 0:
        free = [i for i in range(1, number_of) if holding[i] < largest] or [i for i in range(1, number_of) if holding[i] < most]
        whole, remaining = sum([loads[i] for i in free]), surplus
        for i in free:
            more = min(most - holding[i], max(1, remaining * loads[i] // whole), surplus)
            holding[i] = holding[i] + more
            surplus = surplus - more
    return np.array(holding)


def bell_draw(key, extent, spread, most, cuts=(), kind=jnp.bfloat16):
    array = spread * jax.random.normal(key, extent, jnp.float32)
    if cuts:
        array = array * steps_of(key, extent, cuts, -0.22, 0.18)
    return jnp.clip(array, -most, most).astype(kind)


def setup_inputs(seed: int = 0) -> dict:
    streams_of = jax.random.split(jax.random.key(seed), 14)
    query_stretch = draw_query_stretch(jax.random.fold_in(streams_of[13], 71), 0)
    resid_stretch = draw_resid_stretch(jax.random.fold_in(streams_of[13], 71), 0)
    route_ids_keys = jax.random.split(jax.random.fold_in(streams_of[2], 1), REQS * STRETCH // TOK_EXP)
    route_ids_turns = jax.random.permutation(jax.random.fold_in(streams_of[2], 3), REQS * STRETCH // TOK_EXP)
    route_ids = jax.vmap(lambda own, number: routed_block(jax.random.fold_in(streams_of[2], 2), own, number, TOK_EXP, EXPERTS, TOPK, MOST, 2))(route_ids_keys, route_ids_turns).reshape((REQS, STRETCH, TOPK))
    route_probs = jnp.clip(0.19921875 + 0.80078125 * jax.random.uniform(streams_of[3], (REQS, STRETCH, TOPK), jnp.float32) ** steps_of(streams_of[3], (REQS, STRETCH, TOPK), ((0, 4), (1, 8)), -0.2, 0.2), 0.19921875, 1.0).astype(jnp.bfloat16)
    request_order = jax.random.permutation(streams_of[4], REQS).astype(jnp.int32)
    prior_pages = draw_prior_pages(jax.random.fold_in(streams_of[13], 71), 0)
    page_order = jax.vmap(lambda own: jax.random.permutation(own, PAGES_POOL))(jax.random.split(streams_of[6], GROUPS)).reshape((GROUPS, PAGES_POOL)).astype(jnp.int32)
    key_pool = draw_key_pool(jax.random.fold_in(streams_of[13], 71), 0)
    value_pool = bell_draw(streams_of[8], (GROUPS, PAGES_POOL, PAGE, D), 1.0, 6.0, ((0, 4), (1, 128)))
    norm_gain = jnp.clip(jnp.exp(jax.random.uniform(streams_of[9], (D,), jnp.float32, math.log(0.4), math.log(2.5))), 0.4, 2.5)
    out_proj = bell_draw(streams_of[10], (D, D), D ** -0.5, 0.125, ((0, 16),))
    gate_up = bell_draw(streams_of[11], (EXPERTS, 2, FF, D), D ** -0.5, 0.125, ((0, 8), (2, 16)))
    down_proj = bell_draw(streams_of[12], (EXPERTS, FF, D), FF ** -0.5, 0.109375, ((0, 8), (1, 16)))
    return dict(query_stretch=query_stretch, resid_stretch=resid_stretch, route_ids=route_ids, route_probs=route_probs, request_order=request_order, prior_pages=prior_pages, page_order=page_order, key_pool=key_pool, value_pool=value_pool, norm_gain=norm_gain, out_proj=out_proj, gate_up=gate_up, down_proj=down_proj)


NEG_FILL = -1e+30
EPSILON = 1e-06

def attend_slot(slot_index, queries, key_pool, value_pool, prior_pages, page_order):
    group_index = slot_index // REQ_GRP
    member = slot_index % REQ_GRP
    prior_row = prior_pages[group_index]
    page_counts = prior_row + STRETCH_PAGES
    page_starts = jnp.cumsum(page_counts) - page_counts
    first_page = page_starts[member]
    owned = page_counts[member]
    prior_count = prior_row[member]
    page_span = PRIOR_MOST + STRETCH_PAGES
    logical = jnp.arange(page_span, dtype=jnp.int32)
    located = jnp.minimum(first_page + logical, PAGES_POOL - 1).astype(jnp.int32)
    physical = page_order[group_index][located]
    key_rows = key_pool[group_index][physical].reshape(page_span * PAGE, H, HD).astype(jnp.float32)
    value_rows = value_pool[group_index][physical].reshape(page_span * PAGE, H, HD).astype(jnp.float32)
    key_place = jnp.arange(page_span * PAGE, dtype=jnp.int32)
    query_place = prior_count * PAGE + jnp.arange(STRETCH, dtype=jnp.int32)
    visible = (key_place[None, :] < owned * PAGE) & (key_place[None, :] <= query_place[:, None])
    query_rows = queries[slot_index].reshape(STRETCH, H, HD).astype(jnp.float32)
    scores = jnp.einsum('qhd,khd->hqk', query_rows, key_rows) * (1.0 / math.sqrt(HD))
    scores = jnp.where(visible[None], scores, NEG_FILL)
    row_peak = lax.optimization_barrier(jnp.max(scores, axis=2, keepdims=True))
    weights_bf = jnp.where(visible[None], jnp.exp(scores - row_peak), 0.0).astype(jnp.bfloat16)
    totals = lax.optimization_barrier(jnp.sum(weights_bf.astype(jnp.float32), axis=2))
    context = jnp.einsum('hqk,khd->qhd', weights_bf.astype(jnp.float32), value_rows)
    return (context / jnp.transpose(totals)[:, :, None]).reshape(STRETCH, D).astype(jnp.bfloat16)

def run_expert(packed):
    flat_rows, weights_gu, weights_down = packed
    gate = jnp.dot(flat_rows, weights_gu[0].T, preferred_element_type=jnp.float32)
    up_value = jnp.dot(flat_rows, weights_gu[1].T, preferred_element_type=jnp.float32)
    active = (jax.nn.silu(gate) * up_value).astype(jnp.bfloat16)
    return jnp.dot(active, weights_down, preferred_element_type=jnp.float32).astype(jnp.bfloat16)

def reference(query_stretch, resid_stretch, route_ids, route_probs, request_order, prior_pages, page_order, key_pool, value_pool, norm_gain, out_proj, gate_up, down_proj):
    queries = jnp.take(query_stretch, request_order, axis=0)
    resid = jnp.take(resid_stretch, request_order, axis=0)
    served_ids = jnp.take(route_ids, request_order, axis=0)
    served_probs = jnp.take(route_probs, request_order, axis=0)

    def one_slot(slot_index):
        return attend_slot(slot_index, queries, key_pool, value_pool, prior_pages, page_order)
    attended = lax.map(one_slot, jnp.arange(REQS, dtype=jnp.int32))
    projected = jnp.dot(attended.reshape(REQS * STRETCH, D), out_proj.T, preferred_element_type=jnp.float32)
    projected = projected.astype(jnp.bfloat16).reshape(REQS, STRETCH, D)
    hidden_state = resid.astype(jnp.float32) + projected.astype(jnp.float32)
    mean_square = lax.optimization_barrier(jnp.mean(hidden_state * hidden_state, axis=2, keepdims=True))
    normed = (hidden_state * lax.rsqrt(mean_square + EPSILON) * norm_gain.astype(jnp.float32)).astype(jnp.bfloat16)
    blocks = REQS * STRETCH // TOK_EXP
    block_rows = normed.reshape(blocks, TOK_EXP, D)
    flat_ids = served_ids.reshape(blocks, TOK_EXP * TOPK)
    expert_hot = (flat_ids[:, :, None] == jnp.arange(EXPERTS, dtype=jnp.int32)[None, None, :]).astype(jnp.int32)
    before = jnp.cumsum(expert_hot, axis=1) - expert_hot
    slot_place = lax.optimization_barrier(jnp.sum(before * expert_hot, axis=2))
    slot_hot = (slot_place[:, :, None] == jnp.arange(MOST, dtype=jnp.int32)[None, None, :]).astype(jnp.int32)
    place_table = (expert_hot[:, :, :, None] * slot_hot[:, :, None, :]).reshape(blocks, TOK_EXP, TOPK, EXPERTS, MOST)
    pick_table = lax.optimization_barrier(jnp.sum(place_table, axis=2)).astype(jnp.float32)
    sent_rows = jnp.einsum('btnc,btd->nbcd', pick_table, block_rows.astype(jnp.float32)).astype(jnp.bfloat16)
    results = lax.map(run_expert, (sent_rows.reshape(EXPERTS, blocks * MOST, D), gate_up, down_proj))
    share_table = lax.optimization_barrier(jnp.sum(place_table.astype(jnp.float32) * served_probs.reshape(blocks, TOK_EXP, TOPK).astype(jnp.float32)[:, :, :, None, None], axis=2))
    moe_term = jnp.einsum('btnc,nbcd->btd', share_table, results.reshape(EXPERTS, blocks, MOST, D).astype(jnp.float32), precision=lax.Precision.HIGHEST)
    return (hidden_state + moe_term.reshape(REQS, STRETCH, D)).astype(jnp.bfloat16)
```

```python
import math

import jax
import jax.numpy as jnp
from jax import lax
from jax.sharding import PartitionSpec as P

H = 36


NEG_FILL = -1e30
EPSILON = 1e-06


def expert_rows(received, gate_up, down_proj):
    width = received.shape[-1]
    flat_rows = received.reshape(-1, width)
    both = lax.dot_general(
        flat_rows, gate_up[0], (((1,), (2,)), ((), ())), preferred_element_type=jnp.float32
    )
    active = (jax.nn.silu(both[:, 0]) * both[:, 1]).astype(jnp.bfloat16)
    partial_out = jnp.dot(active, down_proj[0], preferred_element_type=jnp.float32)
    return partial_out.reshape(received.shape)


def on_device(
    query_stretch,
    resid_stretch,
    route_ids,
    route_probs,
    request_order,
    prior_pages,
    page_order,
    key_pool,
    value_pool,
    norm_gain,
    out_proj,
    gate_up,
    down_proj,
):
    members = prior_pages.shape[1]
    tokens_here = query_stretch.shape[1]
    width = query_stretch.shape[2]
    head_size = width // H
    group_index = lax.axis_index("req")
    exp_index = lax.axis_index("exp")
    shard_index = lax.axis_index("shard")
    shard_count = lax.axis_size("shard")
    experts_count = lax.axis_size("exp")
    all_query, all_resid, all_ids, all_probs = (
        lax.all_gather(query_stretch, "req", axis=0, tiled=True),
        lax.all_gather(resid_stretch, "req", axis=0, tiled=True),
        lax.all_gather(route_ids, "req", axis=0, tiled=True),
        lax.all_gather(route_probs, "req", axis=0, tiled=True),
    )
    served = lax.dynamic_slice_in_dim(request_order, group_index * members, members)
    served_query = jnp.take(all_query, served, axis=0)
    served_resid = jnp.take(all_resid, served, axis=0)
    served_ids = jnp.take(all_ids, served, axis=0)
    served_probs = jnp.take(all_probs, served, axis=0)
    group_query = lax.all_gather(served_query, "exp", axis=1, tiled=True)
    stretch_len = group_query.shape[1]
    pages_here = key_pool.shape[1]
    page_size = key_pool.shape[2]
    device_index = exp_index * shard_count + shard_index
    physical = device_index * pages_here + jnp.arange(pages_here, dtype=jnp.int32)
    page_row = page_order[0]
    pool_size = page_row.shape[0]
    matched = page_row[None, :] == physical[:, None]
    located = jnp.sum(
        jnp.where(matched, jnp.arange(pool_size, dtype=jnp.int32)[None, :], 0), axis=1
    )
    prior_row = prior_pages[0]
    page_counts = prior_row + stretch_len // page_size
    page_ends = jnp.cumsum(page_counts)
    page_starts = page_ends - page_counts
    owner_slot = jnp.sum((located[:, None] >= page_ends[None, :]).astype(jnp.int32), axis=1)
    owner_hot = owner_slot[:, None] == jnp.arange(members, dtype=jnp.int32)[None, :]
    logical = located - jnp.sum(jnp.where(owner_hot, page_starts[None, :], 0), axis=1)
    prior_here = jnp.sum(jnp.where(owner_hot, prior_row[None, :], 0), axis=1)
    key_place = logical[:, None] * page_size + jnp.arange(page_size, dtype=jnp.int32)[None, :]
    query_place = (
        prior_here[:, None] * page_size + jnp.arange(stretch_len, dtype=jnp.int32)[None, :]
    )
    visible = key_place[:, None, :] <= query_place[:, :, None]
    page_query = jnp.take(group_query, owner_slot, axis=0).reshape(
        pages_here, stretch_len, H, head_size
    )
    key_rows = key_pool[0].reshape(pages_here, page_size, H, head_size)
    value_rows = value_pool[0].reshape(pages_here, page_size, H, head_size)
    scores = jnp.einsum(
        "pqhd,pkhd->phqk", page_query, key_rows, preferred_element_type=jnp.float32
    ) * (1.0 / math.sqrt(head_size))
    scores = jnp.where(visible[:, None, :, :], scores, NEG_FILL)
    page_peak = jnp.max(scores, axis=3)
    local_peak = jnp.max(
        jnp.where(owner_hot[:, :, None, None], page_peak[:, None], NEG_FILL), axis=0
    )
    local_peak = local_peak.astype(jnp.bfloat16).astype(jnp.float32)
    peak_here = jnp.take(local_peak, owner_slot, axis=0)
    weights_bf = jnp.where(
        visible[:, None, :, :], jnp.exp(scores - peak_here[..., None]), 0.0
    ).astype(jnp.bfloat16)
    page_totals = jnp.sum(weights_bf, axis=3, dtype=jnp.float32)
    page_context = jnp.einsum(
        "phqk,pkhd->pqhd", weights_bf, value_rows, preferred_element_type=jnp.float32
    )
    page_context = page_context.reshape(pages_here, stretch_len, width)
    context = jnp.sum(jnp.where(owner_hot[:, :, None, None], page_context[:, None], 0.0), axis=0)
    totals = jnp.sum(jnp.where(owner_hot[:, :, None, None], page_totals[:, None], 0.0), axis=0)
    packed = jnp.concatenate(
        [
            context.astype(jnp.bfloat16),
            jnp.transpose(local_peak, (0, 2, 1)).astype(jnp.bfloat16),
            jnp.transpose(totals, (0, 2, 1)).astype(jnp.bfloat16),
        ],
        axis=2,
    )
    packed_width = packed.shape[2]
    rows_each = members * tokens_here // shard_count
    packed = packed.reshape(members, experts_count, tokens_here, packed_width)
    packed = jnp.transpose(packed, (1, 0, 2, 3)).reshape(
        experts_count * shard_count, rows_each, packed_width
    )
    arrived = lax.all_to_all(packed, ("exp", "shard"), 0, 0, tiled=True).astype(jnp.float32)
    arrived_context = arrived[:, :, :width].reshape(-1, rows_each, H, head_size)
    arrived_peak = arrived[:, :, width : width + H]
    arrived_totals = arrived[:, :, width + H : width + 2 * H]
    row_peak = jnp.max(arrived_peak, axis=0)
    rescale = jnp.exp(arrived_peak - row_peak[None])
    row_totals = jnp.sum(rescale * arrived_totals, axis=0)
    row_context = jnp.sum(rescale[..., None] * arrived_context, axis=0)
    row_attended = (
        (row_context / row_totals[..., None]).reshape(rows_each, width).astype(jnp.bfloat16)
    )
    attended = lax.all_gather(row_attended, "shard", axis=0, tiled=True).reshape(
        members, tokens_here, width
    )
    projected_part = lax.dot_general(
        attended, out_proj, (((2,), (1,)), ((), ())), preferred_element_type=jnp.float32
    ).astype(jnp.bfloat16)
    projected = lax.all_gather(projected_part, "shard", axis=2, tiled=True)
    hidden_state = served_resid.astype(jnp.float32) + projected.astype(jnp.float32)
    mean_square = jnp.mean(hidden_state * hidden_state, axis=2, keepdims=True)
    normed = (hidden_state * lax.rsqrt(mean_square + EPSILON) * norm_gain).astype(jnp.bfloat16)
    top_count = served_ids.shape[2]
    capacity = min(tokens_here, max(2, 3 * tokens_here * top_count // (2 * experts_count)))
    flat_ids = served_ids.reshape(members, tokens_here * top_count)
    expert_hot = (
        flat_ids[:, :, None] == jnp.arange(experts_count, dtype=jnp.int32)[None, None, :]
    ).astype(jnp.int32)
    before = jnp.cumsum(expert_hot, axis=1) - expert_hot
    slot_place = jnp.sum(before * expert_hot, axis=2)
    slot_hot = (
        slot_place[:, :, None] == jnp.arange(capacity, dtype=jnp.int32)[None, None, :]
    ).astype(jnp.int32)
    place_table = (expert_hot[:, :, :, None] * slot_hot[:, :, None, :]).reshape(
        members, tokens_here, top_count, experts_count, capacity
    )
    pick_table = jnp.sum(place_table, axis=2).astype(jnp.bfloat16)
    sent_rows = jnp.einsum(
        "jtnc,jtd->njcd", pick_table, normed, preferred_element_type=jnp.float32
    ).astype(jnp.bfloat16)
    share_table = jnp.sum(
        place_table.astype(jnp.bfloat16) * served_probs[:, :, :, None, None], axis=2
    )
    partial_out = expert_rows(
        lax.all_to_all(sent_rows, "exp", split_axis=0, concat_axis=0, tiled=True),
        gate_up,
        down_proj,
    )
    expert_out = lax.psum(partial_out.astype(jnp.bfloat16), "shard")
    returned = lax.all_to_all(expert_out, "exp", split_axis=0, concat_axis=0, tiled=True)
    moe_term = jnp.einsum(
        "jtnc,njcd->jtd", share_table, returned, preferred_element_type=jnp.float32
    )
    mixed_out = (hidden_state + moe_term).astype(jnp.bfloat16)
    return mixed_out


def solution(mesh):
    return jax.shard_map(
        on_device,
        mesh=mesh,
        in_specs=(
            P("req", "exp", None),
            P("req", "exp", None),
            P("req", "exp", None),
            P("req", "exp", None),
            P(),
            P("req", None),
            P("req", None),
            P("req", ("exp", "shard"), None, None),
            P("req", ("exp", "shard"), None, None),
            P(),
            P("shard", None),
            P("exp", None, "shard", None),
            P("exp", "shard", None),
        ),
        out_specs=P("req", "exp", None),
        check_vma=False,
    )
```

```python
import math

import jax
import jax.numpy as jnp
from jax import lax
from jax.sharding import PartitionSpec as P

H = 36


NEG_FILL = -1e30
EPSILON = 1e-06


def expert_rows(received, gate_up, down_proj):
    width = received.shape[-1]
    flat_rows = received.reshape(-1, width)
    both = lax.dot_general(
        flat_rows, gate_up[0], (((1,), (2,)), ((), ())), preferred_element_type=jnp.float32
    )
    active = (jax.nn.silu(both[:, 0]) * both[:, 1]).astype(jnp.bfloat16)
    partial_out = jnp.dot(active, down_proj[0], preferred_element_type=jnp.float32)
    return partial_out.reshape(received.shape)


def on_device(
    query_stretch,
    resid_stretch,
    route_ids,
    route_probs,
    request_order,
    prior_pages,
    page_order,
    key_pool,
    value_pool,
    norm_gain,
    out_proj,
    gate_up,
    down_proj,
):
    members = prior_pages.shape[1]
    tokens_here = query_stretch.shape[1]
    width = query_stretch.shape[2]
    head_size = width // H
    group_index = lax.axis_index("req")
    exp_index = lax.axis_index("exp")
    shard_index = lax.axis_index("shard")
    shard_count = lax.axis_size("shard")
    experts_count = lax.axis_size("exp")
    all_query, all_resid, all_ids, all_probs = (
        lax.all_gather(query_stretch, "req", axis=0, tiled=True),
        lax.all_gather(resid_stretch, "req", axis=0, tiled=True),
        lax.all_gather(route_ids, "req", axis=0, tiled=True),
        lax.all_gather(route_probs, "req", axis=0, tiled=True),
    )
    served = lax.dynamic_slice_in_dim(request_order, group_index * members, members)
    served_query = jnp.take(all_query, served, axis=0)
    served_resid = jnp.take(all_resid, served, axis=0)
    served_ids = jnp.take(all_ids, served, axis=0)
    served_probs = jnp.take(all_probs, served, axis=0)
    group_query = lax.all_gather(served_query, "exp", axis=1, tiled=True)
    stretch_len = group_query.shape[1]
    pages_here = key_pool.shape[1]
    page_size = key_pool.shape[2]
    device_index = exp_index * shard_count + shard_index
    physical = device_index * pages_here + jnp.arange(pages_here, dtype=jnp.int32)
    page_row = page_order[0]
    pool_size = page_row.shape[0]
    matched = page_row[None, :] == physical[:, None]
    located = jnp.sum(
        jnp.where(matched, jnp.arange(pool_size, dtype=jnp.int32)[None, :], 0), axis=1
    )
    prior_row = prior_pages[0]
    page_counts = prior_row + stretch_len // page_size
    page_ends = jnp.cumsum(page_counts)
    page_starts = page_ends - page_counts
    owner_slot = jnp.sum((located[:, None] >= page_ends[None, :]).astype(jnp.int32), axis=1)
    owner_hot = owner_slot[:, None] == jnp.arange(members, dtype=jnp.int32)[None, :]
    logical = located - jnp.sum(jnp.where(owner_hot, page_starts[None, :], 0), axis=1)
    prior_here = jnp.sum(jnp.where(owner_hot, prior_row[None, :], 0), axis=1)
    key_place = logical[:, None] * page_size + jnp.arange(page_size, dtype=jnp.int32)[None, :]
    query_place = (
        prior_here[:, None] * page_size + jnp.arange(stretch_len, dtype=jnp.int32)[None, :]
    )
    visible = key_place[:, None, :] <= query_place[:, :, None]
    page_query = jnp.take(group_query, owner_slot, axis=0).reshape(
        pages_here, stretch_len, H, head_size
    )
    key_rows = key_pool[0].reshape(pages_here, page_size, H, head_size)
    value_rows = value_pool[0].reshape(pages_here, page_size, H, head_size)
    scores = jnp.einsum(
        "pqhd,pkhd->phqk", page_query, key_rows, preferred_element_type=jnp.float32
    ) * (1.0 / math.sqrt(head_size))
    scores = jnp.where(visible[:, None, :, :], scores, NEG_FILL)
    page_peak = jnp.max(scores, axis=3)
    local_peak = jnp.max(
        jnp.where(owner_hot[:, :, None, None], page_peak[:, None], NEG_FILL), axis=0
    )
    local_peak = local_peak.astype(jnp.bfloat16).astype(jnp.float32)
    peak_here = jnp.take(local_peak, owner_slot, axis=0)
    weights_bf = jnp.where(
        visible[:, None, :, :], jnp.exp(scores - peak_here[..., None]), 0.0
    ).astype(jnp.bfloat16)
    page_totals = jnp.sum(weights_bf, axis=3, dtype=jnp.float32)
    page_context = jnp.einsum(
        "phqk,pkhd->pqhd", weights_bf, value_rows, preferred_element_type=jnp.float32
    )
    page_context = page_context.reshape(pages_here, stretch_len, width)
    context = jnp.sum(jnp.where(owner_hot[:, :, None, None], page_context[:, None], 0.0), axis=0)
    totals = jnp.sum(jnp.where(owner_hot[:, :, None, None], page_totals[:, None], 0.0), axis=0)
    packed = jnp.concatenate(
        [
            context.astype(jnp.bfloat16),
            jnp.transpose(local_peak, (0, 2, 1)).astype(jnp.bfloat16),
            jnp.transpose(totals, (0, 2, 1)).astype(jnp.bfloat16),
        ],
        axis=2,
    )
    packed_width = packed.shape[2]
    rows_each = members * tokens_here // shard_count
    packed = packed.reshape(members, experts_count, tokens_here, packed_width)
    packed = jnp.transpose(packed, (1, 0, 2, 3)).reshape(
        experts_count * shard_count, rows_each, packed_width
    )
    arrived = lax.all_to_all(packed, ("exp", "shard"), 0, 0, tiled=True).astype(jnp.float32)
    arrived_context = arrived[:, :, :width].reshape(-1, rows_each, H, head_size)
    arrived_peak = arrived[:, :, width : width + H]
    arrived_totals = arrived[:, :, width + H : width + 2 * H]
    row_peak = jnp.max(arrived_peak, axis=0)
    rescale = jnp.exp(arrived_peak - row_peak[None])
    row_totals = jnp.sum(rescale * arrived_totals, axis=0)
    row_context = jnp.sum(rescale[..., None] * arrived_context, axis=0)
    row_attended = (
        (row_context / row_totals[..., None]).reshape(rows_each, width).astype(jnp.bfloat16)
    )
    attended = lax.all_gather(row_attended, "shard", axis=0, tiled=True).reshape(
        members, tokens_here, width
    )
    projected_part = lax.dot_general(
        attended, out_proj, (((2,), (1,)), ((), ())), preferred_element_type=jnp.float32
    ).astype(jnp.bfloat16)
    projected = lax.all_gather(projected_part, "shard", axis=2, tiled=True)
    hidden_state = served_resid.astype(jnp.float32) + projected.astype(jnp.float32)
    mean_square = jnp.mean(hidden_state * hidden_state, axis=2, keepdims=True)
    normed = (hidden_state * lax.rsqrt(mean_square + EPSILON) * norm_gain).astype(jnp.bfloat16)
    top_count = served_ids.shape[2]
    capacity = min(tokens_here, max(2, 3 * tokens_here * top_count // (2 * experts_count)))
    flat_ids = served_ids.reshape(members, tokens_here * top_count)
    expert_hot = (
        flat_ids[:, :, None] == jnp.arange(experts_count, dtype=jnp.int32)[None, None, :]
    ).astype(jnp.int32)
    before = jnp.cumsum(expert_hot, axis=1) - expert_hot
    slot_place = jnp.sum(before * expert_hot, axis=2)
    slot_hot = (
        slot_place[:, :, None] == jnp.arange(capacity, dtype=jnp.int32)[None, None, :]
    ).astype(jnp.int32)
    place_table = (expert_hot[:, :, :, None] * slot_hot[:, :, None, :]).reshape(
        members, tokens_here, top_count, experts_count, capacity
    )
    pick_table = jnp.sum(place_table, axis=2).astype(jnp.bfloat16)
    sent_rows = jnp.einsum(
        "jtnc,jtd->njcd", pick_table, normed, preferred_element_type=jnp.float32
    ).astype(jnp.bfloat16)
    share_table = jnp.sum(
        place_table.astype(jnp.bfloat16) * served_probs[:, :, :, None, None], axis=2
    )
    partial_out = expert_rows(
        lax.all_to_all(sent_rows, "exp", split_axis=0, concat_axis=0, tiled=True),
        gate_up,
        down_proj,
    ).astype(jnp.bfloat16)
    feature_block = width // shard_count
    partial_out = partial_out.reshape(
        experts_count, members, capacity, shard_count, feature_block
    )
    partial_out = jnp.transpose(partial_out, (0, 3, 1, 2, 4)).reshape(
        experts_count * shard_count, members, capacity, feature_block
    )
    gathered_parts = lax.all_to_all(partial_out, ("exp", "shard"), 0, 0, tiled=True)
    expert_out = (
        jnp.sum(
            gathered_parts.reshape(
                experts_count, shard_count, members, capacity, feature_block
            ).astype(jnp.float32),
            axis=1,
        )
        .astype(jnp.bfloat16)
    )
    moe_term = jnp.einsum(
        "jtnc,njcd->jtd", share_table, expert_out, preferred_element_type=jnp.float32
    )
    hidden_block = lax.dynamic_slice_in_dim(
        hidden_state, shard_index * feature_block, feature_block, 2
    )
    mixed_block = (hidden_block + moe_term).astype(jnp.bfloat16)
    mixed_out = lax.all_gather(mixed_block, "shard", axis=2, tiled=True)
    return mixed_out


def solution(mesh):
    return jax.shard_map(
        on_device,
        mesh=mesh,
        in_specs=(
            P("req", "exp", None),
            P("req", "exp", None),
            P("req", "exp", None),
            P("req", "exp", None),
            P(),
            P("req", None),
            P("req", None),
            P("req", ("exp", "shard"), None, None),
            P("req", ("exp", "shard"), None, None),
            P(),
            P("shard", None),
            P("exp", None, "shard", None),
            P("exp", "shard", None),
        ),
        out_specs=P("req", "exp", None),
        check_vma=False,
    )
```

```python
import math

import jax
import jax.numpy as jnp
from jax import lax
from jax.sharding import PartitionSpec as P

H = 36


NEG_FILL = -1e30
EPSILON = 1e-06


def expert_rows(received, gate_up, down_proj):
    width = received.shape[-1]
    flat_rows = received.reshape(-1, width)
    both = lax.dot_general(
        flat_rows, gate_up[0], (((1,), (2,)), ((), ())), preferred_element_type=jnp.float32
    )
    active = (jax.nn.silu(both[:, 0]) * both[:, 1]).astype(jnp.bfloat16)
    partial_out = jnp.dot(active, down_proj[0], preferred_element_type=jnp.float32)
    return partial_out.reshape(received.shape)


def on_device(
    query_stretch,
    resid_stretch,
    route_ids,
    route_probs,
    request_order,
    prior_pages,
    page_order,
    key_pool,
    value_pool,
    norm_gain,
    out_proj,
    gate_up,
    down_proj,
):
    members = prior_pages.shape[1]
    tokens_here = query_stretch.shape[1]
    width = query_stretch.shape[2]
    head_size = width // H
    group_index = lax.axis_index("req")
    exp_index = lax.axis_index("exp")
    shard_index = lax.axis_index("shard")
    shard_count = lax.axis_size("shard")
    experts_count = lax.axis_size("exp")
    extras = jnp.concatenate(
        [resid_stretch, route_probs, route_ids.astype(jnp.bfloat16)], axis=2
    )
    all_query = lax.all_gather(query_stretch, "req", axis=0, tiled=True)
    all_extras = lax.all_gather(extras, "req", axis=0, tiled=True)
    served = lax.dynamic_slice_in_dim(request_order, group_index * members, members)
    served_query = jnp.take(all_query, served, axis=0)
    served_extras = jnp.take(all_extras, served, axis=0)
    top_count = route_ids.shape[2]
    served_resid = served_extras[:, :, :width]
    served_probs = served_extras[:, :, width : width + top_count]
    served_ids = served_extras[:, :, width + top_count :].astype(jnp.int32)
    spread_query = jnp.broadcast_to(
        served_query[None], (experts_count,) + served_query.shape
    )
    group_query = lax.all_to_all(spread_query, "exp", 0, 0, tiled=False)
    group_query = jnp.transpose(group_query, (1, 0, 2, 3)).reshape(
        members, experts_count * tokens_here, width
    )
    stretch_len = group_query.shape[1]
    pages_here = key_pool.shape[1]
    page_size = key_pool.shape[2]
    device_index = exp_index * shard_count + shard_index
    physical = device_index * pages_here + jnp.arange(pages_here, dtype=jnp.int32)
    page_row = page_order[0]
    pool_size = page_row.shape[0]
    matched = page_row[None, :] == physical[:, None]
    located = jnp.sum(
        jnp.where(matched, jnp.arange(pool_size, dtype=jnp.int32)[None, :], 0), axis=1
    )
    prior_row = prior_pages[0]
    page_counts = prior_row + stretch_len // page_size
    page_ends = jnp.cumsum(page_counts)
    page_starts = page_ends - page_counts
    owner_slot = jnp.sum((located[:, None] >= page_ends[None, :]).astype(jnp.int32), axis=1)
    owner_hot = owner_slot[:, None] == jnp.arange(members, dtype=jnp.int32)[None, :]
    logical = located - jnp.sum(jnp.where(owner_hot, page_starts[None, :], 0), axis=1)
    prior_here = jnp.sum(jnp.where(owner_hot, prior_row[None, :], 0), axis=1)
    key_place = logical[:, None] * page_size + jnp.arange(page_size, dtype=jnp.int32)[None, :]
    query_place = (
        prior_here[:, None] * page_size + jnp.arange(stretch_len, dtype=jnp.int32)[None, :]
    )
    visible = key_place[:, None, :] <= query_place[:, :, None]
    page_query = jnp.take(group_query, owner_slot, axis=0).reshape(
        pages_here, stretch_len, H, head_size
    )
    key_rows = key_pool[0].reshape(pages_here, page_size, H, head_size)
    value_rows = value_pool[0].reshape(pages_here, page_size, H, head_size)
    scores = jnp.einsum(
        "pqhd,pkhd->phqk", page_query, key_rows, preferred_element_type=jnp.float32
    ) * (1.0 / math.sqrt(head_size))
    scores = jnp.where(visible[:, None, :, :], scores, NEG_FILL)
    page_peak = jnp.max(scores, axis=3)
    local_peak = jnp.max(
        jnp.where(owner_hot[:, :, None, None], page_peak[:, None], NEG_FILL), axis=0
    )
    local_peak = local_peak.astype(jnp.bfloat16).astype(jnp.float32)
    peak_here = jnp.take(local_peak, owner_slot, axis=0)
    weights_bf = jnp.where(
        visible[:, None, :, :], jnp.exp(scores - peak_here[..., None]), 0.0
    ).astype(jnp.bfloat16)
    page_totals = jnp.sum(weights_bf, axis=3, dtype=jnp.float32)
    page_context = jnp.einsum(
        "phqk,pkhd->pqhd", weights_bf, value_rows, preferred_element_type=jnp.float32
    )
    page_context = page_context.reshape(pages_here, stretch_len, width)
    context = jnp.sum(jnp.where(owner_hot[:, :, None, None], page_context[:, None], 0.0), axis=0)
    totals = jnp.sum(jnp.where(owner_hot[:, :, None, None], page_totals[:, None], 0.0), axis=0)
    packed = jnp.concatenate(
        [
            context.astype(jnp.bfloat16),
            jnp.transpose(local_peak, (0, 2, 1)).astype(jnp.bfloat16),
            jnp.transpose(totals, (0, 2, 1)).astype(jnp.bfloat16),
        ],
        axis=2,
    )
    packed_width = packed.shape[2]
    rows_each = members * tokens_here // shard_count
    packed = packed.reshape(members, experts_count, tokens_here, packed_width)
    packed = jnp.transpose(packed, (1, 0, 2, 3)).reshape(
        experts_count * shard_count, rows_each, packed_width
    )
    arrived = lax.all_to_all(packed, ("exp", "shard"), 0, 0, tiled=True).astype(jnp.float32)
    arrived_context = arrived[:, :, :width].reshape(-1, rows_each, H, head_size)
    arrived_peak = arrived[:, :, width : width + H]
    arrived_totals = arrived[:, :, width + H : width + 2 * H]
    row_peak = jnp.max(arrived_peak, axis=0)
    rescale = jnp.exp(arrived_peak - row_peak[None])
    row_totals = jnp.sum(rescale * arrived_totals, axis=0)
    row_context = jnp.sum(rescale[..., None] * arrived_context, axis=0)
    row_attended = (
        (row_context / row_totals[..., None]).reshape(rows_each, width).astype(jnp.bfloat16)
    )
    attended = lax.all_gather(row_attended, "shard", axis=0, tiled=True).reshape(
        members, tokens_here, width
    )
    projected_part = lax.dot_general(
        attended, out_proj, (((2,), (1,)), ((), ())), preferred_element_type=jnp.float32
    ).astype(jnp.bfloat16)
    projected = lax.all_gather(projected_part, "shard", axis=2, tiled=True)
    hidden_state = served_resid.astype(jnp.float32) + projected.astype(jnp.float32)
    mean_square = jnp.mean(hidden_state * hidden_state, axis=2, keepdims=True)
    normed = (hidden_state * lax.rsqrt(mean_square + EPSILON) * norm_gain).astype(jnp.bfloat16)
    capacity = min(tokens_here, max(2, 3 * tokens_here * top_count // (2 * experts_count)))
    flat_ids = served_ids.reshape(members, tokens_here * top_count)
    expert_hot = (
        flat_ids[:, :, None] == jnp.arange(experts_count, dtype=jnp.int32)[None, None, :]
    ).astype(jnp.int32)
    before = jnp.cumsum(expert_hot, axis=1) - expert_hot
    slot_place = jnp.sum(before * expert_hot, axis=2)
    slot_hot = (
        slot_place[:, :, None] == jnp.arange(capacity, dtype=jnp.int32)[None, None, :]
    ).astype(jnp.int32)
    place_table = (expert_hot[:, :, :, None] * slot_hot[:, :, None, :]).reshape(
        members, tokens_here, top_count, experts_count, capacity
    )
    pick_table = jnp.sum(place_table, axis=2).astype(jnp.bfloat16)
    sent_rows = jnp.einsum(
        "jtnc,jtd->njcd", pick_table, normed, preferred_element_type=jnp.float32
    ).astype(jnp.bfloat16)
    share_table = jnp.sum(
        place_table.astype(jnp.bfloat16) * served_probs[:, :, :, None, None], axis=2
    )
    partial_out = expert_rows(
        lax.all_to_all(sent_rows, "exp", split_axis=0, concat_axis=0, tiled=True),
        gate_up,
        down_proj,
    ).astype(jnp.bfloat16)
    feature_block = width // shard_count
    partial_out = partial_out.reshape(
        experts_count, members, capacity, shard_count, feature_block
    )
    partial_out = jnp.transpose(partial_out, (0, 3, 1, 2, 4)).reshape(
        experts_count * shard_count, members, capacity, feature_block
    )
    gathered_parts = lax.all_to_all(partial_out, ("exp", "shard"), 0, 0, tiled=True)
    expert_out = (
        jnp.sum(
            gathered_parts.reshape(
                experts_count, shard_count, members, capacity, feature_block
            ).astype(jnp.float32),
            axis=1,
        )
        .astype(jnp.bfloat16)
    )
    moe_term = jnp.einsum(
        "jtnc,njcd->jtd", share_table, expert_out, preferred_element_type=jnp.float32
    )
    hidden_block = lax.dynamic_slice_in_dim(
        hidden_state, shard_index * feature_block, feature_block, 2
    )
    mixed_block = (hidden_block + moe_term).astype(jnp.bfloat16)
    mixed_out = lax.all_gather(mixed_block, "shard", axis=2, tiled=True)
    return mixed_out


def solution(mesh):
    return jax.shard_map(
        on_device,
        mesh=mesh,
        in_specs=(
            P("req", "exp", None),
            P("req", "exp", None),
            P("req", "exp", None),
            P("req", "exp", None),
            P(),
            P("req", None),
            P("req", None),
            P("req", ("exp", "shard"), None, None),
            P("req", ("exp", "shard"), None, None),
            P(),
            P("shard", None),
            P("exp", None, "shard", None),
            P("exp", "shard", None),
        ),
        out_specs=P("req", "exp", None),
        check_vma=False,
    )
```

```python
import math

import jax
import jax.numpy as jnp
from jax import lax
from jax.sharding import PartitionSpec as P

H = 36


NEG_FILL = -1e30
EPSILON = 1e-06


def expert_rows(received, gate_up, down_proj):
    width = received.shape[-1]
    flat_rows = received.reshape(-1, width)
    both = lax.dot_general(
        flat_rows, gate_up[0], (((1,), (2,)), ((), ())), preferred_element_type=jnp.float32
    )
    active = (jax.nn.silu(both[:, 0]) * both[:, 1]).astype(jnp.bfloat16)
    partial_out = jnp.dot(active, down_proj[0], preferred_element_type=jnp.float32)
    return partial_out.reshape(received.shape)


def on_device(
    query_stretch,
    resid_stretch,
    route_ids,
    route_probs,
    request_order,
    prior_pages,
    page_order,
    key_pool,
    value_pool,
    norm_gain,
    out_proj,
    gate_up,
    down_proj,
):
    members = prior_pages.shape[1]
    tokens_here = query_stretch.shape[1]
    width = query_stretch.shape[2]
    head_size = width // H
    group_index = lax.axis_index("req")
    exp_index = lax.axis_index("exp")
    shard_index = lax.axis_index("shard")
    shard_count = lax.axis_size("shard")
    experts_count = lax.axis_size("exp")
    extras = jnp.concatenate(
        [resid_stretch, route_probs, route_ids.astype(jnp.bfloat16)], axis=2
    )
    all_query = lax.all_gather(query_stretch, "req", axis=0, tiled=True)
    all_extras = lax.all_gather(extras, "req", axis=0, tiled=True)
    served = lax.dynamic_slice_in_dim(request_order, group_index * members, members)
    served_query = jnp.take(all_query, served, axis=0)
    served_extras = jnp.take(all_extras, served, axis=0)
    top_count = route_ids.shape[2]
    served_resid = served_extras[:, :, :width]
    served_probs = served_extras[:, :, width : width + top_count]
    served_ids = served_extras[:, :, width + top_count :].astype(jnp.int32)
    spread_query = jnp.broadcast_to(
        served_query[None], (experts_count,) + served_query.shape
    )
    group_query = lax.all_to_all(spread_query, "exp", 0, 0, tiled=False)
    pages_here = key_pool.shape[1]
    page_size = key_pool.shape[2]
    keys_here = pages_here * page_size
    device_index = exp_index * shard_count + shard_index
    physical = device_index * pages_here + jnp.arange(pages_here, dtype=jnp.int32)
    page_row = page_order[0]
    pool_size = page_row.shape[0]
    matched = page_row[None, :] == physical[:, None]
    located = jnp.sum(
        jnp.where(matched, jnp.arange(pool_size, dtype=jnp.int32)[None, :], 0), axis=1
    )
    prior_row = prior_pages[0]
    page_counts = prior_row + experts_count * tokens_here // page_size
    page_ends = jnp.cumsum(page_counts)
    page_starts = page_ends - page_counts
    owner_slot = jnp.sum((located[:, None] >= page_ends[None, :]).astype(jnp.int32), axis=1)
    owner_hot = owner_slot[:, None] == jnp.arange(members, dtype=jnp.int32)[None, :]
    logical = located - jnp.sum(jnp.where(owner_hot, page_starts[None, :], 0), axis=1)
    key_place = (
        logical[:, None] * page_size + jnp.arange(page_size, dtype=jnp.int32)[None, :]
    ).reshape(keys_here)
    key_owner = jnp.repeat(owner_slot, page_size)
    query_place = (
        prior_row[None, :, None] * page_size
        + jnp.arange(experts_count, dtype=jnp.int32)[:, None, None] * tokens_here
        + jnp.arange(tokens_here, dtype=jnp.int32)[None, None, :]
    )
    visible = (key_owner[None, None, None, :] == jnp.arange(members, dtype=jnp.int32)[None, :, None, None]) & (
        key_place[None, None, None, :] <= query_place[..., None]
    )
    query_rows = group_query.reshape(experts_count, members, tokens_here, H, head_size)
    key_rows = key_pool[0].reshape(keys_here, H, head_size)
    value_rows = value_pool[0].reshape(keys_here, H, head_size)
    scores = jnp.einsum(
        "ejthd,khd->ejhtk", query_rows, key_rows, preferred_element_type=jnp.float32
    ) * (1.0 / math.sqrt(head_size))
    scores = jnp.where(visible[:, :, None], scores, NEG_FILL)
    local_peak = jnp.max(scores, axis=4).astype(jnp.bfloat16).astype(jnp.float32)
    weights_bf = jnp.where(
        visible[:, :, None], jnp.exp(scores - local_peak[..., None]), 0.0
    ).astype(jnp.bfloat16)
    totals = jnp.sum(weights_bf, axis=4, dtype=jnp.float32)
    context = jnp.einsum(
        "ejhtk,khd->ejthd", weights_bf, value_rows, preferred_element_type=jnp.float32
    ).reshape(experts_count, members, tokens_here, width)
    packed = jnp.concatenate(
        [
            context.astype(jnp.bfloat16),
            jnp.transpose(local_peak, (0, 1, 3, 2)).astype(jnp.bfloat16),
            jnp.transpose(totals, (0, 1, 3, 2)).astype(jnp.bfloat16),
        ],
        axis=3,
    )
    packed_width = packed.shape[3]
    rows_each = members * tokens_here // shard_count
    packed = packed.reshape(experts_count * shard_count, rows_each, packed_width)
    arrived = lax.all_to_all(packed, ("exp", "shard"), 0, 0, tiled=True).astype(jnp.float32)
    arrived_context = arrived[:, :, :width].reshape(-1, rows_each, H, head_size)
    arrived_peak = arrived[:, :, width : width + H]
    arrived_totals = arrived[:, :, width + H : width + 2 * H]
    row_peak = jnp.max(arrived_peak, axis=0)
    rescale = jnp.exp(arrived_peak - row_peak[None])
    row_totals = jnp.sum(rescale * arrived_totals, axis=0)
    row_context = jnp.sum(rescale[..., None] * arrived_context, axis=0)
    row_attended = (
        (row_context / row_totals[..., None]).reshape(rows_each, width).astype(jnp.bfloat16)
    )
    attended = lax.all_gather(row_attended, "shard", axis=0, tiled=True).reshape(
        members, tokens_here, width
    )
    projected_part = lax.dot_general(
        attended, out_proj, (((2,), (1,)), ((), ())), preferred_element_type=jnp.float32
    ).astype(jnp.bfloat16)
    projected = lax.all_gather(projected_part, "shard", axis=2, tiled=True)
    hidden_state = served_resid.astype(jnp.float32) + projected.astype(jnp.float32)
    mean_square = jnp.mean(hidden_state * hidden_state, axis=2, keepdims=True)
    normed = (hidden_state * lax.rsqrt(mean_square + EPSILON) * norm_gain).astype(jnp.bfloat16)
    capacity = min(tokens_here, max(2, 3 * tokens_here * top_count // (2 * experts_count)))
    flat_ids = served_ids.reshape(members, tokens_here * top_count)
    expert_hot = (
        flat_ids[:, :, None] == jnp.arange(experts_count, dtype=jnp.int32)[None, None, :]
    ).astype(jnp.int32)
    before = jnp.cumsum(expert_hot, axis=1) - expert_hot
    slot_place = jnp.sum(before * expert_hot, axis=2)
    slot_hot = (
        slot_place[:, :, None] == jnp.arange(capacity, dtype=jnp.int32)[None, None, :]
    ).astype(jnp.int32)
    place_table = (expert_hot[:, :, :, None] * slot_hot[:, :, None, :]).reshape(
        members, tokens_here, top_count, experts_count, capacity
    )
    pick_table = jnp.sum(place_table, axis=2).astype(jnp.bfloat16)
    sent_rows = jnp.einsum(
        "jtnc,jtd->njcd", pick_table, normed, preferred_element_type=jnp.float32
    ).astype(jnp.bfloat16)
    share_table = jnp.sum(
        place_table.astype(jnp.bfloat16) * served_probs[:, :, :, None, None], axis=2
    )
    partial_out = expert_rows(
        lax.all_to_all(sent_rows, "exp", split_axis=0, concat_axis=0, tiled=True),
        gate_up,
        down_proj,
    ).astype(jnp.bfloat16)
    feature_block = width // shard_count
    partial_out = partial_out.reshape(
        experts_count, members, capacity, shard_count, feature_block
    )
    partial_out = jnp.transpose(partial_out, (0, 3, 1, 2, 4)).reshape(
        experts_count * shard_count, members, capacity, feature_block
    )
    gathered_parts = lax.all_to_all(partial_out, ("exp", "shard"), 0, 0, tiled=True)
    expert_out = (
        jnp.sum(
            gathered_parts.reshape(
                experts_count, shard_count, members, capacity, feature_block
            ).astype(jnp.float32),
            axis=1,
        )
        .astype(jnp.bfloat16)
    )
    moe_term = jnp.einsum(
        "jtnc,njcd->jtd", share_table, expert_out, preferred_element_type=jnp.float32
    )
    hidden_block = lax.dynamic_slice_in_dim(
        hidden_state, shard_index * feature_block, feature_block, 2
    )
    mixed_block = (hidden_block + moe_term).astype(jnp.bfloat16)
    mixed_out = lax.all_gather(mixed_block, "shard", axis=2, tiled=True)
    return mixed_out


def solution(mesh):
    return jax.shard_map(
        on_device,
        mesh=mesh,
        in_specs=(
            P("req", "exp", None),
            P("req", "exp", None),
            P("req", "exp", None),
            P("req", "exp", None),
            P(),
            P("req", None),
            P("req", None),
            P("req", ("exp", "shard"), None, None),
            P("req", ("exp", "shard"), None, None),
            P(),
            P("shard", None),
            P("exp", None, "shard", None),
            P("exp", "shard", None),
        ),
        out_specs=P("req", "exp", None),
        check_vma=False,
    )
```

```python
import math

import jax
import jax.numpy as jnp
from jax import lax
from jax.sharding import PartitionSpec as P

H = 36


NEG_FILL = -1e30
EPSILON = 1e-06


def expert_rows(received, gate_up, down_proj):
    width = received.shape[-1]
    flat_rows = received.reshape(-1, width)
    both = lax.dot_general(
        flat_rows, gate_up[0], (((1,), (2,)), ((), ())), preferred_element_type=jnp.float32
    )
    active = (jax.nn.silu(both[:, 0]) * both[:, 1]).astype(jnp.bfloat16)
    partial_out = jnp.dot(active, down_proj[0], preferred_element_type=jnp.float32)
    return partial_out.reshape(received.shape)


def on_device(
    query_stretch,
    resid_stretch,
    route_ids,
    route_probs,
    request_order,
    prior_pages,
    page_order,
    key_pool,
    value_pool,
    norm_gain,
    out_proj,
    gate_up,
    down_proj,
):
    members = prior_pages.shape[1]
    tokens_here = query_stretch.shape[1]
    width = query_stretch.shape[2]
    head_size = width // H
    group_index = lax.axis_index("req")
    exp_index = lax.axis_index("exp")
    shard_index = lax.axis_index("shard")
    shard_count = lax.axis_size("shard")
    experts_count = lax.axis_size("exp")
    extras = jnp.concatenate(
        [resid_stretch, route_probs, route_ids.astype(jnp.bfloat16)], axis=2
    )
    all_query = lax.all_gather(query_stretch, "req", axis=0, tiled=True)
    all_extras = lax.all_gather(extras, "req", axis=0, tiled=True)
    served = lax.dynamic_slice_in_dim(request_order, group_index * members, members)
    served_query = jnp.take(all_query, served, axis=0)
    served_extras = jnp.take(all_extras, served, axis=0)
    spread_query = jnp.broadcast_to(
        served_query[None], (experts_count,) + served_query.shape
    )
    group_query = lax.all_to_all(spread_query, "exp", 0, 0, tiled=False)
    group_query, served_extras = lax.optimization_barrier((group_query, served_extras))
    top_count = route_ids.shape[2]
    served_resid = served_extras[:, :, :width]
    served_probs = served_extras[:, :, width : width + top_count]
    served_ids = served_extras[:, :, width + top_count :].astype(jnp.int32)
    pages_here = key_pool.shape[1]
    page_size = key_pool.shape[2]
    keys_here = pages_here * page_size
    device_index = exp_index * shard_count + shard_index
    physical = device_index * pages_here + jnp.arange(pages_here, dtype=jnp.int32)
    page_row = page_order[0]
    pool_size = page_row.shape[0]
    matched = page_row[None, :] == physical[:, None]
    located = jnp.sum(
        jnp.where(matched, jnp.arange(pool_size, dtype=jnp.int32)[None, :], 0), axis=1
    )
    prior_row = prior_pages[0]
    page_counts = prior_row + experts_count * tokens_here // page_size
    page_ends = jnp.cumsum(page_counts)
    page_starts = page_ends - page_counts
    owner_slot = jnp.sum((located[:, None] >= page_ends[None, :]).astype(jnp.int32), axis=1)
    owner_hot = owner_slot[:, None] == jnp.arange(members, dtype=jnp.int32)[None, :]
    logical = located - jnp.sum(jnp.where(owner_hot, page_starts[None, :], 0), axis=1)
    key_place = (
        logical[:, None] * page_size + jnp.arange(page_size, dtype=jnp.int32)[None, :]
    ).reshape(keys_here)
    key_owner = jnp.repeat(owner_slot, page_size)
    query_place = (
        prior_row[None, :, None] * page_size
        + jnp.arange(experts_count, dtype=jnp.int32)[:, None, None] * tokens_here
        + jnp.arange(tokens_here, dtype=jnp.int32)[None, None, :]
    )
    visible = (key_owner[None, None, None, :] == jnp.arange(members, dtype=jnp.int32)[None, :, None, None]) & (
        key_place[None, None, None, :] <= query_place[..., None]
    )
    query_rows = group_query.reshape(experts_count, members, tokens_here, H, head_size)
    key_rows = key_pool[0].reshape(keys_here, H, head_size)
    value_rows = value_pool[0].reshape(keys_here, H, head_size)
    scores = jnp.einsum(
        "ejthd,khd->ejhtk", query_rows, key_rows, preferred_element_type=jnp.float32
    ) * (1.0 / math.sqrt(head_size))
    scores = jnp.where(visible[:, :, None], scores, NEG_FILL)
    local_peak = jnp.max(scores, axis=4).astype(jnp.bfloat16).astype(jnp.float32)
    weights_bf = jnp.where(
        visible[:, :, None], jnp.exp(scores - local_peak[..., None]), 0.0
    ).astype(jnp.bfloat16)
    totals = jnp.sum(weights_bf, axis=4, dtype=jnp.float32)
    context = jnp.einsum(
        "ejhtk,khd->ejthd", weights_bf, value_rows, preferred_element_type=jnp.float32
    ).reshape(experts_count, members, tokens_here, width)
    packed = jnp.concatenate(
        [
            context.astype(jnp.bfloat16),
            jnp.transpose(local_peak, (0, 1, 3, 2)).astype(jnp.bfloat16),
            jnp.transpose(totals, (0, 1, 3, 2)).astype(jnp.bfloat16),
        ],
        axis=3,
    )
    packed_width = packed.shape[3]
    rows_each = members * tokens_here // shard_count
    packed = packed.reshape(experts_count * shard_count, rows_each, packed_width)
    arrived = lax.all_to_all(packed, ("exp", "shard"), 0, 0, tiled=True).astype(jnp.float32)
    arrived_context = arrived[:, :, :width].reshape(-1, rows_each, H, head_size)
    arrived_peak = arrived[:, :, width : width + H]
    arrived_totals = arrived[:, :, width + H : width + 2 * H]
    row_peak = jnp.max(arrived_peak, axis=0)
    rescale = jnp.exp(arrived_peak - row_peak[None])
    row_totals = jnp.sum(rescale * arrived_totals, axis=0)
    row_context = jnp.sum(rescale[..., None] * arrived_context, axis=0)
    row_attended = (
        (row_context / row_totals[..., None]).reshape(rows_each, width).astype(jnp.bfloat16)
    )
    attended = lax.all_gather(row_attended, "shard", axis=0, tiled=True).reshape(
        members, tokens_here, width
    )
    projected_part = lax.dot_general(
        attended, out_proj, (((2,), (1,)), ((), ())), preferred_element_type=jnp.float32
    ).astype(jnp.bfloat16)
    projected = lax.all_gather(projected_part, "shard", axis=2, tiled=True)
    hidden_state = served_resid.astype(jnp.float32) + projected.astype(jnp.float32)
    mean_square = jnp.mean(hidden_state * hidden_state, axis=2, keepdims=True)
    normed = (hidden_state * lax.rsqrt(mean_square + EPSILON) * norm_gain).astype(jnp.bfloat16)
    capacity = min(tokens_here, max(2, 3 * tokens_here * top_count // (2 * experts_count)))
    flat_ids = served_ids.reshape(members, tokens_here * top_count)
    expert_hot = (
        flat_ids[:, :, None] == jnp.arange(experts_count, dtype=jnp.int32)[None, None, :]
    ).astype(jnp.int32)
    before = jnp.cumsum(expert_hot, axis=1) - expert_hot
    slot_place = jnp.sum(before * expert_hot, axis=2)
    slot_hot = (
        slot_place[:, :, None] == jnp.arange(capacity, dtype=jnp.int32)[None, None, :]
    ).astype(jnp.int32)
    place_table = (expert_hot[:, :, :, None] * slot_hot[:, :, None, :]).reshape(
        members, tokens_here, top_count, experts_count, capacity
    )
    pick_table = jnp.sum(place_table, axis=2).astype(jnp.bfloat16)
    sent_rows = jnp.einsum(
        "jtnc,jtd->njcd", pick_table, normed, preferred_element_type=jnp.float32
    ).astype(jnp.bfloat16)
    share_table = jnp.sum(
        place_table.astype(jnp.bfloat16) * served_probs[:, :, :, None, None], axis=2
    )
    partial_out = expert_rows(
        lax.all_to_all(sent_rows, "exp", split_axis=0, concat_axis=0, tiled=True),
        gate_up,
        down_proj,
    ).astype(jnp.bfloat16)
    feature_block = width // shard_count
    partial_out = partial_out.reshape(
        experts_count, members, capacity, shard_count, feature_block
    )
    partial_out = jnp.transpose(partial_out, (0, 3, 1, 2, 4)).reshape(
        experts_count * shard_count, members, capacity, feature_block
    )
    gathered_parts = lax.all_to_all(partial_out, ("exp", "shard"), 0, 0, tiled=True)
    expert_out = (
        jnp.sum(
            gathered_parts.reshape(
                experts_count, shard_count, members, capacity, feature_block
            ).astype(jnp.float32),
            axis=1,
        )
        .astype(jnp.bfloat16)
    )
    moe_term = jnp.einsum(
        "jtnc,njcd->jtd", share_table, expert_out, preferred_element_type=jnp.float32
    )
    hidden_block = lax.dynamic_slice_in_dim(
        hidden_state, shard_index * feature_block, feature_block, 2
    )
    mixed_block = (hidden_block + moe_term).astype(jnp.bfloat16)
    mixed_out = lax.all_gather(mixed_block, "shard", axis=2, tiled=True)
    return mixed_out


def solution(mesh):
    return jax.shard_map(
        on_device,
        mesh=mesh,
        in_specs=(
            P("req", "exp", None),
            P("req", "exp", None),
            P("req", "exp", None),
            P("req", "exp", None),
            P(),
            P("req", None),
            P("req", None),
            P("req", ("exp", "shard"), None, None),
            P("req", ("exp", "shard"), None, None),
            P(),
            P("shard", None),
            P("exp", None, "shard", None),
            P("exp", "shard", None),
        ),
        out_specs=P("req", "exp", None),
        check_vma=False,
    )
```

```python
import math

import jax
import jax.numpy as jnp
from jax import lax
from jax.sharding import PartitionSpec as P

H = 36


NEG_FILL = -1e30
EPSILON = 1e-06


def expert_rows(received, gate_up, down_proj):
    width = received.shape[-1]
    flat_rows = received.reshape(-1, width)
    both = lax.dot_general(
        flat_rows, gate_up[0], (((1,), (2,)), ((), ())), preferred_element_type=jnp.float32
    )
    active = (jax.nn.silu(both[:, 0]) * both[:, 1]).astype(jnp.bfloat16)
    partial_out = jnp.dot(active, down_proj[0], preferred_element_type=jnp.float32)
    return partial_out.reshape(received.shape)


def gather_blocks(block, axis_name, count):
    spread = jnp.broadcast_to(block[None], (count,) + block.shape)
    return lax.all_to_all(spread, axis_name, 0, 0, tiled=False)


def on_device(
    query_stretch,
    resid_stretch,
    route_ids,
    route_probs,
    request_order,
    prior_pages,
    page_order,
    key_pool,
    value_pool,
    norm_gain,
    out_proj,
    gate_up,
    down_proj,
):
    members = prior_pages.shape[1]
    tokens_here = query_stretch.shape[1]
    width = query_stretch.shape[2]
    head_size = width // H
    group_index = lax.axis_index("req")
    exp_index = lax.axis_index("exp")
    shard_index = lax.axis_index("shard")
    shard_count = lax.axis_size("shard")
    experts_count = lax.axis_size("exp")
    extras = jnp.concatenate(
        [resid_stretch, route_probs, route_ids.astype(jnp.bfloat16)], axis=2
    )
    all_query = lax.all_gather(query_stretch, "req", axis=0, tiled=True)
    all_extras = lax.all_gather(extras, "req", axis=0, tiled=True)
    served = lax.dynamic_slice_in_dim(request_order, group_index * members, members)
    served_query = jnp.take(all_query, served, axis=0)
    served_extras = jnp.take(all_extras, served, axis=0)
    spread_query = jnp.broadcast_to(
        served_query[None], (experts_count,) + served_query.shape
    )
    group_query = lax.all_to_all(spread_query, "exp", 0, 0, tiled=False)
    group_query, served_extras = lax.optimization_barrier((group_query, served_extras))
    top_count = route_ids.shape[2]
    served_resid = served_extras[:, :, :width]
    served_probs = served_extras[:, :, width : width + top_count]
    served_ids = served_extras[:, :, width + top_count :].astype(jnp.int32)
    pages_here = key_pool.shape[1]
    page_size = key_pool.shape[2]
    keys_here = pages_here * page_size
    device_index = exp_index * shard_count + shard_index
    physical = device_index * pages_here + jnp.arange(pages_here, dtype=jnp.int32)
    page_row = page_order[0]
    pool_size = page_row.shape[0]
    matched = page_row[None, :] == physical[:, None]
    located = jnp.sum(
        jnp.where(matched, jnp.arange(pool_size, dtype=jnp.int32)[None, :], 0), axis=1
    )
    prior_row = prior_pages[0]
    page_counts = prior_row + experts_count * tokens_here // page_size
    page_ends = jnp.cumsum(page_counts)
    page_starts = page_ends - page_counts
    owner_slot = jnp.sum((located[:, None] >= page_ends[None, :]).astype(jnp.int32), axis=1)
    owner_hot = owner_slot[:, None] == jnp.arange(members, dtype=jnp.int32)[None, :]
    logical = located - jnp.sum(jnp.where(owner_hot, page_starts[None, :], 0), axis=1)
    key_place = (
        logical[:, None] * page_size + jnp.arange(page_size, dtype=jnp.int32)[None, :]
    ).reshape(keys_here)
    key_owner = jnp.repeat(owner_slot, page_size)
    query_place = (
        prior_row[None, :, None] * page_size
        + jnp.arange(experts_count, dtype=jnp.int32)[:, None, None] * tokens_here
        + jnp.arange(tokens_here, dtype=jnp.int32)[None, None, :]
    )
    visible = (key_owner[None, None, None, :] == jnp.arange(members, dtype=jnp.int32)[None, :, None, None]) & (
        key_place[None, None, None, :] <= query_place[..., None]
    )
    query_rows = group_query.reshape(experts_count, members, tokens_here, H, head_size)
    key_rows = key_pool[0].reshape(keys_here, H, head_size)
    value_rows = value_pool[0].reshape(keys_here, H, head_size)
    scores = jnp.einsum(
        "ejthd,khd->ejhtk", query_rows, key_rows, preferred_element_type=jnp.float32
    ) * (1.0 / math.sqrt(head_size))
    scores = jnp.where(visible[:, :, None], scores, NEG_FILL)
    local_peak = jnp.max(scores, axis=4).astype(jnp.bfloat16).astype(jnp.float32)
    weights_bf = jnp.where(
        visible[:, :, None], jnp.exp(scores - local_peak[..., None]), 0.0
    ).astype(jnp.bfloat16)
    totals = jnp.sum(weights_bf, axis=4, dtype=jnp.float32)
    context = jnp.einsum(
        "ejhtk,khd->ejthd", weights_bf, value_rows, preferred_element_type=jnp.float32
    ).reshape(experts_count, members, tokens_here, width)
    packed = jnp.concatenate(
        [
            context.astype(jnp.bfloat16),
            jnp.transpose(local_peak, (0, 1, 3, 2)).astype(jnp.bfloat16),
            jnp.transpose(totals, (0, 1, 3, 2)).astype(jnp.bfloat16),
        ],
        axis=3,
    )
    packed_width = packed.shape[3]
    rows_each = members * tokens_here // shard_count
    packed = packed.reshape(experts_count * shard_count, rows_each, packed_width)
    arrived = lax.all_to_all(packed, ("exp", "shard"), 0, 0, tiled=True).astype(jnp.float32)
    arrived_context = arrived[:, :, :width].reshape(-1, rows_each, H, head_size)
    arrived_peak = arrived[:, :, width : width + H]
    arrived_totals = arrived[:, :, width + H : width + 2 * H]
    row_peak = jnp.max(arrived_peak, axis=0)
    rescale = jnp.exp(arrived_peak - row_peak[None])
    row_totals = jnp.sum(rescale * arrived_totals, axis=0)
    row_context = jnp.sum(rescale[..., None] * arrived_context, axis=0)
    row_attended = (
        (row_context / row_totals[..., None]).reshape(rows_each, width).astype(jnp.bfloat16)
    )
    attended = gather_blocks(row_attended, "shard", shard_count).reshape(
        members, tokens_here, width
    )
    projected_part = lax.dot_general(
        attended, out_proj, (((2,), (1,)), ((), ())), preferred_element_type=jnp.float32
    ).astype(jnp.bfloat16)
    projected = jnp.transpose(
        gather_blocks(projected_part, "shard", shard_count), (1, 2, 0, 3)
    ).reshape(members, tokens_here, width)
    hidden_state = served_resid.astype(jnp.float32) + projected.astype(jnp.float32)
    mean_square = jnp.mean(hidden_state * hidden_state, axis=2, keepdims=True)
    normed = (hidden_state * lax.rsqrt(mean_square + EPSILON) * norm_gain).astype(jnp.bfloat16)
    capacity = min(tokens_here, max(2, 3 * tokens_here * top_count // (2 * experts_count)))
    flat_ids = served_ids.reshape(members, tokens_here * top_count)
    expert_hot = (
        flat_ids[:, :, None] == jnp.arange(experts_count, dtype=jnp.int32)[None, None, :]
    ).astype(jnp.int32)
    before = jnp.cumsum(expert_hot, axis=1) - expert_hot
    slot_place = jnp.sum(before * expert_hot, axis=2)
    slot_hot = (
        slot_place[:, :, None] == jnp.arange(capacity, dtype=jnp.int32)[None, None, :]
    ).astype(jnp.int32)
    place_table = (expert_hot[:, :, :, None] * slot_hot[:, :, None, :]).reshape(
        members, tokens_here, top_count, experts_count, capacity
    )
    pick_table = jnp.sum(place_table, axis=2).astype(jnp.bfloat16)
    sent_rows = jnp.einsum(
        "jtnc,jtd->njcd", pick_table, normed, preferred_element_type=jnp.float32
    ).astype(jnp.bfloat16)
    share_table = jnp.sum(
        place_table.astype(jnp.bfloat16) * served_probs[:, :, :, None, None], axis=2
    )
    partial_out = expert_rows(
        lax.all_to_all(sent_rows, "exp", split_axis=0, concat_axis=0, tiled=True),
        gate_up,
        down_proj,
    ).astype(jnp.bfloat16)
    feature_block = width // shard_count
    partial_out = partial_out.reshape(
        experts_count, members, capacity, shard_count, feature_block
    )
    partial_out = jnp.transpose(partial_out, (0, 3, 1, 2, 4)).reshape(
        experts_count * shard_count, members, capacity, feature_block
    )
    gathered_parts = lax.all_to_all(partial_out, ("exp", "shard"), 0, 0, tiled=True)
    expert_out = (
        jnp.sum(
            gathered_parts.reshape(
                experts_count, shard_count, members, capacity, feature_block
            ).astype(jnp.float32),
            axis=1,
        )
        .astype(jnp.bfloat16)
    )
    moe_term = jnp.einsum(
        "jtnc,njcd->jtd", share_table, expert_out, preferred_element_type=jnp.float32
    )
    hidden_block = lax.dynamic_slice_in_dim(
        hidden_state, shard_index * feature_block, feature_block, 2
    )
    mixed_block = (hidden_block + moe_term).astype(jnp.bfloat16)
    mixed_out = jnp.transpose(
        gather_blocks(mixed_block, "shard", shard_count), (1, 2, 0, 3)
    ).reshape(members, tokens_here, width)
    return mixed_out


def solution(mesh):
    return jax.shard_map(
        on_device,
        mesh=mesh,
        in_specs=(
            P("req", "exp", None),
            P("req", "exp", None),
            P("req", "exp", None),
            P("req", "exp", None),
            P(),
            P("req", None),
            P("req", None),
            P("req", ("exp", "shard"), None, None),
            P("req", ("exp", "shard"), None, None),
            P(),
            P("shard", None),
            P("exp", None, "shard", None),
            P("exp", "shard", None),
        ),
        out_specs=P("req", "exp", None),
        check_vma=False,
    )
```

```python
import math

import jax
import jax.numpy as jnp
from jax import lax
from jax.sharding import PartitionSpec as P

H = 36


NEG_FILL = -1e30
EPSILON = 1e-06


def expert_rows(received, gate_up, down_proj):
    width = received.shape[-1]
    flat_rows = received.reshape(-1, width)
    both = lax.dot_general(
        flat_rows, gate_up[0], (((1,), (2,)), ((), ())), preferred_element_type=jnp.float32
    )
    active = (jax.nn.silu(both[:, 0]) * both[:, 1]).astype(jnp.bfloat16)
    partial_out = jnp.dot(active, down_proj[0], preferred_element_type=jnp.float32)
    return partial_out.reshape(received.shape)


def gather_blocks(block, axis_name, count):
    spread = jnp.broadcast_to(block[None], (count,) + block.shape)
    return lax.all_to_all(spread, axis_name, 0, 0, tiled=False)


def on_device(
    query_stretch,
    resid_stretch,
    route_ids,
    route_probs,
    request_order,
    prior_pages,
    page_order,
    key_pool,
    value_pool,
    norm_gain,
    out_proj,
    gate_up,
    down_proj,
):
    members = prior_pages.shape[1]
    tokens_here = query_stretch.shape[1]
    width = query_stretch.shape[2]
    head_size = width // H
    group_index = lax.axis_index("req")
    exp_index = lax.axis_index("exp")
    shard_index = lax.axis_index("shard")
    shard_count = lax.axis_size("shard")
    experts_count = lax.axis_size("exp")
    extras = jnp.concatenate(
        [resid_stretch, route_probs, route_ids.astype(jnp.bfloat16)], axis=2
    )
    all_query = lax.all_gather(query_stretch, "req", axis=0, tiled=True)
    all_extras = lax.all_gather(extras, "req", axis=0, tiled=True)
    served = lax.dynamic_slice_in_dim(request_order, group_index * members, members)
    served_query = jnp.take(all_query, served, axis=0)
    served_extras = jnp.take(all_extras, served, axis=0)
    core_index = shard_index % 2
    own_member = lax.dynamic_slice_in_dim(served_query, core_index, 1, 0)
    own_query = gather_blocks(own_member, "exp", experts_count)
    partner_query = lax.ppermute(
        own_query, "shard", [(i, i ^ 1) for i in range(shard_count)]
    )
    group_query = jnp.where(
        core_index == 0,
        jnp.concatenate([own_query, partner_query], axis=1),
        jnp.concatenate([partner_query, own_query], axis=1),
    )
    group_query, served_extras = lax.optimization_barrier((group_query, served_extras))
    top_count = route_ids.shape[2]
    served_resid = served_extras[:, :, :width]
    served_probs = served_extras[:, :, width : width + top_count]
    served_ids = served_extras[:, :, width + top_count :].astype(jnp.int32)
    pages_here = key_pool.shape[1]
    page_size = key_pool.shape[2]
    keys_here = pages_here * page_size
    device_index = exp_index * shard_count + shard_index
    physical = device_index * pages_here + jnp.arange(pages_here, dtype=jnp.int32)
    page_row = page_order[0]
    pool_size = page_row.shape[0]
    matched = page_row[None, :] == physical[:, None]
    located = jnp.sum(
        jnp.where(matched, jnp.arange(pool_size, dtype=jnp.int32)[None, :], 0), axis=1
    )
    prior_row = prior_pages[0]
    page_counts = prior_row + experts_count * tokens_here // page_size
    page_ends = jnp.cumsum(page_counts)
    page_starts = page_ends - page_counts
    owner_slot = jnp.sum((located[:, None] >= page_ends[None, :]).astype(jnp.int32), axis=1)
    owner_hot = owner_slot[:, None] == jnp.arange(members, dtype=jnp.int32)[None, :]
    logical = located - jnp.sum(jnp.where(owner_hot, page_starts[None, :], 0), axis=1)
    key_place = (
        logical[:, None] * page_size + jnp.arange(page_size, dtype=jnp.int32)[None, :]
    ).reshape(keys_here)
    key_owner = jnp.repeat(owner_slot, page_size)
    query_place = (
        prior_row[None, :, None] * page_size
        + jnp.arange(experts_count, dtype=jnp.int32)[:, None, None] * tokens_here
        + jnp.arange(tokens_here, dtype=jnp.int32)[None, None, :]
    )
    visible = (key_owner[None, None, None, :] == jnp.arange(members, dtype=jnp.int32)[None, :, None, None]) & (
        key_place[None, None, None, :] <= query_place[..., None]
    )
    query_rows = group_query.reshape(experts_count, members, tokens_here, H, head_size)
    key_rows = key_pool[0].reshape(keys_here, H, head_size)
    value_rows = value_pool[0].reshape(keys_here, H, head_size)
    scores = jnp.einsum(
        "ejthd,khd->ejhtk", query_rows, key_rows, preferred_element_type=jnp.float32
    ) * (1.0 / math.sqrt(head_size))
    scores = jnp.where(visible[:, :, None], scores, NEG_FILL)
    local_peak = jnp.max(scores, axis=4).astype(jnp.bfloat16).astype(jnp.float32)
    weights_bf = jnp.where(
        visible[:, :, None], jnp.exp(scores - local_peak[..., None]), 0.0
    ).astype(jnp.bfloat16)
    totals = jnp.sum(weights_bf, axis=4, dtype=jnp.float32)
    context = jnp.einsum(
        "ejhtk,khd->ejthd", weights_bf, value_rows, preferred_element_type=jnp.float32
    ).reshape(experts_count, members, tokens_here, width)
    packed = jnp.concatenate(
        [
            context.astype(jnp.bfloat16),
            jnp.transpose(local_peak, (0, 1, 3, 2)).astype(jnp.bfloat16),
            jnp.transpose(totals, (0, 1, 3, 2)).astype(jnp.bfloat16),
        ],
        axis=3,
    )
    packed_width = packed.shape[3]
    rows_each = members * tokens_here // shard_count
    packed = packed.reshape(experts_count * shard_count, rows_each, packed_width)
    arrived = lax.all_to_all(packed, ("exp", "shard"), 0, 0, tiled=True).astype(jnp.float32)
    arrived_context = arrived[:, :, :width].reshape(-1, rows_each, H, head_size)
    arrived_peak = arrived[:, :, width : width + H]
    arrived_totals = arrived[:, :, width + H : width + 2 * H]
    row_peak = jnp.max(arrived_peak, axis=0)
    rescale = jnp.exp(arrived_peak - row_peak[None])
    row_totals = jnp.sum(rescale * arrived_totals, axis=0)
    row_context = jnp.sum(rescale[..., None] * arrived_context, axis=0)
    row_attended = (
        (row_context / row_totals[..., None]).reshape(rows_each, width).astype(jnp.bfloat16)
    )
    attended = gather_blocks(row_attended, "shard", shard_count).reshape(
        members, tokens_here, width
    )
    projected_part = lax.dot_general(
        attended, out_proj, (((2,), (1,)), ((), ())), preferred_element_type=jnp.float32
    ).astype(jnp.bfloat16)
    projected = jnp.transpose(
        gather_blocks(projected_part, "shard", shard_count), (1, 2, 0, 3)
    ).reshape(members, tokens_here, width)
    hidden_state = served_resid.astype(jnp.float32) + projected.astype(jnp.float32)
    mean_square = jnp.mean(hidden_state * hidden_state, axis=2, keepdims=True)
    normed = (hidden_state * lax.rsqrt(mean_square + EPSILON) * norm_gain).astype(jnp.bfloat16)
    capacity = min(tokens_here, max(2, 3 * tokens_here * top_count // (2 * experts_count)))
    flat_ids = served_ids.reshape(members, tokens_here * top_count)
    expert_hot = (
        flat_ids[:, :, None] == jnp.arange(experts_count, dtype=jnp.int32)[None, None, :]
    ).astype(jnp.int32)
    before = jnp.cumsum(expert_hot, axis=1) - expert_hot
    slot_place = jnp.sum(before * expert_hot, axis=2)
    slot_hot = (
        slot_place[:, :, None] == jnp.arange(capacity, dtype=jnp.int32)[None, None, :]
    ).astype(jnp.int32)
    place_table = (expert_hot[:, :, :, None] * slot_hot[:, :, None, :]).reshape(
        members, tokens_here, top_count, experts_count, capacity
    )
    pick_table = jnp.sum(place_table, axis=2).astype(jnp.bfloat16)
    sent_rows = jnp.einsum(
        "jtnc,jtd->njcd", pick_table, normed, preferred_element_type=jnp.float32
    ).astype(jnp.bfloat16)
    share_table = jnp.sum(
        place_table.astype(jnp.bfloat16) * served_probs[:, :, :, None, None], axis=2
    )
    partial_out = expert_rows(
        lax.all_to_all(sent_rows, "exp", split_axis=0, concat_axis=0, tiled=True),
        gate_up,
        down_proj,
    ).astype(jnp.bfloat16)
    feature_block = width // shard_count
    partial_out = partial_out.reshape(
        experts_count, members, capacity, shard_count, feature_block
    )
    partial_out = jnp.transpose(partial_out, (0, 3, 1, 2, 4)).reshape(
        experts_count * shard_count, members, capacity, feature_block
    )
    gathered_parts = lax.all_to_all(partial_out, ("exp", "shard"), 0, 0, tiled=True)
    expert_out = (
        jnp.sum(
            gathered_parts.reshape(
                experts_count, shard_count, members, capacity, feature_block
            ).astype(jnp.float32),
            axis=1,
        )
        .astype(jnp.bfloat16)
    )
    moe_term = jnp.einsum(
        "jtnc,njcd->jtd", share_table, expert_out, preferred_element_type=jnp.float32
    )
    hidden_block = lax.dynamic_slice_in_dim(
        hidden_state, shard_index * feature_block, feature_block, 2
    )
    mixed_block = (hidden_block + moe_term).astype(jnp.bfloat16)
    mixed_out = jnp.transpose(
        gather_blocks(mixed_block, "shard", shard_count), (1, 2, 0, 3)
    ).reshape(members, tokens_here, width)
    return mixed_out


def solution(mesh):
    return jax.shard_map(
        on_device,
        mesh=mesh,
        in_specs=(
            P("req", "exp", None),
            P("req", "exp", None),
            P("req", "exp", None),
            P("req", "exp", None),
            P(),
            P("req", None),
            P("req", None),
            P("req", ("exp", "shard"), None, None),
            P("req", ("exp", "shard"), None, None),
            P(),
            P("shard", None),
            P("exp", None, "shard", None),
            P("exp", "shard", None),
        ),
        out_specs=P("req", "exp", None),
        check_vma=False,
    )
```

```python
import math

import jax
import jax.numpy as jnp
from jax import lax
from jax.sharding import PartitionSpec as P

H = 36


NEG_FILL = -1e30
EPSILON = 1e-06


def expert_rows(received, gate_up, down_proj):
    width = received.shape[-1]
    flat_rows = received.reshape(-1, width)
    both = lax.dot_general(
        flat_rows, gate_up[0], (((1,), (2,)), ((), ())), preferred_element_type=jnp.float32
    )
    active = (jax.nn.silu(both[:, 0]) * both[:, 1]).astype(jnp.bfloat16)
    partial_out = jnp.dot(active, down_proj[0], preferred_element_type=jnp.float32)
    return partial_out.reshape(received.shape)


def gather_blocks(block, axis_name, count):
    spread = jnp.broadcast_to(block[None], (count,) + block.shape)
    return lax.all_to_all(spread, axis_name, 0, 0, tiled=False)


def on_device(
    query_stretch,
    resid_stretch,
    route_ids,
    route_probs,
    request_order,
    prior_pages,
    page_order,
    key_pool,
    value_pool,
    norm_gain,
    out_proj,
    gate_up,
    down_proj,
):
    members = prior_pages.shape[1]
    tokens_here = query_stretch.shape[1]
    width = query_stretch.shape[2]
    head_size = width // H
    group_index = lax.axis_index("req")
    exp_index = lax.axis_index("exp")
    shard_index = lax.axis_index("shard")
    shard_count = lax.axis_size("shard")
    experts_count = lax.axis_size("exp")
    extras = jnp.concatenate(
        [resid_stretch, route_probs, route_ids.astype(jnp.bfloat16)], axis=2
    )
    all_query = lax.all_gather(query_stretch, "req", axis=0, tiled=True)
    all_extras = lax.all_gather(extras, "req", axis=0, tiled=True)
    served = lax.dynamic_slice_in_dim(request_order, group_index * members, members)
    served_query = jnp.take(all_query, served, axis=0)
    served_extras = jnp.take(all_extras, served, axis=0)
    core_index = shard_index % 2
    own_member = lax.dynamic_slice_in_dim(served_query, core_index, 1, 0)
    own_query = gather_blocks(own_member, "exp", experts_count)
    partner_query = lax.ppermute(
        own_query, "shard", [(i, i ^ 1) for i in range(shard_count)]
    )
    group_query = jnp.where(
        core_index == 0,
        jnp.concatenate([own_query, partner_query], axis=1),
        jnp.concatenate([partner_query, own_query], axis=1),
    )
    group_query, served_extras = lax.optimization_barrier((group_query, served_extras))
    top_count = route_ids.shape[2]
    served_resid = served_extras[:, :, :width]
    served_probs = served_extras[:, :, width : width + top_count]
    served_ids = served_extras[:, :, width + top_count :].astype(jnp.int32)
    pages_here = key_pool.shape[1]
    page_size = key_pool.shape[2]
    keys_here = pages_here * page_size
    device_index = exp_index * shard_count + shard_index
    physical = device_index * pages_here + jnp.arange(pages_here, dtype=jnp.int32)
    page_row = page_order[0]
    pool_size = page_row.shape[0]
    matched = page_row[None, :] == physical[:, None]
    located = jnp.sum(
        jnp.where(matched, jnp.arange(pool_size, dtype=jnp.int32)[None, :], 0), axis=1
    )
    prior_row = prior_pages[0]
    page_counts = prior_row + experts_count * tokens_here // page_size
    page_ends = jnp.cumsum(page_counts)
    page_starts = page_ends - page_counts
    owner_slot = jnp.sum((located[:, None] >= page_ends[None, :]).astype(jnp.int32), axis=1)
    owner_hot = owner_slot[:, None] == jnp.arange(members, dtype=jnp.int32)[None, :]
    logical = located - jnp.sum(jnp.where(owner_hot, page_starts[None, :], 0), axis=1)
    key_place = (
        logical[:, None] * page_size + jnp.arange(page_size, dtype=jnp.int32)[None, :]
    ).reshape(keys_here)
    key_owner = jnp.repeat(owner_slot, page_size)
    query_place = (
        prior_row[None, :, None] * page_size
        + jnp.arange(experts_count, dtype=jnp.int32)[:, None, None] * tokens_here
        + jnp.arange(tokens_here, dtype=jnp.int32)[None, None, :]
    )
    visible = (key_owner[None, None, None, :] == jnp.arange(members, dtype=jnp.int32)[None, :, None, None]) & (
        key_place[None, None, None, :] <= query_place[..., None]
    )
    query_rows = group_query.reshape(experts_count, members, tokens_here, H, head_size)
    key_rows = key_pool[0].reshape(keys_here, H, head_size)
    value_rows = value_pool[0].reshape(keys_here, H, head_size)
    scores = jnp.einsum(
        "ejthd,khd->ejhtk", query_rows, key_rows, preferred_element_type=jnp.float32
    ) * (1.0 / math.sqrt(head_size))
    scores = jnp.where(visible[:, :, None], scores, NEG_FILL)
    local_peak = jnp.max(scores, axis=4).astype(jnp.bfloat16).astype(jnp.float32)
    weights_bf = jnp.where(
        visible[:, :, None], jnp.exp(scores - local_peak[..., None]), 0.0
    ).astype(jnp.bfloat16)
    totals = jnp.sum(weights_bf, axis=4, dtype=jnp.float32)
    context = jnp.einsum(
        "ejhtk,khd->ejthd", weights_bf, value_rows, preferred_element_type=jnp.float32
    ).reshape(experts_count, members, tokens_here, width)
    half_width = width // 2
    half_heads = H // 2
    own_peak = jnp.transpose(local_peak, (0, 1, 3, 2))
    own_totals = jnp.transpose(totals, (0, 1, 3, 2)).astype(jnp.bfloat16).astype(jnp.float32)
    low_context = context[..., :half_width]
    high_context = context[..., half_width:]
    keep_context = jnp.where(core_index == 0, low_context, high_context)
    give_context = jnp.where(core_index == 0, high_context, low_context)
    message = jnp.concatenate(
        [
            give_context.astype(jnp.bfloat16),
            own_peak.astype(jnp.bfloat16),
            own_totals.astype(jnp.bfloat16),
        ],
        axis=3,
    )
    message = lax.ppermute(message, "shard", [(i, i ^ 1) for i in range(shard_count)])
    other_context = message[..., :half_width].astype(jnp.float32)
    other_peak = message[..., half_width : half_width + H].astype(jnp.float32)
    other_totals = message[..., half_width + H :].astype(jnp.float32)
    pair_peak = jnp.maximum(own_peak, other_peak)
    own_scale = jnp.exp(own_peak - pair_peak)
    other_scale = jnp.exp(other_peak - pair_peak)
    pair_totals = own_scale * own_totals + other_scale * other_totals

    def half_scale(scale):
        kept = jnp.where(core_index == 0, scale[..., :half_heads], scale[..., half_heads:])
        return jnp.repeat(kept, head_size, axis=3)

    pair_context = half_scale(own_scale) * keep_context + half_scale(other_scale) * other_context
    packed = jnp.concatenate(
        [
            pair_context.astype(jnp.bfloat16),
            pair_peak.astype(jnp.bfloat16),
            pair_totals.astype(jnp.bfloat16),
        ],
        axis=3,
    )
    packed_width = packed.shape[3]
    rows_each = members * tokens_here // shard_count
    packed = packed.reshape(experts_count * shard_count, rows_each, packed_width)
    arrived = lax.all_to_all(packed, ("exp", "shard"), 0, 0, tiled=True)
    arrived = arrived.reshape(-1, 2, rows_each, packed_width)
    arrived_peak = arrived[:, 0, :, half_width : half_width + H].astype(jnp.float32)
    arrived_totals = arrived[:, 0, :, half_width + H :].astype(jnp.float32)
    row_peak = jnp.max(arrived_peak, axis=0)
    rescale = jnp.exp(arrived_peak - row_peak[None])
    row_totals = jnp.sum(rescale * arrived_totals, axis=0)
    row_halves = []
    for half in range(2):
        half_rescale = jnp.repeat(
            rescale[:, :, half * half_heads : (half + 1) * half_heads], head_size, axis=2
        )
        row_halves.append(
            jnp.sum(
                half_rescale * arrived[:, half, :, :half_width].astype(jnp.float32), axis=0
            )
        )
    row_context = jnp.concatenate(row_halves, axis=1)
    row_attended = (row_context / jnp.repeat(row_totals, head_size, axis=1)).astype(
        jnp.bfloat16
    )
    attended = gather_blocks(row_attended, "shard", shard_count).reshape(
        members, tokens_here, width
    )
    projected_part = lax.dot_general(
        attended, out_proj, (((2,), (1,)), ((), ())), preferred_element_type=jnp.float32
    ).astype(jnp.bfloat16)
    projected = jnp.transpose(
        gather_blocks(projected_part, "shard", shard_count), (1, 2, 0, 3)
    ).reshape(members, tokens_here, width)
    hidden_state = served_resid.astype(jnp.float32) + projected.astype(jnp.float32)
    mean_square = jnp.mean(hidden_state * hidden_state, axis=2, keepdims=True)
    normed = (hidden_state * lax.rsqrt(mean_square + EPSILON) * norm_gain).astype(jnp.bfloat16)
    capacity = min(tokens_here, max(2, 3 * tokens_here * top_count // (2 * experts_count)))
    flat_ids = served_ids.reshape(members, tokens_here * top_count)
    expert_hot = (
        flat_ids[:, :, None] == jnp.arange(experts_count, dtype=jnp.int32)[None, None, :]
    ).astype(jnp.int32)
    before = jnp.cumsum(expert_hot, axis=1) - expert_hot
    slot_place = jnp.sum(before * expert_hot, axis=2)
    slot_hot = (
        slot_place[:, :, None] == jnp.arange(capacity, dtype=jnp.int32)[None, None, :]
    ).astype(jnp.int32)
    place_table = (expert_hot[:, :, :, None] * slot_hot[:, :, None, :]).reshape(
        members, tokens_here, top_count, experts_count, capacity
    )
    pick_table = jnp.sum(place_table, axis=2).astype(jnp.bfloat16)
    sent_rows = jnp.einsum(
        "jtnc,jtd->njcd", pick_table, normed, preferred_element_type=jnp.float32
    ).astype(jnp.bfloat16)
    share_table = jnp.sum(
        place_table.astype(jnp.bfloat16) * served_probs[:, :, :, None, None], axis=2
    )
    partial_out = expert_rows(
        lax.all_to_all(sent_rows, "exp", split_axis=0, concat_axis=0, tiled=True),
        gate_up,
        down_proj,
    ).astype(jnp.bfloat16)
    feature_block = width // shard_count
    partial_out = partial_out.reshape(
        experts_count, members, capacity, shard_count, feature_block
    )
    partial_out = jnp.transpose(partial_out, (0, 3, 1, 2, 4)).reshape(
        experts_count * shard_count, members, capacity, feature_block
    )
    gathered_parts = lax.all_to_all(partial_out, ("exp", "shard"), 0, 0, tiled=True)
    expert_out = (
        jnp.sum(
            gathered_parts.reshape(
                experts_count, shard_count, members, capacity, feature_block
            ).astype(jnp.float32),
            axis=1,
        )
        .astype(jnp.bfloat16)
    )
    moe_term = jnp.einsum(
        "jtnc,njcd->jtd", share_table, expert_out, preferred_element_type=jnp.float32
    )
    hidden_block = lax.dynamic_slice_in_dim(
        hidden_state, shard_index * feature_block, feature_block, 2
    )
    mixed_block = (hidden_block + moe_term).astype(jnp.bfloat16)
    mixed_out = jnp.transpose(
        gather_blocks(mixed_block, "shard", shard_count), (1, 2, 0, 3)
    ).reshape(members, tokens_here, width)
    return mixed_out


def solution(mesh):
    return jax.shard_map(
        on_device,
        mesh=mesh,
        in_specs=(
            P("req", "exp", None),
            P("req", "exp", None),
            P("req", "exp", None),
            P("req", "exp", None),
            P(),
            P("req", None),
            P("req", None),
            P("req", ("exp", "shard"), None, None),
            P("req", ("exp", "shard"), None, None),
            P(),
            P("shard", None),
            P("exp", None, "shard", None),
            P("exp", "shard", None),
        ),
        out_specs=P("req", "exp", None),
        check_vma=False,
    )
```

```python
import math

import jax
import jax.numpy as jnp
from jax import lax
from jax.sharding import PartitionSpec as P

H = 36


NEG_FILL = -1e30
EPSILON = 1e-06


def expert_rows(received, gate_up, down_proj):
    width = received.shape[-1]
    flat_rows = received.reshape(-1, width)
    both = lax.dot_general(
        flat_rows, gate_up[0], (((1,), (2,)), ((), ())), preferred_element_type=jnp.float32
    )
    active = (jax.nn.silu(both[:, 0]) * both[:, 1]).astype(jnp.bfloat16)
    partial_out = jnp.dot(active, down_proj[0], preferred_element_type=jnp.float32)
    return partial_out.reshape(received.shape)


def gather_blocks(block, axis_name, count):
    spread = jnp.broadcast_to(block[None], (count,) + block.shape)
    return lax.all_to_all(spread, axis_name, 0, 0, tiled=False)


def on_device(
    query_stretch,
    resid_stretch,
    route_ids,
    route_probs,
    request_order,
    prior_pages,
    page_order,
    key_pool,
    value_pool,
    norm_gain,
    out_proj,
    gate_up,
    down_proj,
):
    members = prior_pages.shape[1]
    tokens_here = query_stretch.shape[1]
    width = query_stretch.shape[2]
    head_size = width // H
    group_index = lax.axis_index("req")
    exp_index = lax.axis_index("exp")
    shard_index = lax.axis_index("shard")
    shard_count = lax.axis_size("shard")
    experts_count = lax.axis_size("exp")
    extras = jnp.concatenate(
        [resid_stretch, route_probs, route_ids.astype(jnp.bfloat16)], axis=2
    )
    all_query = lax.all_gather(query_stretch, "req", axis=0, tiled=True)
    all_extras = lax.all_gather(extras, "req", axis=0, tiled=True)
    served = lax.dynamic_slice_in_dim(request_order, group_index * members, members)
    served_query = jnp.take(all_query, served, axis=0)
    served_extras = jnp.take(all_extras, served, axis=0)
    core_index = shard_index % 2
    own_member = lax.dynamic_slice_in_dim(served_query, core_index, 1, 0)
    own_query = gather_blocks(own_member, "exp", experts_count)
    partner_query = lax.ppermute(
        own_query, "shard", [(i, i ^ 1) for i in range(shard_count)]
    )
    group_query = jnp.where(
        core_index == 0,
        jnp.concatenate([own_query, partner_query], axis=1),
        jnp.concatenate([partner_query, own_query], axis=1),
    )
    group_query, served_extras = lax.optimization_barrier((group_query, served_extras))
    top_count = route_ids.shape[2]
    served_resid = served_extras[:, :, :width]
    served_probs = served_extras[:, :, width : width + top_count]
    served_ids = served_extras[:, :, width + top_count :].astype(jnp.int32)
    pages_here = key_pool.shape[1]
    page_size = key_pool.shape[2]
    keys_here = pages_here * page_size
    device_index = exp_index * shard_count + shard_index
    physical = device_index * pages_here + jnp.arange(pages_here, dtype=jnp.int32)
    page_row = page_order[0]
    pool_size = page_row.shape[0]
    matched = page_row[None, :] == physical[:, None]
    located = jnp.sum(
        jnp.where(matched, jnp.arange(pool_size, dtype=jnp.int32)[None, :], 0), axis=1
    )
    prior_row = prior_pages[0]
    page_counts = prior_row + experts_count * tokens_here // page_size
    page_ends = jnp.cumsum(page_counts)
    page_starts = page_ends - page_counts
    owner_slot = jnp.sum((located[:, None] >= page_ends[None, :]).astype(jnp.int32), axis=1)
    owner_hot = owner_slot[:, None] == jnp.arange(members, dtype=jnp.int32)[None, :]
    logical = located - jnp.sum(jnp.where(owner_hot, page_starts[None, :], 0), axis=1)
    key_place = (
        logical[:, None] * page_size + jnp.arange(page_size, dtype=jnp.int32)[None, :]
    ).reshape(keys_here)
    key_owner = jnp.repeat(owner_slot, page_size)
    query_place = (
        prior_row[None, :, None] * page_size
        + jnp.arange(experts_count, dtype=jnp.int32)[:, None, None] * tokens_here
        + jnp.arange(tokens_here, dtype=jnp.int32)[None, None, :]
    )
    visible = (key_owner[None, None, None, :] == jnp.arange(members, dtype=jnp.int32)[None, :, None, None]) & (
        key_place[None, None, None, :] <= query_place[..., None]
    )
    query_rows = group_query.reshape(experts_count, members, tokens_here, H, head_size)
    key_rows = key_pool[0].reshape(keys_here, H, head_size)
    value_rows = value_pool[0].reshape(keys_here, H, head_size)
    scores = jnp.einsum(
        "ejthd,khd->ejhtk", query_rows, key_rows, preferred_element_type=jnp.float32
    ) * (1.0 / math.sqrt(head_size))
    scores = jnp.where(visible[:, :, None], scores, NEG_FILL)
    local_peak = jnp.max(scores, axis=4).astype(jnp.bfloat16).astype(jnp.float32)
    weights_bf = jnp.where(
        visible[:, :, None], jnp.exp(scores - local_peak[..., None]), 0.0
    ).astype(jnp.bfloat16)
    totals = jnp.sum(weights_bf, axis=4, dtype=jnp.float32)
    context = jnp.einsum(
        "ejhtk,khd->ejthd", weights_bf, value_rows, preferred_element_type=jnp.float32
    ).reshape(experts_count, members, tokens_here, width)
    half_width = width // 2
    half_heads = H // 2
    own_peak = jnp.transpose(local_peak, (0, 1, 3, 2))
    own_totals = jnp.transpose(totals, (0, 1, 3, 2)).astype(jnp.bfloat16).astype(jnp.float32)
    head_of_column = jnp.arange(half_width, dtype=jnp.int32) // head_size
    widen_table = (
        jnp.arange(half_heads, dtype=jnp.int32)[:, None] == head_of_column[None, :]
    ).astype(jnp.float32)

    def widen(scale):
        return jnp.einsum(
            "...h,hc->...c", scale, widen_table, precision=lax.Precision.HIGHEST
        )

    keep_context = lax.dynamic_slice_in_dim(context, core_index * half_width, half_width, 3)
    give_context = lax.dynamic_slice_in_dim(
        context, (1 - core_index) * half_width, half_width, 3
    )
    message = jnp.concatenate(
        [
            give_context.astype(jnp.bfloat16),
            own_peak.astype(jnp.bfloat16),
            own_totals.astype(jnp.bfloat16),
        ],
        axis=3,
    )
    message = lax.ppermute(message, "shard", [(i, i ^ 1) for i in range(shard_count)])
    other_context = message[..., :half_width].astype(jnp.float32)
    other_peak = message[..., half_width : half_width + H].astype(jnp.float32)
    other_totals = message[..., half_width + H :].astype(jnp.float32)
    pair_peak = jnp.maximum(own_peak, other_peak)
    own_scale = jnp.exp(own_peak - pair_peak)
    other_scale = jnp.exp(other_peak - pair_peak)
    pair_totals = own_scale * own_totals + other_scale * other_totals

    def half_scale(scale):
        return widen(lax.dynamic_slice_in_dim(scale, core_index * half_heads, half_heads, 3))

    pair_context = half_scale(own_scale) * keep_context + half_scale(other_scale) * other_context
    packed = jnp.concatenate(
        [
            pair_context.astype(jnp.bfloat16),
            pair_peak.astype(jnp.bfloat16),
            pair_totals.astype(jnp.bfloat16),
        ],
        axis=3,
    )
    packed_width = packed.shape[3]
    rows_each = members * tokens_here // shard_count
    packed = packed.reshape(experts_count * shard_count, rows_each, packed_width)
    arrived = lax.all_to_all(packed, ("exp", "shard"), 0, 0, tiled=True)
    arrived = arrived.reshape(-1, 2, rows_each, packed_width)
    arrived_peak = arrived[:, 0, :, half_width : half_width + H].astype(jnp.float32)
    arrived_totals = arrived[:, 0, :, half_width + H :].astype(jnp.float32)
    row_peak = jnp.max(arrived_peak, axis=0)
    rescale = jnp.exp(arrived_peak - row_peak[None])
    row_totals = jnp.sum(rescale * arrived_totals, axis=0)
    row_halves = []
    for half in range(2):
        half_rescale = widen(rescale[:, :, half * half_heads : (half + 1) * half_heads])
        half_context = jnp.sum(
            half_rescale * arrived[:, half, :, :half_width].astype(jnp.float32), axis=0
        )
        half_totals = widen(row_totals[:, half * half_heads : (half + 1) * half_heads])
        row_halves.append(half_context / half_totals)
    row_attended = jnp.concatenate(row_halves, axis=1).astype(jnp.bfloat16)
    attended = gather_blocks(row_attended, "shard", shard_count).reshape(
        members, tokens_here, width
    )
    projected_part = lax.dot_general(
        attended, out_proj, (((2,), (1,)), ((), ())), preferred_element_type=jnp.float32
    ).astype(jnp.bfloat16)
    projected = jnp.transpose(
        gather_blocks(projected_part, "shard", shard_count), (1, 2, 0, 3)
    ).reshape(members, tokens_here, width)
    hidden_state = served_resid.astype(jnp.float32) + projected.astype(jnp.float32)
    mean_square = jnp.mean(hidden_state * hidden_state, axis=2, keepdims=True)
    normed = (hidden_state * lax.rsqrt(mean_square + EPSILON) * norm_gain).astype(jnp.bfloat16)
    capacity = min(tokens_here, max(2, 3 * tokens_here * top_count // (2 * experts_count)))
    flat_ids = served_ids.reshape(members, tokens_here * top_count)
    expert_hot = (
        flat_ids[:, :, None] == jnp.arange(experts_count, dtype=jnp.int32)[None, None, :]
    ).astype(jnp.int32)
    before = jnp.cumsum(expert_hot, axis=1) - expert_hot
    slot_place = jnp.sum(before * expert_hot, axis=2)
    slot_hot = (
        slot_place[:, :, None] == jnp.arange(capacity, dtype=jnp.int32)[None, None, :]
    ).astype(jnp.int32)
    place_table = (expert_hot[:, :, :, None] * slot_hot[:, :, None, :]).reshape(
        members, tokens_here, top_count, experts_count, capacity
    )
    pick_table = jnp.sum(place_table, axis=2).astype(jnp.bfloat16)
    sent_rows = jnp.einsum(
        "jtnc,jtd->njcd", pick_table, normed, preferred_element_type=jnp.float32
    ).astype(jnp.bfloat16)
    share_table = jnp.sum(
        place_table.astype(jnp.bfloat16) * served_probs[:, :, :, None, None], axis=2
    )
    partial_out = expert_rows(
        lax.all_to_all(sent_rows, "exp", split_axis=0, concat_axis=0, tiled=True),
        gate_up,
        down_proj,
    ).astype(jnp.bfloat16)
    feature_block = width // shard_count
    partial_out = partial_out.reshape(
        experts_count, members, capacity, shard_count, feature_block
    )
    partial_out = jnp.transpose(partial_out, (0, 3, 1, 2, 4)).reshape(
        experts_count * shard_count, members, capacity, feature_block
    )
    gathered_parts = lax.all_to_all(partial_out, ("exp", "shard"), 0, 0, tiled=True)
    expert_out = (
        jnp.sum(
            gathered_parts.reshape(
                experts_count, shard_count, members, capacity, feature_block
            ).astype(jnp.float32),
            axis=1,
        )
        .astype(jnp.bfloat16)
    )
    moe_term = jnp.einsum(
        "jtnc,njcd->jtd", share_table, expert_out, preferred_element_type=jnp.float32
    )
    hidden_block = lax.dynamic_slice_in_dim(
        hidden_state, shard_index * feature_block, feature_block, 2
    )
    mixed_block = (hidden_block + moe_term).astype(jnp.bfloat16)
    mixed_out = jnp.transpose(
        gather_blocks(mixed_block, "shard", shard_count), (1, 2, 0, 3)
    ).reshape(members, tokens_here, width)
    return mixed_out


def solution(mesh):
    return jax.shard_map(
        on_device,
        mesh=mesh,
        in_specs=(
            P("req", "exp", None),
            P("req", "exp", None),
            P("req", "exp", None),
            P("req", "exp", None),
            P(),
            P("req", None),
            P("req", None),
            P("req", ("exp", "shard"), None, None),
            P("req", ("exp", "shard"), None, None),
            P(),
            P("shard", None),
            P("exp", None, "shard", None),
            P("exp", "shard", None),
        ),
        out_specs=P("req", "exp", None),
        check_vma=False,
    )
```

```python
import math

import jax
import jax.numpy as jnp
from jax import lax
from jax.sharding import PartitionSpec as P

H = 36


NEG_FILL = -1e30
EPSILON = 1e-06


def expert_rows(received, gate_up, down_proj):
    width = received.shape[-1]
    flat_rows = received.reshape(-1, width)
    both = lax.dot_general(
        flat_rows, gate_up[0], (((1,), (2,)), ((), ())), preferred_element_type=jnp.float32
    )
    active = (jax.nn.silu(both[:, 0]) * both[:, 1]).astype(jnp.bfloat16)
    partial_out = jnp.dot(active, down_proj[0], preferred_element_type=jnp.float32)
    return partial_out.reshape(received.shape)


def gather_blocks(block, axis_name, count):
    spread = jnp.broadcast_to(block[None], (count,) + block.shape)
    return lax.all_to_all(spread, axis_name, 0, 0, tiled=False)


def on_device(
    query_stretch,
    resid_stretch,
    route_ids,
    route_probs,
    request_order,
    prior_pages,
    page_order,
    key_pool,
    value_pool,
    norm_gain,
    out_proj,
    gate_up,
    down_proj,
):
    members = prior_pages.shape[1]
    tokens_here = query_stretch.shape[1]
    width = query_stretch.shape[2]
    head_size = width // H
    group_index = lax.axis_index("req")
    exp_index = lax.axis_index("exp")
    shard_index = lax.axis_index("shard")
    shard_count = lax.axis_size("shard")
    experts_count = lax.axis_size("exp")
    extras = jnp.concatenate(
        [resid_stretch, route_probs, route_ids.astype(jnp.bfloat16)], axis=2
    )
    all_query = lax.all_gather(query_stretch, "req", axis=0, tiled=True)
    all_extras = lax.all_gather(extras, "req", axis=0, tiled=True)
    served = lax.dynamic_slice_in_dim(request_order, group_index * members, members)
    served_query = jnp.take(all_query, served, axis=0)
    served_extras = jnp.take(all_extras, served, axis=0)
    core_index = shard_index % 2
    own_member = lax.dynamic_slice_in_dim(served_query, core_index, 1, 0)
    own_query = gather_blocks(own_member, "exp", experts_count)
    partner_query = lax.ppermute(
        own_query, "shard", [(i, i ^ 1) for i in range(shard_count)]
    )
    group_query = jnp.where(
        core_index == 0,
        jnp.concatenate([own_query, partner_query], axis=1),
        jnp.concatenate([partner_query, own_query], axis=1),
    )
    group_query, served_extras = lax.optimization_barrier((group_query, served_extras))
    top_count = route_ids.shape[2]
    served_resid = served_extras[:, :, :width]
    served_probs = served_extras[:, :, width : width + top_count]
    served_ids = served_extras[:, :, width + top_count :].astype(jnp.int32)
    pages_here = key_pool.shape[1]
    page_size = key_pool.shape[2]
    keys_here = pages_here * page_size
    device_index = exp_index * shard_count + shard_index
    physical = device_index * pages_here + jnp.arange(pages_here, dtype=jnp.int32)
    page_row = page_order[0]
    pool_size = page_row.shape[0]
    matched = page_row[None, :] == physical[:, None]
    located = jnp.sum(
        jnp.where(matched, jnp.arange(pool_size, dtype=jnp.int32)[None, :], 0), axis=1
    )
    prior_row = prior_pages[0]
    page_counts = prior_row + experts_count * tokens_here // page_size
    page_ends = jnp.cumsum(page_counts)
    page_starts = page_ends - page_counts
    owner_slot = jnp.sum((located[:, None] >= page_ends[None, :]).astype(jnp.int32), axis=1)
    owner_hot = owner_slot[:, None] == jnp.arange(members, dtype=jnp.int32)[None, :]
    logical = located - jnp.sum(jnp.where(owner_hot, page_starts[None, :], 0), axis=1)
    key_place = (
        logical[:, None] * page_size + jnp.arange(page_size, dtype=jnp.int32)[None, :]
    ).reshape(keys_here)
    key_owner = jnp.repeat(owner_slot, page_size)
    query_place = (
        prior_row[None, :, None] * page_size
        + jnp.arange(experts_count, dtype=jnp.int32)[:, None, None] * tokens_here
        + jnp.arange(tokens_here, dtype=jnp.int32)[None, None, :]
    )
    visible = (key_owner[None, None, None, :] == jnp.arange(members, dtype=jnp.int32)[None, :, None, None]) & (
        key_place[None, None, None, :] <= query_place[..., None]
    )
    query_rows = group_query.reshape(experts_count, members, tokens_here, H, head_size)
    key_rows = key_pool[0].reshape(keys_here, H, head_size)
    value_rows = value_pool[0].reshape(keys_here, H, head_size)
    scores = jnp.einsum(
        "ejthd,khd->ejhtk", query_rows, key_rows, preferred_element_type=jnp.float32
    ) * (1.0 / math.sqrt(head_size))
    scores = jnp.where(visible[:, :, None], scores, NEG_FILL)
    local_peak = lax.reduce_precision(jnp.max(scores, axis=4), 8, 7)
    weights_bf = jnp.where(
        visible[:, :, None], jnp.exp(scores - local_peak[..., None]), 0.0
    ).astype(jnp.bfloat16)
    totals = jnp.sum(weights_bf, axis=4, dtype=jnp.float32)
    context = jnp.einsum(
        "ejhtk,khd->ejthd", weights_bf, value_rows, preferred_element_type=jnp.float32
    ).reshape(experts_count, members, tokens_here, width)
    half_width = width // 2
    half_heads = H // 2
    own_peak = jnp.transpose(local_peak, (0, 1, 3, 2))
    own_totals = lax.reduce_precision(jnp.transpose(totals, (0, 1, 3, 2)), 8, 7)
    head_of_column = jnp.arange(half_width, dtype=jnp.int32) // head_size
    widen_table = (
        jnp.arange(half_heads, dtype=jnp.int32)[:, None] == head_of_column[None, :]
    ).astype(jnp.float32)

    def widen(scale):
        return jnp.einsum(
            "...h,hc->...c", scale, widen_table, precision=lax.Precision.HIGHEST
        )

    keep_context = lax.dynamic_slice_in_dim(context, core_index * half_width, half_width, 3)
    give_context = lax.dynamic_slice_in_dim(
        context, (1 - core_index) * half_width, half_width, 3
    )
    message = jnp.concatenate(
        [
            give_context.astype(jnp.bfloat16),
            own_peak.astype(jnp.bfloat16),
            own_totals.astype(jnp.bfloat16),
        ],
        axis=3,
    )
    message = lax.ppermute(message, "shard", [(i, i ^ 1) for i in range(shard_count)])
    other_context = message[..., :half_width].astype(jnp.float32)
    other_peak = message[..., half_width : half_width + H].astype(jnp.float32)
    other_totals = message[..., half_width + H :].astype(jnp.float32)
    pair_peak = jnp.maximum(own_peak, other_peak)
    own_scale = jnp.exp(own_peak - pair_peak)
    other_scale = jnp.exp(other_peak - pair_peak)
    pair_totals = own_scale * own_totals + other_scale * other_totals

    def half_scale(scale):
        return widen(lax.dynamic_slice_in_dim(scale, core_index * half_heads, half_heads, 3))

    pair_context = half_scale(own_scale) * keep_context + half_scale(other_scale) * other_context
    packed = jnp.concatenate(
        [
            pair_context.astype(jnp.bfloat16),
            pair_peak.astype(jnp.bfloat16),
            pair_totals.astype(jnp.bfloat16),
        ],
        axis=3,
    )
    packed_width = packed.shape[3]
    rows_each = members * tokens_here // shard_count
    packed = packed.reshape(experts_count * shard_count, rows_each, packed_width)
    arrived = lax.all_to_all(packed, ("exp", "shard"), 0, 0, tiled=True)
    arrived = arrived.reshape(-1, 2, rows_each, packed_width)
    arrived_peak = arrived[:, 0, :, half_width : half_width + H].astype(jnp.float32)
    arrived_totals = arrived[:, 0, :, half_width + H :].astype(jnp.float32)
    row_peak = jnp.max(arrived_peak, axis=0)
    rescale = jnp.exp(arrived_peak - row_peak[None])
    row_totals = jnp.sum(rescale * arrived_totals, axis=0)
    row_halves = []
    for half in range(2):
        half_rescale = widen(rescale[:, :, half * half_heads : (half + 1) * half_heads])
        half_context = jnp.sum(
            half_rescale * arrived[:, half, :, :half_width].astype(jnp.float32), axis=0
        )
        half_totals = widen(row_totals[:, half * half_heads : (half + 1) * half_heads])
        row_halves.append(half_context / half_totals)
    row_attended = jnp.concatenate(row_halves, axis=1).astype(jnp.bfloat16)
    attended = gather_blocks(row_attended, "shard", shard_count).reshape(
        members, tokens_here, width
    )
    projected_part = lax.dot_general(
        attended, out_proj, (((2,), (1,)), ((), ())), preferred_element_type=jnp.float32
    ).astype(jnp.bfloat16)
    projected = jnp.transpose(
        gather_blocks(projected_part, "shard", shard_count), (1, 2, 0, 3)
    ).reshape(members, tokens_here, width)
    hidden_state = served_resid.astype(jnp.float32) + projected.astype(jnp.float32)
    mean_square = jnp.mean(hidden_state * hidden_state, axis=2, keepdims=True)
    normed = (hidden_state * lax.rsqrt(mean_square + EPSILON) * norm_gain).astype(jnp.bfloat16)
    capacity = min(tokens_here, max(2, 3 * tokens_here * top_count // (2 * experts_count)))
    flat_ids = served_ids.reshape(members, tokens_here * top_count)
    expert_hot = (
        flat_ids[:, :, None] == jnp.arange(experts_count, dtype=jnp.int32)[None, None, :]
    ).astype(jnp.int32)
    before = jnp.cumsum(expert_hot, axis=1) - expert_hot
    slot_place = jnp.sum(before * expert_hot, axis=2)
    slot_hot = (
        slot_place[:, :, None] == jnp.arange(capacity, dtype=jnp.int32)[None, None, :]
    ).astype(jnp.int32)
    place_table = (expert_hot[:, :, :, None] * slot_hot[:, :, None, :]).reshape(
        members, tokens_here, top_count, experts_count, capacity
    )
    pick_table = jnp.sum(place_table, axis=2).astype(jnp.bfloat16)
    sent_rows = jnp.einsum(
        "jtnc,jtd->njcd", pick_table, normed, preferred_element_type=jnp.float32
    ).astype(jnp.bfloat16)
    share_table = jnp.sum(
        place_table.astype(jnp.bfloat16) * served_probs[:, :, :, None, None], axis=2
    )
    partial_out = expert_rows(
        lax.all_to_all(sent_rows, "exp", split_axis=0, concat_axis=0, tiled=True),
        gate_up,
        down_proj,
    ).astype(jnp.bfloat16)
    feature_block = width // shard_count
    partial_out = partial_out.reshape(
        experts_count, members, capacity, shard_count, feature_block
    )
    partial_out = jnp.transpose(partial_out, (0, 3, 1, 2, 4)).reshape(
        experts_count * shard_count, members, capacity, feature_block
    )
    gathered_parts = lax.all_to_all(partial_out, ("exp", "shard"), 0, 0, tiled=True)
    expert_out = (
        jnp.sum(
            gathered_parts.reshape(
                experts_count, shard_count, members, capacity, feature_block
            ).astype(jnp.float32),
            axis=1,
        )
        .astype(jnp.bfloat16)
    )
    moe_term = jnp.einsum(
        "jtnc,njcd->jtd", share_table, expert_out, preferred_element_type=jnp.float32
    )
    hidden_block = lax.dynamic_slice_in_dim(
        hidden_state, shard_index * feature_block, feature_block, 2
    )
    mixed_block = (hidden_block + moe_term).astype(jnp.bfloat16)
    mixed_out = jnp.transpose(
        gather_blocks(mixed_block, "shard", shard_count), (1, 2, 0, 3)
    ).reshape(members, tokens_here, width)
    return mixed_out


def solution(mesh):
    return jax.shard_map(
        on_device,
        mesh=mesh,
        in_specs=(
            P("req", "exp", None),
            P("req", "exp", None),
            P("req", "exp", None),
            P("req", "exp", None),
            P(),
            P("req", None),
            P("req", None),
            P("req", ("exp", "shard"), None, None),
            P("req", ("exp", "shard"), None, None),
            P(),
            P("shard", None),
            P("exp", None, "shard", None),
            P("exp", "shard", None),
        ),
        out_specs=P("req", "exp", None),
        check_vma=False,
    )
```

```python
import math

import jax
import jax.numpy as jnp
from jax import lax
from jax.experimental import pallas as pl
from jax.experimental.pallas import tpu as pltpu
from jax.sharding import PartitionSpec as P
import functools

H = 36


NEG_FILL = -1e30
EPSILON = 1e-06


def expert_rows(received, gate_up, down_proj):
    width = received.shape[-1]
    flat_rows = received.reshape(-1, width)
    both = lax.dot_general(
        flat_rows, gate_up[0], (((1,), (2,)), ((), ())), preferred_element_type=jnp.float32
    )
    active = (jax.nn.silu(both[:, 0]) * both[:, 1]).astype(jnp.bfloat16)
    partial_out = jnp.dot(active, down_proj[0], preferred_element_type=jnp.float32)
    return partial_out.reshape(received.shape)


def attend_kernel(heads, head_size, q_ref, k_ref, v_ref, mask_ref, ctx_ref, peak_ref, tot_ref):
    vis = mask_ref[...] != 0
    for h in range(heads):
        cols = slice(h * head_size, (h + 1) * head_size)
        q_h = q_ref[:, cols]
        k_h = k_ref[:, cols]
        s = lax.dot_general(q_h, k_h, (((1,), (1,)), ((), ())), preferred_element_type=jnp.float32)
        s = jnp.where(vis, s * (1.0 / math.sqrt(head_size)), NEG_FILL)
        m = jnp.max(s, axis=1, keepdims=True).astype(jnp.bfloat16).astype(jnp.float32)
        w = jnp.where(vis, jnp.exp(s - m), 0.0).astype(jnp.bfloat16)
        t = jnp.sum(w.astype(jnp.float32), axis=1, keepdims=True)
        c = jnp.dot(w, v_ref[:, cols], preferred_element_type=jnp.float32)
        ctx_ref[:, cols] = c
        peak_ref[:, h : h + 1] = m
        tot_ref[:, h : h + 1] = t

def attend(q, k, v, mask, heads):
    rows, width = q.shape
    head_size = width // heads
    return pl.pallas_call(
        functools.partial(attend_kernel, heads, head_size),
        out_shape=(
            jax.ShapeDtypeStruct((rows, width), jnp.float32),
            jax.ShapeDtypeStruct((rows, heads), jnp.float32),
            jax.ShapeDtypeStruct((rows, heads), jnp.float32),
        ),
        in_specs=[pl.BlockSpec(memory_space=pltpu.VMEM)] * 4,
        out_specs=[pl.BlockSpec(memory_space=pltpu.VMEM)] * 3,
    )(q, k, v, mask)


def gather_blocks(block, axis_name, count):
    spread = jnp.broadcast_to(block[None], (count,) + block.shape)
    return lax.all_to_all(spread, axis_name, 0, 0, tiled=False)


def on_device(
    query_stretch,
    resid_stretch,
    route_ids,
    route_probs,
    request_order,
    prior_pages,
    page_order,
    key_pool,
    value_pool,
    norm_gain,
    out_proj,
    gate_up,
    down_proj,
):
    members = prior_pages.shape[1]
    tokens_here = query_stretch.shape[1]
    width = query_stretch.shape[2]
    head_size = width // H
    group_index = lax.axis_index("req")
    exp_index = lax.axis_index("exp")
    shard_index = lax.axis_index("shard")
    shard_count = lax.axis_size("shard")
    experts_count = lax.axis_size("exp")
    extras = jnp.concatenate(
        [resid_stretch, route_probs, route_ids.astype(jnp.bfloat16)], axis=2
    )
    all_query = lax.all_gather(query_stretch, "req", axis=0, tiled=True)
    all_extras = lax.all_gather(extras, "req", axis=0, tiled=True)
    served = lax.dynamic_slice_in_dim(request_order, group_index * members, members)
    served_query = jnp.take(all_query, served, axis=0)
    served_extras = jnp.take(all_extras, served, axis=0)
    core_index = shard_index % 2
    own_member = lax.dynamic_slice_in_dim(served_query, core_index, 1, 0)
    own_query = gather_blocks(own_member, "exp", experts_count)
    partner_query = lax.ppermute(
        own_query, "shard", [(i, i ^ 1) for i in range(shard_count)]
    )
    group_query = jnp.where(
        core_index == 0,
        jnp.concatenate([own_query, partner_query], axis=1),
        jnp.concatenate([partner_query, own_query], axis=1),
    )
    group_query, served_extras = lax.optimization_barrier((group_query, served_extras))
    top_count = route_ids.shape[2]
    served_resid = served_extras[:, :, :width]
    served_probs = served_extras[:, :, width : width + top_count]
    served_ids = served_extras[:, :, width + top_count :].astype(jnp.int32)
    pages_here = key_pool.shape[1]
    page_size = key_pool.shape[2]
    keys_here = pages_here * page_size
    device_index = exp_index * shard_count + shard_index
    physical = device_index * pages_here + jnp.arange(pages_here, dtype=jnp.int32)
    page_row = page_order[0]
    pool_size = page_row.shape[0]
    matched = page_row[None, :] == physical[:, None]
    located = jnp.sum(
        jnp.where(matched, jnp.arange(pool_size, dtype=jnp.int32)[None, :], 0), axis=1
    )
    prior_row = prior_pages[0]
    page_counts = prior_row + experts_count * tokens_here // page_size
    page_ends = jnp.cumsum(page_counts)
    page_starts = page_ends - page_counts
    owner_slot = jnp.sum((located[:, None] >= page_ends[None, :]).astype(jnp.int32), axis=1)
    owner_hot = owner_slot[:, None] == jnp.arange(members, dtype=jnp.int32)[None, :]
    logical = located - jnp.sum(jnp.where(owner_hot, page_starts[None, :], 0), axis=1)
    key_place = (
        logical[:, None] * page_size + jnp.arange(page_size, dtype=jnp.int32)[None, :]
    ).reshape(keys_here)
    key_owner = jnp.repeat(owner_slot, page_size)
    query_place = (
        prior_row[None, :, None] * page_size
        + jnp.arange(experts_count, dtype=jnp.int32)[:, None, None] * tokens_here
        + jnp.arange(tokens_here, dtype=jnp.int32)[None, None, :]
    )
    visible = (key_owner[None, None, None, :] == jnp.arange(members, dtype=jnp.int32)[None, :, None, None]) & (
        key_place[None, None, None, :] <= query_place[..., None]
    )
    attend_rows = experts_count * members * tokens_here
    context, peak_rows, total_rows = attend(
        group_query.reshape(attend_rows, width),
        key_pool[0].reshape(keys_here, width),
        value_pool[0].reshape(keys_here, width),
        visible.reshape(attend_rows, keys_here).astype(jnp.int32),
        H,
    )
    context = context.reshape(experts_count, members, tokens_here, width)
    half_width = width // 2
    half_heads = H // 2
    own_peak = peak_rows.reshape(experts_count, members, tokens_here, H)
    own_totals = lax.reduce_precision(
        total_rows.reshape(experts_count, members, tokens_here, H), 8, 7
    )
    head_of_column = jnp.arange(half_width, dtype=jnp.int32) // head_size
    widen_table = (
        jnp.arange(half_heads, dtype=jnp.int32)[:, None] == head_of_column[None, :]
    ).astype(jnp.float32)

    def widen(scale):
        return jnp.einsum(
            "...h,hc->...c", scale, widen_table, precision=lax.Precision.HIGHEST
        )

    keep_context = lax.dynamic_slice_in_dim(context, core_index * half_width, half_width, 3)
    give_context = lax.dynamic_slice_in_dim(
        context, (1 - core_index) * half_width, half_width, 3
    )
    message = jnp.concatenate(
        [
            give_context.astype(jnp.bfloat16),
            own_peak.astype(jnp.bfloat16),
            own_totals.astype(jnp.bfloat16),
        ],
        axis=3,
    )
    message = lax.ppermute(message, "shard", [(i, i ^ 1) for i in range(shard_count)])
    other_context = message[..., :half_width].astype(jnp.float32)
    other_peak = message[..., half_width : half_width + H].astype(jnp.float32)
    other_totals = message[..., half_width + H :].astype(jnp.float32)
    pair_peak = jnp.maximum(own_peak, other_peak)
    own_scale = jnp.exp(own_peak - pair_peak)
    other_scale = jnp.exp(other_peak - pair_peak)
    pair_totals = own_scale * own_totals + other_scale * other_totals

    def half_scale(scale):
        return widen(lax.dynamic_slice_in_dim(scale, core_index * half_heads, half_heads, 3))

    pair_context = half_scale(own_scale) * keep_context + half_scale(other_scale) * other_context
    packed = jnp.concatenate(
        [
            pair_context.astype(jnp.bfloat16),
            pair_peak.astype(jnp.bfloat16),
            pair_totals.astype(jnp.bfloat16),
        ],
        axis=3,
    )
    packed_width = packed.shape[3]
    rows_each = members * tokens_here // shard_count
    packed = packed.reshape(experts_count * shard_count, rows_each, packed_width)
    arrived = lax.all_to_all(packed, ("exp", "shard"), 0, 0, tiled=True)
    arrived = arrived.reshape(-1, 2, rows_each, packed_width)
    arrived_peak = arrived[:, 0, :, half_width : half_width + H].astype(jnp.float32)
    arrived_totals = arrived[:, 0, :, half_width + H :].astype(jnp.float32)
    row_peak = jnp.max(arrived_peak, axis=0)
    rescale = jnp.exp(arrived_peak - row_peak[None])
    row_totals = jnp.sum(rescale * arrived_totals, axis=0)
    row_halves = []
    for half in range(2):
        half_rescale = widen(rescale[:, :, half * half_heads : (half + 1) * half_heads])
        half_context = jnp.sum(
            half_rescale * arrived[:, half, :, :half_width].astype(jnp.float32), axis=0
        )
        half_totals = widen(row_totals[:, half * half_heads : (half + 1) * half_heads])
        row_halves.append(half_context / half_totals)
    row_attended = jnp.concatenate(row_halves, axis=1).astype(jnp.bfloat16)
    attended = gather_blocks(row_attended, "shard", shard_count).reshape(
        members, tokens_here, width
    )
    projected_part = lax.dot_general(
        attended, out_proj, (((2,), (1,)), ((), ())), preferred_element_type=jnp.float32
    ).astype(jnp.bfloat16)
    projected = jnp.transpose(
        gather_blocks(projected_part, "shard", shard_count), (1, 2, 0, 3)
    ).reshape(members, tokens_here, width)
    hidden_state = served_resid.astype(jnp.float32) + projected.astype(jnp.float32)
    mean_square = jnp.mean(hidden_state * hidden_state, axis=2, keepdims=True)
    normed = (hidden_state * lax.rsqrt(mean_square + EPSILON) * norm_gain).astype(jnp.bfloat16)
    capacity = min(tokens_here, max(2, 3 * tokens_here * top_count // (2 * experts_count)))
    flat_ids = served_ids.reshape(members, tokens_here * top_count)
    expert_hot = (
        flat_ids[:, :, None] == jnp.arange(experts_count, dtype=jnp.int32)[None, None, :]
    ).astype(jnp.int32)
    before = jnp.cumsum(expert_hot, axis=1) - expert_hot
    slot_place = jnp.sum(before * expert_hot, axis=2)
    slot_hot = (
        slot_place[:, :, None] == jnp.arange(capacity, dtype=jnp.int32)[None, None, :]
    ).astype(jnp.int32)
    place_table = (expert_hot[:, :, :, None] * slot_hot[:, :, None, :]).reshape(
        members, tokens_here, top_count, experts_count, capacity
    )
    pick_table = jnp.sum(place_table, axis=2).astype(jnp.bfloat16)
    sent_rows = jnp.einsum(
        "jtnc,jtd->njcd", pick_table, normed, preferred_element_type=jnp.float32
    ).astype(jnp.bfloat16)
    share_table = jnp.sum(
        place_table.astype(jnp.bfloat16) * served_probs[:, :, :, None, None], axis=2
    )
    partial_out = expert_rows(
        lax.all_to_all(sent_rows, "exp", split_axis=0, concat_axis=0, tiled=True),
        gate_up,
        down_proj,
    ).astype(jnp.bfloat16)
    feature_block = width // shard_count
    partial_out = partial_out.reshape(
        experts_count, members, capacity, shard_count, feature_block
    )
    partial_out = jnp.transpose(partial_out, (0, 3, 1, 2, 4)).reshape(
        experts_count * shard_count, members, capacity, feature_block
    )
    gathered_parts = lax.all_to_all(partial_out, ("exp", "shard"), 0, 0, tiled=True)
    expert_out = (
        jnp.sum(
            gathered_parts.reshape(
                experts_count, shard_count, members, capacity, feature_block
            ).astype(jnp.float32),
            axis=1,
        )
        .astype(jnp.bfloat16)
    )
    moe_term = jnp.einsum(
        "jtnc,njcd->jtd", share_table, expert_out, preferred_element_type=jnp.float32
    )
    hidden_block = lax.dynamic_slice_in_dim(
        hidden_state, shard_index * feature_block, feature_block, 2
    )
    mixed_block = (hidden_block + moe_term).astype(jnp.bfloat16)
    mixed_out = jnp.transpose(
        gather_blocks(mixed_block, "shard", shard_count), (1, 2, 0, 3)
    ).reshape(members, tokens_here, width)
    return mixed_out


def solution(mesh):
    return jax.shard_map(
        on_device,
        mesh=mesh,
        in_specs=(
            P("req", "exp", None),
            P("req", "exp", None),
            P("req", "exp", None),
            P("req", "exp", None),
            P(),
            P("req", None),
            P("req", None),
            P("req", ("exp", "shard"), None, None),
            P("req", ("exp", "shard"), None, None),
            P(),
            P("shard", None),
            P("exp", None, "shard", None),
            P("exp", "shard", None),
        ),
        out_specs=P("req", "exp", None),
        check_vma=False,
    )
```

```python
import math

import jax
import jax.numpy as jnp
from jax import lax
from jax.experimental import pallas as pl
from jax.experimental.pallas import tpu as pltpu
from jax.sharding import PartitionSpec as P
import functools

H = 36


NEG_FILL = -1e30
EPSILON = 1e-06


def expert_rows(received, gate_up, down_proj):
    width = received.shape[-1]
    flat_rows = received.reshape(-1, width)
    both = lax.dot_general(
        flat_rows, gate_up[0], (((1,), (2,)), ((), ())), preferred_element_type=jnp.float32
    )
    active = (jax.nn.silu(both[:, 0]) * both[:, 1]).astype(jnp.bfloat16)
    partial_out = jnp.dot(active, down_proj[0], preferred_element_type=jnp.float32)
    return partial_out.reshape(received.shape)


def attend_kernel(heads, head_size, q_ref, k_ref, v_ref, mask_ref, ctx_ref, peak_ref, tot_ref):
    vis = mask_ref[...] != 0
    for h in range(heads):
        cols = slice(h * head_size, (h + 1) * head_size)
        q_h = q_ref[:, cols]
        k_h = k_ref[:, cols]
        s = lax.dot_general(q_h, k_h, (((1,), (1,)), ((), ())), preferred_element_type=jnp.float32)
        s = jnp.where(vis, s * (1.0 / math.sqrt(head_size)), NEG_FILL)
        m = jnp.max(s, axis=1, keepdims=True).astype(jnp.bfloat16).astype(jnp.float32)
        w = jnp.where(vis, jnp.exp(s - m), 0.0).astype(jnp.bfloat16)
        t = jnp.sum(w.astype(jnp.float32), axis=1, keepdims=True)
        c = jnp.dot(w, v_ref[:, cols], preferred_element_type=jnp.float32)
        ctx_ref[:, cols] = c
        peak_ref[:, h : h + 1] = m
        tot_ref[:, h : h + 1] = t

def attend(q, k, v, mask, heads):
    rows, width = q.shape
    head_size = width // heads
    return pl.pallas_call(
        functools.partial(attend_kernel, heads, head_size),
        out_shape=(
            jax.ShapeDtypeStruct((rows, width), jnp.float32),
            jax.ShapeDtypeStruct((rows, heads), jnp.float32),
            jax.ShapeDtypeStruct((rows, heads), jnp.float32),
        ),
        in_specs=[pl.BlockSpec(memory_space=pltpu.VMEM)] * 4,
        out_specs=[pl.BlockSpec(memory_space=pltpu.VMEM)] * 3,
    )(q, k, v, mask)


def gather_blocks(block, axis_name, count):
    spread = jnp.broadcast_to(block[None], (count,) + block.shape)
    return lax.all_to_all(spread, axis_name, 0, 0, tiled=False)


def on_device(
    query_stretch,
    resid_stretch,
    route_ids,
    route_probs,
    request_order,
    prior_pages,
    page_order,
    key_pool,
    value_pool,
    norm_gain,
    out_proj,
    gate_up,
    down_proj,
):
    members = prior_pages.shape[1]
    tokens_here = query_stretch.shape[1]
    width = query_stretch.shape[2]
    head_size = width // H
    group_index = lax.axis_index("req")
    exp_index = lax.axis_index("exp")
    shard_index = lax.axis_index("shard")
    shard_count = lax.axis_size("shard")
    experts_count = lax.axis_size("exp")
    extras = jnp.concatenate(
        [resid_stretch, route_probs, route_ids.astype(jnp.bfloat16)], axis=2
    )
    all_query = lax.all_gather(query_stretch, "req", axis=0, tiled=True)
    all_extras = lax.all_gather(extras, "req", axis=0, tiled=True)
    served = lax.dynamic_slice_in_dim(request_order, group_index * members, members)
    served_query = jnp.take(all_query, served, axis=0)
    served_extras = jnp.take(all_extras, served, axis=0)
    core_index = shard_index % 2
    own_member = lax.dynamic_slice_in_dim(served_query, core_index, 1, 0)
    own_query = gather_blocks(own_member, "exp", experts_count)
    partner_query = lax.ppermute(
        own_query, "shard", [(i, i ^ 1) for i in range(shard_count)]
    )
    group_query = jnp.where(
        core_index == 0,
        jnp.concatenate([own_query, partner_query], axis=1),
        jnp.concatenate([partner_query, own_query], axis=1),
    )
    group_query, served_extras = lax.optimization_barrier((group_query, served_extras))
    top_count = route_ids.shape[2]
    served_resid = served_extras[:, :, :width]
    served_probs = served_extras[:, :, width : width + top_count]
    served_ids = served_extras[:, :, width + top_count :].astype(jnp.int32)
    pages_here = key_pool.shape[1]
    page_size = key_pool.shape[2]
    keys_here = pages_here * page_size
    device_index = exp_index * shard_count + shard_index
    physical = device_index * pages_here + jnp.arange(pages_here, dtype=jnp.int32)
    page_row = page_order[0]
    pool_size = page_row.shape[0]
    matched = page_row[None, :] == physical[:, None]
    located = jnp.sum(
        jnp.where(matched, jnp.arange(pool_size, dtype=jnp.int32)[None, :], 0), axis=1
    )
    prior_row = prior_pages[0]
    page_counts = prior_row + experts_count * tokens_here // page_size
    page_ends = jnp.cumsum(page_counts)
    page_starts = page_ends - page_counts
    owner_slot = jnp.sum((located[:, None] >= page_ends[None, :]).astype(jnp.int32), axis=1)
    owner_hot = owner_slot[:, None] == jnp.arange(members, dtype=jnp.int32)[None, :]
    logical = located - jnp.sum(jnp.where(owner_hot, page_starts[None, :], 0), axis=1)
    key_place = (
        logical[:, None] * page_size + jnp.arange(page_size, dtype=jnp.int32)[None, :]
    ).reshape(keys_here)
    key_owner = jnp.repeat(owner_slot, page_size)
    query_place = (
        prior_row[None, :, None] * page_size
        + jnp.arange(experts_count, dtype=jnp.int32)[:, None, None] * tokens_here
        + jnp.arange(tokens_here, dtype=jnp.int32)[None, None, :]
    )
    visible = (key_owner[None, None, None, :] == jnp.arange(members, dtype=jnp.int32)[None, :, None, None]) & (
        key_place[None, None, None, :] <= query_place[..., None]
    )
    attend_rows = experts_count * members * tokens_here
    context, peak_rows, total_rows = attend(
        group_query.reshape(attend_rows, width),
        key_pool[0].reshape(keys_here, width),
        value_pool[0].reshape(keys_here, width),
        visible.reshape(attend_rows, keys_here).astype(jnp.int32),
        H,
    )
    context = context.reshape(experts_count, members, tokens_here, width)
    half_width = width // 2
    half_heads = H // 2
    own_peak = peak_rows.reshape(experts_count, members, tokens_here, H)
    own_totals = lax.reduce_precision(
        total_rows.reshape(experts_count, members, tokens_here, H), 8, 7
    )
    head_of_column = jnp.arange(half_width, dtype=jnp.int32) // head_size
    widen_table = (
        jnp.arange(half_heads, dtype=jnp.int32)[:, None] == head_of_column[None, :]
    ).astype(jnp.float32)

    def widen(scale):
        return jnp.einsum(
            "...h,hc->...c", scale, widen_table, precision=lax.Precision.HIGHEST
        )

    keep_context = lax.dynamic_slice_in_dim(context, core_index * half_width, half_width, 3)
    give_context = lax.dynamic_slice_in_dim(
        context, (1 - core_index) * half_width, half_width, 3
    )
    message = jnp.concatenate(
        [
            give_context.astype(jnp.bfloat16),
            own_peak.astype(jnp.bfloat16),
            own_totals.astype(jnp.bfloat16),
        ],
        axis=3,
    )
    message = lax.ppermute(message, "shard", [(i, i ^ 1) for i in range(shard_count)])
    other_context = message[..., :half_width].astype(jnp.float32)
    other_peak = message[..., half_width : half_width + H].astype(jnp.float32)
    other_totals = message[..., half_width + H :].astype(jnp.float32)
    pair_peak = jnp.maximum(own_peak, other_peak)
    own_scale = jnp.exp(own_peak - pair_peak)
    other_scale = jnp.exp(other_peak - pair_peak)
    pair_totals = own_scale * own_totals + other_scale * other_totals

    def half_scale(scale):
        return widen(lax.dynamic_slice_in_dim(scale, core_index * half_heads, half_heads, 3))

    pair_context = half_scale(own_scale) * keep_context + half_scale(other_scale) * other_context
    packed = jnp.concatenate(
        [
            pair_context.astype(jnp.bfloat16),
            pair_peak.astype(jnp.bfloat16),
            pair_totals.astype(jnp.bfloat16),
        ],
        axis=3,
    )
    packed_width = packed.shape[3]
    rows_each = members * tokens_here // shard_count
    packed = packed.reshape(experts_count * shard_count, rows_each, packed_width)
    arrived = lax.all_to_all(packed, ("exp", "shard"), 0, 0, tiled=True)
    arrived = arrived.reshape(-1, 2, rows_each, packed_width)
    arrived_peak = arrived[:, 0, :, half_width : half_width + H].astype(jnp.float32)
    arrived_totals = arrived[:, 0, :, half_width + H :].astype(jnp.float32)
    row_peak = jnp.max(arrived_peak, axis=0)
    rescale = jnp.exp(arrived_peak - row_peak[None])
    row_totals = jnp.sum(rescale * arrived_totals, axis=0)
    row_halves = []
    for half in range(2):
        half_rescale = widen(rescale[:, :, half * half_heads : (half + 1) * half_heads])
        half_context = jnp.sum(
            half_rescale * arrived[:, half, :, :half_width].astype(jnp.float32), axis=0
        )
        half_totals = widen(row_totals[:, half * half_heads : (half + 1) * half_heads])
        row_halves.append(half_context / half_totals)
    row_attended = jnp.concatenate(row_halves, axis=1).astype(jnp.bfloat16)
    attended = gather_blocks(row_attended, "shard", shard_count).reshape(
        members, tokens_here, width
    )
    projected_part = lax.dot_general(
        attended, out_proj, (((2,), (1,)), ((), ())), preferred_element_type=jnp.float32
    ).astype(jnp.bfloat16)
    projected = jnp.transpose(
        gather_blocks(projected_part, "shard", shard_count), (1, 2, 0, 3)
    ).reshape(members, tokens_here, width)
    hidden_state = served_resid.astype(jnp.float32) + projected.astype(jnp.float32)
    mean_square = jnp.mean(hidden_state * hidden_state, axis=2, keepdims=True)
    normed = (hidden_state * lax.rsqrt(mean_square + EPSILON) * norm_gain).astype(jnp.bfloat16)
    capacity = min(tokens_here, max(2, 3 * tokens_here * top_count // (2 * experts_count)))
    flat_ids = served_ids.reshape(members, tokens_here * top_count)
    expert_hot = (
        flat_ids[:, :, None] == jnp.arange(experts_count, dtype=jnp.int32)[None, None, :]
    ).astype(jnp.int32)
    before = jnp.cumsum(expert_hot, axis=1) - expert_hot
    slot_place = jnp.sum(before * expert_hot, axis=2)
    slot_hot = (
        slot_place[:, :, None] == jnp.arange(capacity, dtype=jnp.int32)[None, None, :]
    ).astype(jnp.int32)
    place_table = (expert_hot[:, :, :, None] * slot_hot[:, :, None, :]).reshape(
        members, tokens_here, top_count, experts_count, capacity
    )
    pick_table = jnp.sum(place_table, axis=2).astype(jnp.bfloat16)
    sent_rows = jnp.einsum(
        "jtnc,jtd->njcd", pick_table, normed, preferred_element_type=jnp.float32
    ).astype(jnp.bfloat16)
    share_table = jnp.sum(
        place_table.astype(jnp.bfloat16) * served_probs[:, :, :, None, None], axis=2
    )
    partial_out = expert_rows(
        lax.all_to_all(sent_rows, "exp", split_axis=0, concat_axis=0, tiled=True),
        gate_up,
        down_proj,
    )
    feature_block = width // shard_count
    keep_rows = lax.dynamic_slice_in_dim(partial_out, core_index, 1, 1)
    give_rows = lax.dynamic_slice_in_dim(partial_out, 1 - core_index, 1, 1)
    pair_rows = keep_rows + lax.ppermute(
        give_rows, "shard", [(i, i ^ 1) for i in range(shard_count)]
    )
    pair_rows = pair_rows.astype(jnp.bfloat16).reshape(
        experts_count, 1, capacity, shard_count, feature_block
    )
    pair_rows = jnp.transpose(pair_rows, (0, 3, 1, 2, 4)).reshape(
        experts_count * shard_count, 1, capacity, feature_block
    )
    gathered_parts = lax.all_to_all(pair_rows, ("exp", "shard"), 0, 0, tiled=True)
    expert_out = (
        jnp.sum(
            gathered_parts.reshape(
                experts_count, shard_count // 2, 2, capacity, feature_block
            ).astype(jnp.float32),
            axis=1,
        )
        .astype(jnp.bfloat16)
    )
    moe_term = jnp.einsum(
        "jtnc,njcd->jtd", share_table, expert_out, preferred_element_type=jnp.float32
    )
    hidden_block = lax.dynamic_slice_in_dim(
        hidden_state, shard_index * feature_block, feature_block, 2
    )
    mixed_block = (hidden_block + moe_term).astype(jnp.bfloat16)
    mixed_out = jnp.transpose(
        gather_blocks(mixed_block, "shard", shard_count), (1, 2, 0, 3)
    ).reshape(members, tokens_here, width)
    return mixed_out


def solution(mesh):
    return jax.shard_map(
        on_device,
        mesh=mesh,
        in_specs=(
            P("req", "exp", None),
            P("req", "exp", None),
            P("req", "exp", None),
            P("req", "exp", None),
            P(),
            P("req", None),
            P("req", None),
            P("req", ("exp", "shard"), None, None),
            P("req", ("exp", "shard"), None, None),
            P(),
            P("shard", None),
            P("exp", None, "shard", None),
            P("exp", "shard", None),
        ),
        out_specs=P("req", "exp", None),
        check_vma=False,
    )
```

```python
import math

import jax
import jax.numpy as jnp
from jax import lax
from jax.experimental import pallas as pl
from jax.experimental.pallas import tpu as pltpu
from jax.sharding import PartitionSpec as P
import functools

H = 36


NEG_FILL = -1e30
EPSILON = 1e-06


def expert_rows(received, gate_up, down_proj):
    width = received.shape[-1]
    flat_rows = received.reshape(-1, width)
    both = lax.dot_general(
        flat_rows, gate_up[0], (((1,), (2,)), ((), ())), preferred_element_type=jnp.float32
    )
    active = (jax.nn.silu(both[:, 0]) * both[:, 1]).astype(jnp.bfloat16)
    partial_out = jnp.dot(active, down_proj[0], preferred_element_type=jnp.float32)
    return partial_out.reshape(received.shape)


def attend_kernel(heads, head_size, q_ref, k_ref, v_ref, mask_ref, ctx_ref, peak_ref, tot_ref):
    vis = mask_ref[...] != 0
    for h in range(heads):
        cols = slice(h * head_size, (h + 1) * head_size)
        q_h = q_ref[:, cols]
        k_h = k_ref[:, cols]
        s = lax.dot_general(q_h, k_h, (((1,), (1,)), ((), ())), preferred_element_type=jnp.float32)
        s = jnp.where(vis, s * (1.0 / math.sqrt(head_size)), NEG_FILL)
        m = jnp.max(s, axis=1, keepdims=True).astype(jnp.bfloat16).astype(jnp.float32)
        w = jnp.where(vis, jnp.exp(s - m), 0.0).astype(jnp.bfloat16)
        t = jnp.sum(w.astype(jnp.float32), axis=1, keepdims=True)
        c = jnp.dot(w, v_ref[:, cols], preferred_element_type=jnp.float32)
        ctx_ref[:, cols] = c
        peak_ref[:, h : h + 1] = m
        tot_ref[:, h : h + 1] = t

def attend(q, k, v, mask, heads):
    rows, width = q.shape
    head_size = width // heads
    return pl.pallas_call(
        functools.partial(attend_kernel, heads, head_size),
        out_shape=(
            jax.ShapeDtypeStruct((rows, width), jnp.float32),
            jax.ShapeDtypeStruct((rows, heads), jnp.float32),
            jax.ShapeDtypeStruct((rows, heads), jnp.float32),
        ),
        in_specs=[pl.BlockSpec(memory_space=pltpu.VMEM)] * 4,
        out_specs=[pl.BlockSpec(memory_space=pltpu.VMEM)] * 3,
    )(q, k, v, mask)


def gather_blocks(block, axis_name, count):
    spread = jnp.broadcast_to(block[None], (count,) + block.shape)
    return lax.all_to_all(spread, axis_name, 0, 0, tiled=False)


def on_device(
    query_stretch,
    resid_stretch,
    route_ids,
    route_probs,
    request_order,
    prior_pages,
    page_order,
    key_pool,
    value_pool,
    norm_gain,
    out_proj,
    gate_up,
    down_proj,
):
    members = prior_pages.shape[1]
    tokens_here = query_stretch.shape[1]
    width = query_stretch.shape[2]
    head_size = width // H
    group_index = lax.axis_index("req")
    exp_index = lax.axis_index("exp")
    shard_index = lax.axis_index("shard")
    shard_count = lax.axis_size("shard")
    experts_count = lax.axis_size("exp")
    extras = jnp.concatenate(
        [resid_stretch, route_probs, route_ids.astype(jnp.bfloat16)], axis=2
    )
    all_query = lax.all_gather(query_stretch, "req", axis=0, tiled=True)
    all_extras = lax.all_gather(extras, "req", axis=0, tiled=True)
    served = lax.dynamic_slice_in_dim(request_order, group_index * members, members)
    served_query = jnp.take(all_query, served, axis=0)
    served_extras = jnp.take(all_extras, served, axis=0)
    core_index = shard_index % 2
    own_member = lax.dynamic_slice_in_dim(served_query, core_index, 1, 0)
    own_query = gather_blocks(own_member, "exp", experts_count)
    partner_query = lax.ppermute(
        own_query, "shard", [(i, i ^ 1) for i in range(shard_count)]
    )
    group_query = jnp.where(
        core_index == 0,
        jnp.concatenate([own_query, partner_query], axis=1),
        jnp.concatenate([partner_query, own_query], axis=1),
    )
    group_query, served_extras = lax.optimization_barrier((group_query, served_extras))
    top_count = route_ids.shape[2]
    served_resid = served_extras[:, :, :width]
    served_probs = served_extras[:, :, width : width + top_count]
    served_ids = served_extras[:, :, width + top_count :].astype(jnp.int32)
    pages_here = key_pool.shape[1]
    page_size = key_pool.shape[2]
    keys_here = pages_here * page_size
    device_index = exp_index * shard_count + shard_index
    physical = device_index * pages_here + jnp.arange(pages_here, dtype=jnp.int32)
    page_row = page_order[0]
    pool_size = page_row.shape[0]
    matched = page_row[None, :] == physical[:, None]
    located = jnp.sum(
        jnp.where(matched, jnp.arange(pool_size, dtype=jnp.int32)[None, :], 0), axis=1
    )
    prior_row = prior_pages[0]
    page_counts = prior_row + experts_count * tokens_here // page_size
    page_ends = jnp.cumsum(page_counts)
    page_starts = page_ends - page_counts
    owner_slot = jnp.sum((located[:, None] >= page_ends[None, :]).astype(jnp.int32), axis=1)
    owner_hot = owner_slot[:, None] == jnp.arange(members, dtype=jnp.int32)[None, :]
    logical = located - jnp.sum(jnp.where(owner_hot, page_starts[None, :], 0), axis=1)
    key_place = (
        logical[:, None] * page_size + jnp.arange(page_size, dtype=jnp.int32)[None, :]
    ).reshape(keys_here)
    key_owner = jnp.repeat(owner_slot, page_size)
    query_place = (
        prior_row[None, :, None] * page_size
        + jnp.arange(experts_count, dtype=jnp.int32)[:, None, None] * tokens_here
        + jnp.arange(tokens_here, dtype=jnp.int32)[None, None, :]
    )
    visible = (key_owner[None, None, None, :] == jnp.arange(members, dtype=jnp.int32)[None, :, None, None]) & (
        key_place[None, None, None, :] <= query_place[..., None]
    )
    attend_rows = experts_count * members * tokens_here
    context, peak_rows, total_rows = attend(
        group_query.reshape(attend_rows, width),
        key_pool[0].reshape(keys_here, width),
        value_pool[0].reshape(keys_here, width),
        visible.reshape(attend_rows, keys_here).astype(jnp.int32),
        H,
    )
    context = context.reshape(experts_count, members, tokens_here, width)
    half_width = width // 2
    half_heads = H // 2
    own_peak = peak_rows.reshape(experts_count, members, tokens_here, H)
    own_totals = lax.reduce_precision(
        total_rows.reshape(experts_count, members, tokens_here, H), 8, 7
    )
    head_of_column = jnp.arange(half_width, dtype=jnp.int32) // head_size
    widen_table = (
        jnp.arange(half_heads, dtype=jnp.int32)[:, None] == head_of_column[None, :]
    ).astype(jnp.float32)

    def widen(scale):
        return jnp.einsum(
            "...h,hc->...c", scale, widen_table, precision=lax.Precision.HIGHEST
        )

    keep_context = lax.dynamic_slice_in_dim(context, core_index * half_width, half_width, 3)
    give_context = lax.dynamic_slice_in_dim(
        context, (1 - core_index) * half_width, half_width, 3
    )
    message = jnp.concatenate(
        [
            give_context.astype(jnp.bfloat16),
            own_peak.astype(jnp.bfloat16),
            own_totals.astype(jnp.bfloat16),
        ],
        axis=3,
    )
    message = lax.ppermute(message, "shard", [(i, i ^ 1) for i in range(shard_count)])
    other_context = message[..., :half_width].astype(jnp.float32)
    other_peak = message[..., half_width : half_width + H].astype(jnp.float32)
    other_totals = message[..., half_width + H :].astype(jnp.float32)
    pair_peak = jnp.maximum(own_peak, other_peak)
    own_scale = jnp.exp(own_peak - pair_peak)
    other_scale = jnp.exp(other_peak - pair_peak)
    pair_totals = own_scale * own_totals + other_scale * other_totals

    def half_scale(scale):
        return widen(lax.dynamic_slice_in_dim(scale, core_index * half_heads, half_heads, 3))

    pair_context = half_scale(own_scale) * keep_context + half_scale(other_scale) * other_context
    packed = jnp.concatenate(
        [
            pair_context.astype(jnp.bfloat16),
            pair_peak.astype(jnp.bfloat16),
            pair_totals.astype(jnp.bfloat16),
        ],
        axis=3,
    )
    packed_width = packed.shape[3]
    rows_each = members * tokens_here // shard_count
    packed = packed.reshape(experts_count * shard_count, rows_each, packed_width)
    arrived = lax.all_to_all(packed, ("exp", "shard"), 0, 0, tiled=True)
    arrived = arrived.reshape(-1, 2, rows_each, packed_width)
    arrived_peak = arrived[:, 0, :, half_width : half_width + H].astype(jnp.float32)
    arrived_totals = arrived[:, 0, :, half_width + H :].astype(jnp.float32)
    row_peak = jnp.max(arrived_peak, axis=0)
    rescale = jnp.exp(arrived_peak - row_peak[None])
    row_totals = jnp.sum(rescale * arrived_totals, axis=0)
    row_halves = []
    for half in range(2):
        half_rescale = widen(rescale[:, :, half * half_heads : (half + 1) * half_heads])
        half_context = jnp.sum(
            half_rescale * arrived[:, half, :, :half_width].astype(jnp.float32), axis=0
        )
        half_totals = widen(row_totals[:, half * half_heads : (half + 1) * half_heads])
        row_halves.append(half_context / half_totals)
    row_attended = jnp.concatenate(row_halves, axis=1).astype(jnp.bfloat16)
    attended = gather_blocks(row_attended, "shard", shard_count).reshape(
        members, tokens_here, width
    )
    projected_part = lax.dot_general(
        attended, out_proj, (((2,), (1,)), ((), ())), preferred_element_type=jnp.float32
    ).astype(jnp.bfloat16)
    projected = jnp.transpose(
        gather_blocks(projected_part, "shard", shard_count), (1, 2, 0, 3)
    ).reshape(members, tokens_here, width)
    hidden_state = served_resid.astype(jnp.float32) + projected.astype(jnp.float32)
    mean_square = jnp.mean(hidden_state * hidden_state, axis=2, keepdims=True)
    normed = (hidden_state * lax.rsqrt(mean_square + EPSILON) * norm_gain).astype(jnp.bfloat16)
    capacity = min(tokens_here, max(2, 3 * tokens_here * top_count // (2 * experts_count)))
    flat_ids = served_ids.reshape(members, tokens_here * top_count)
    expert_hot = (
        flat_ids[:, :, None] == jnp.arange(experts_count, dtype=jnp.int32)[None, None, :]
    ).astype(jnp.int32)
    before = jnp.cumsum(expert_hot, axis=1) - expert_hot
    slot_place = jnp.sum(before * expert_hot, axis=2)
    slot_hot = (
        slot_place[:, :, None] == jnp.arange(capacity, dtype=jnp.int32)[None, None, :]
    ).astype(jnp.int32)
    place_table = (expert_hot[:, :, :, None] * slot_hot[:, :, None, :]).reshape(
        members, tokens_here, top_count, experts_count, capacity
    )
    pick_table = jnp.sum(place_table, axis=2).astype(jnp.bfloat16)
    sent_rows = jnp.einsum(
        "jtnc,jtd->njcd", pick_table, normed, preferred_element_type=jnp.float32
    ).astype(jnp.bfloat16)
    share_table = jnp.sum(
        place_table.astype(jnp.bfloat16) * served_probs[:, :, :, None, None], axis=2
    )
    own_rows = lax.all_to_all(
        lax.dynamic_slice_in_dim(sent_rows, core_index, 1, 1),
        "exp",
        split_axis=0,
        concat_axis=0,
        tiled=True,
    )
    partner_rows = lax.ppermute(own_rows, "shard", [(i, i ^ 1) for i in range(shard_count)])
    received_rows = jnp.where(
        core_index == 0,
        jnp.concatenate([own_rows, partner_rows], axis=1),
        jnp.concatenate([partner_rows, own_rows], axis=1),
    )
    partial_out = expert_rows(received_rows, gate_up, down_proj)
    feature_block = width // shard_count
    keep_rows = lax.dynamic_slice_in_dim(partial_out, core_index, 1, 1)
    give_rows = lax.dynamic_slice_in_dim(partial_out, 1 - core_index, 1, 1)
    pair_rows = keep_rows + lax.ppermute(
        give_rows, "shard", [(i, i ^ 1) for i in range(shard_count)]
    )
    pair_rows = pair_rows.astype(jnp.bfloat16).reshape(
        experts_count, 1, capacity, shard_count, feature_block
    )
    pair_rows = jnp.transpose(pair_rows, (0, 3, 1, 2, 4)).reshape(
        experts_count * shard_count, 1, capacity, feature_block
    )
    gathered_parts = lax.all_to_all(pair_rows, ("exp", "shard"), 0, 0, tiled=True)
    expert_out = (
        jnp.sum(
            gathered_parts.reshape(
                experts_count, shard_count // 2, 2, capacity, feature_block
            ).astype(jnp.float32),
            axis=1,
        )
        .astype(jnp.bfloat16)
    )
    moe_term = jnp.einsum(
        "jtnc,njcd->jtd", share_table, expert_out, preferred_element_type=jnp.float32
    )
    hidden_block = lax.dynamic_slice_in_dim(
        hidden_state, shard_index * feature_block, feature_block, 2
    )
    mixed_block = (hidden_block + moe_term).astype(jnp.bfloat16)
    mixed_out = jnp.transpose(
        gather_blocks(mixed_block, "shard", shard_count), (1, 2, 0, 3)
    ).reshape(members, tokens_here, width)
    return mixed_out


def solution(mesh):
    return jax.shard_map(
        on_device,
        mesh=mesh,
        in_specs=(
            P("req", "exp", None),
            P("req", "exp", None),
            P("req", "exp", None),
            P("req", "exp", None),
            P(),
            P("req", None),
            P("req", None),
            P("req", ("exp", "shard"), None, None),
            P("req", ("exp", "shard"), None, None),
            P(),
            P("shard", None),
            P("exp", None, "shard", None),
            P("exp", "shard", None),
        ),
        out_specs=P("req", "exp", None),
        check_vma=False,
    )
```

```python
import math

import jax
import jax.numpy as jnp
from jax import lax
from jax.experimental import pallas as pl
from jax.experimental.pallas import tpu as pltpu
from jax.sharding import PartitionSpec as P
import functools

H = 36


NEG_FILL = -1e30
EPSILON = 1e-06


def expert_rows(received, gate_up, down_proj):
    width = received.shape[-1]
    flat_rows = received.reshape(-1, width)
    both = lax.dot_general(
        flat_rows, gate_up[0], (((1,), (2,)), ((), ())), preferred_element_type=jnp.float32
    )
    active = (jax.nn.silu(both[:, 0]) * both[:, 1]).astype(jnp.bfloat16)
    partial_out = jnp.dot(active, down_proj[0], preferred_element_type=jnp.float32)
    return partial_out.reshape(received.shape)


def attend_kernel(heads, head_size, q_ref, k_ref, v_ref, mask_ref, ctx_ref, peak_ref, tot_ref):
    vis = mask_ref[...] != 0
    for h in range(heads):
        cols = slice(h * head_size, (h + 1) * head_size)
        q_h = q_ref[:, cols]
        k_h = k_ref[:, cols]
        s = lax.dot_general(q_h, k_h, (((1,), (1,)), ((), ())), preferred_element_type=jnp.float32)
        s = jnp.where(vis, s * (1.0 / math.sqrt(head_size)), NEG_FILL)
        m = jnp.max(s, axis=1, keepdims=True).astype(jnp.bfloat16).astype(jnp.float32)
        w = jnp.where(vis, jnp.exp(s - m), 0.0).astype(jnp.bfloat16)
        t = jnp.sum(w.astype(jnp.float32), axis=1, keepdims=True)
        c = jnp.dot(w, v_ref[:, cols], preferred_element_type=jnp.float32)
        ctx_ref[:, cols] = c
        peak_ref[:, h : h + 1] = m
        tot_ref[:, h : h + 1] = t

def attend(q, k, v, mask, heads):
    rows, width = q.shape
    head_size = width // heads
    return pl.pallas_call(
        functools.partial(attend_kernel, heads, head_size),
        out_shape=(
            jax.ShapeDtypeStruct((rows, width), jnp.float32),
            jax.ShapeDtypeStruct((rows, heads), jnp.float32),
            jax.ShapeDtypeStruct((rows, heads), jnp.float32),
        ),
        in_specs=[pl.BlockSpec(memory_space=pltpu.VMEM)] * 4,
        out_specs=[pl.BlockSpec(memory_space=pltpu.VMEM)] * 3,
    )(q, k, v, mask)


def gather_blocks(block, axis_name, count):
    spread = jnp.broadcast_to(block[None], (count,) + block.shape)
    return lax.all_to_all(spread, axis_name, 0, 0, tiled=False)


def on_device(
    query_stretch,
    resid_stretch,
    route_ids,
    route_probs,
    request_order,
    prior_pages,
    page_order,
    key_pool,
    value_pool,
    norm_gain,
    out_proj,
    gate_up,
    down_proj,
):
    members = prior_pages.shape[1]
    tokens_here = query_stretch.shape[1]
    width = query_stretch.shape[2]
    head_size = width // H
    group_index = lax.axis_index("req")
    exp_index = lax.axis_index("exp")
    shard_index = lax.axis_index("shard")
    shard_count = lax.axis_size("shard")
    experts_count = lax.axis_size("exp")
    extras = jnp.concatenate(
        [resid_stretch, route_probs, route_ids.astype(jnp.bfloat16)], axis=2
    )
    group_count = lax.axis_size("req")
    all_query = gather_blocks(query_stretch, "req", group_count).reshape(
        (-1,) + query_stretch.shape[1:]
    )
    all_extras = gather_blocks(extras, "req", group_count).reshape((-1,) + extras.shape[1:])
    served = lax.dynamic_slice_in_dim(request_order, group_index * members, members)
    served_query = jnp.take(all_query, served, axis=0)
    served_extras = jnp.take(all_extras, served, axis=0)
    core_index = shard_index % 2
    own_member = lax.dynamic_slice_in_dim(served_query, core_index, 1, 0)
    own_query = gather_blocks(own_member, "exp", experts_count)
    partner_query = lax.ppermute(
        own_query, "shard", [(i, i ^ 1) for i in range(shard_count)]
    )
    group_query = jnp.where(
        core_index == 0,
        jnp.concatenate([own_query, partner_query], axis=1),
        jnp.concatenate([partner_query, own_query], axis=1),
    )
    group_query, served_extras = lax.optimization_barrier((group_query, served_extras))
    top_count = route_ids.shape[2]
    served_resid = served_extras[:, :, :width]
    served_probs = served_extras[:, :, width : width + top_count]
    served_ids = served_extras[:, :, width + top_count :].astype(jnp.int32)
    pages_here = key_pool.shape[1]
    page_size = key_pool.shape[2]
    keys_here = pages_here * page_size
    device_index = exp_index * shard_count + shard_index
    physical = device_index * pages_here + jnp.arange(pages_here, dtype=jnp.int32)
    page_row = page_order[0]
    pool_size = page_row.shape[0]
    matched = page_row[None, :] == physical[:, None]
    located = jnp.sum(
        jnp.where(matched, jnp.arange(pool_size, dtype=jnp.int32)[None, :], 0), axis=1
    )
    prior_row = prior_pages[0]
    page_counts = prior_row + experts_count * tokens_here // page_size
    page_ends = jnp.cumsum(page_counts)
    page_starts = page_ends - page_counts
    owner_slot = jnp.sum((located[:, None] >= page_ends[None, :]).astype(jnp.int32), axis=1)
    owner_hot = owner_slot[:, None] == jnp.arange(members, dtype=jnp.int32)[None, :]
    logical = located - jnp.sum(jnp.where(owner_hot, page_starts[None, :], 0), axis=1)
    key_place = (
        logical[:, None] * page_size + jnp.arange(page_size, dtype=jnp.int32)[None, :]
    ).reshape(keys_here)
    key_owner = jnp.repeat(owner_slot, page_size)
    query_place = (
        prior_row[None, :, None] * page_size
        + jnp.arange(experts_count, dtype=jnp.int32)[:, None, None] * tokens_here
        + jnp.arange(tokens_here, dtype=jnp.int32)[None, None, :]
    )
    visible = (key_owner[None, None, None, :] == jnp.arange(members, dtype=jnp.int32)[None, :, None, None]) & (
        key_place[None, None, None, :] <= query_place[..., None]
    )
    attend_rows = experts_count * members * tokens_here
    context, peak_rows, total_rows = attend(
        group_query.reshape(attend_rows, width),
        key_pool[0].reshape(keys_here, width),
        value_pool[0].reshape(keys_here, width),
        visible.reshape(attend_rows, keys_here).astype(jnp.int32),
        H,
    )
    context = context.reshape(experts_count, members, tokens_here, width)
    half_width = width // 2
    half_heads = H // 2
    own_peak = peak_rows.reshape(experts_count, members, tokens_here, H)
    own_totals = lax.reduce_precision(
        total_rows.reshape(experts_count, members, tokens_here, H), 8, 7
    )
    head_of_column = jnp.arange(half_width, dtype=jnp.int32) // head_size
    widen_table = (
        jnp.arange(half_heads, dtype=jnp.int32)[:, None] == head_of_column[None, :]
    ).astype(jnp.float32)

    def widen(scale):
        return jnp.einsum(
            "...h,hc->...c", scale, widen_table, precision=lax.Precision.HIGHEST
        )

    keep_context = lax.dynamic_slice_in_dim(context, core_index * half_width, half_width, 3)
    give_context = lax.dynamic_slice_in_dim(
        context, (1 - core_index) * half_width, half_width, 3
    )
    message = jnp.concatenate(
        [
            give_context.astype(jnp.bfloat16),
            own_peak.astype(jnp.bfloat16),
            own_totals.astype(jnp.bfloat16),
        ],
        axis=3,
    )
    message = lax.ppermute(message, "shard", [(i, i ^ 1) for i in range(shard_count)])
    other_context = message[..., :half_width].astype(jnp.float32)
    other_peak = message[..., half_width : half_width + H].astype(jnp.float32)
    other_totals = message[..., half_width + H :].astype(jnp.float32)
    pair_peak = jnp.maximum(own_peak, other_peak)
    own_scale = jnp.exp(own_peak - pair_peak)
    other_scale = jnp.exp(other_peak - pair_peak)
    pair_totals = own_scale * own_totals + other_scale * other_totals

    def half_scale(scale):
        return widen(lax.dynamic_slice_in_dim(scale, core_index * half_heads, half_heads, 3))

    pair_context = half_scale(own_scale) * keep_context + half_scale(other_scale) * other_context
    packed = jnp.concatenate(
        [
            pair_context.astype(jnp.bfloat16),
            pair_peak.astype(jnp.bfloat16),
            pair_totals.astype(jnp.bfloat16),
        ],
        axis=3,
    )
    packed_width = packed.shape[3]
    rows_each = members * tokens_here // shard_count
    packed = packed.reshape(experts_count * shard_count, rows_each, packed_width)
    arrived = lax.all_to_all(packed, ("exp", "shard"), 0, 0, tiled=True)
    arrived = arrived.reshape(-1, 2, rows_each, packed_width)
    arrived_peak = arrived[:, 0, :, half_width : half_width + H].astype(jnp.float32)
    arrived_totals = arrived[:, 0, :, half_width + H :].astype(jnp.float32)
    row_peak = jnp.max(arrived_peak, axis=0)
    rescale = jnp.exp(arrived_peak - row_peak[None])
    row_totals = jnp.sum(rescale * arrived_totals, axis=0)
    row_halves = []
    for half in range(2):
        half_rescale = widen(rescale[:, :, half * half_heads : (half + 1) * half_heads])
        half_context = jnp.sum(
            half_rescale * arrived[:, half, :, :half_width].astype(jnp.float32), axis=0
        )
        half_totals = widen(row_totals[:, half * half_heads : (half + 1) * half_heads])
        row_halves.append(half_context / half_totals)
    row_attended = jnp.concatenate(row_halves, axis=1).astype(jnp.bfloat16)
    attended = gather_blocks(row_attended, "shard", shard_count).reshape(
        members, tokens_here, width
    )
    projected_part = lax.dot_general(
        attended, out_proj, (((2,), (1,)), ((), ())), preferred_element_type=jnp.float32
    ).astype(jnp.bfloat16)
    projected = jnp.transpose(
        gather_blocks(projected_part, "shard", shard_count), (1, 2, 0, 3)
    ).reshape(members, tokens_here, width)
    hidden_state = served_resid.astype(jnp.float32) + projected.astype(jnp.float32)
    mean_square = jnp.mean(hidden_state * hidden_state, axis=2, keepdims=True)
    normed = (hidden_state * lax.rsqrt(mean_square + EPSILON) * norm_gain).astype(jnp.bfloat16)
    capacity = min(tokens_here, max(2, 3 * tokens_here * top_count // (2 * experts_count)))
    flat_ids = served_ids.reshape(members, tokens_here * top_count)
    expert_hot = (
        flat_ids[:, :, None] == jnp.arange(experts_count, dtype=jnp.int32)[None, None, :]
    ).astype(jnp.int32)
    before = jnp.cumsum(expert_hot, axis=1) - expert_hot
    slot_place = jnp.sum(before * expert_hot, axis=2)
    slot_hot = (
        slot_place[:, :, None] == jnp.arange(capacity, dtype=jnp.int32)[None, None, :]
    ).astype(jnp.int32)
    place_table = (expert_hot[:, :, :, None] * slot_hot[:, :, None, :]).reshape(
        members, tokens_here, top_count, experts_count, capacity
    )
    pick_table = jnp.sum(place_table, axis=2).astype(jnp.bfloat16)
    sent_rows = jnp.einsum(
        "jtnc,jtd->njcd", pick_table, normed, preferred_element_type=jnp.float32
    ).astype(jnp.bfloat16)
    share_table = jnp.sum(
        place_table.astype(jnp.bfloat16) * served_probs[:, :, :, None, None], axis=2
    )
    own_rows = lax.all_to_all(
        lax.dynamic_slice_in_dim(sent_rows, core_index, 1, 1),
        "exp",
        split_axis=0,
        concat_axis=0,
        tiled=True,
    )
    partner_rows = lax.ppermute(own_rows, "shard", [(i, i ^ 1) for i in range(shard_count)])
    received_rows = jnp.where(
        core_index == 0,
        jnp.concatenate([own_rows, partner_rows], axis=1),
        jnp.concatenate([partner_rows, own_rows], axis=1),
    )
    partial_out = expert_rows(received_rows, gate_up, down_proj)
    feature_block = width // shard_count
    keep_rows = lax.dynamic_slice_in_dim(partial_out, core_index, 1, 1)
    give_rows = lax.dynamic_slice_in_dim(partial_out, 1 - core_index, 1, 1)
    pair_rows = keep_rows + lax.ppermute(
        give_rows, "shard", [(i, i ^ 1) for i in range(shard_count)]
    )
    pair_rows = pair_rows.astype(jnp.bfloat16).reshape(
        experts_count, 1, capacity, shard_count, feature_block
    )
    pair_rows = jnp.transpose(pair_rows, (0, 3, 1, 2, 4)).reshape(
        experts_count * shard_count, 1, capacity, feature_block
    )
    gathered_parts = lax.all_to_all(pair_rows, ("exp", "shard"), 0, 0, tiled=True)
    expert_out = (
        jnp.sum(
            gathered_parts.reshape(
                experts_count, shard_count // 2, 2, capacity, feature_block
            ).astype(jnp.float32),
            axis=1,
        )
        .astype(jnp.bfloat16)
    )
    moe_term = jnp.einsum(
        "jtnc,njcd->jtd", share_table, expert_out, preferred_element_type=jnp.float32
    )
    hidden_block = lax.dynamic_slice_in_dim(
        hidden_state, shard_index * feature_block, feature_block, 2
    )
    mixed_block = (hidden_block + moe_term).astype(jnp.bfloat16)
    mixed_out = jnp.transpose(
        gather_blocks(mixed_block, "shard", shard_count), (1, 2, 0, 3)
    ).reshape(members, tokens_here, width)
    return mixed_out


def solution(mesh):
    return jax.shard_map(
        on_device,
        mesh=mesh,
        in_specs=(
            P("req", "exp", None),
            P("req", "exp", None),
            P("req", "exp", None),
            P("req", "exp", None),
            P(),
            P("req", None),
            P("req", None),
            P("req", ("exp", "shard"), None, None),
            P("req", ("exp", "shard"), None, None),
            P(),
            P("shard", None),
            P("exp", None, "shard", None),
            P("exp", "shard", None),
        ),
        out_specs=P("req", "exp", None),
        check_vma=False,
    )
```

```python
import math

import jax
import jax.numpy as jnp
from jax import lax
from jax.experimental import pallas as pl
from jax.experimental.pallas import tpu as pltpu
from jax.sharding import PartitionSpec as P
import functools

H = 36


NEG_FILL = -1e30
EPSILON = 1e-06


def expert_rows(received, gate_up, down_proj):
    width = received.shape[-1]
    flat_rows = received.reshape(-1, width)
    both = lax.dot_general(
        flat_rows, gate_up[0], (((1,), (2,)), ((), ())), preferred_element_type=jnp.float32
    )
    active = (jax.nn.silu(both[:, 0]) * both[:, 1]).astype(jnp.bfloat16)
    partial_out = jnp.dot(active, down_proj[0], preferred_element_type=jnp.float32)
    return partial_out.reshape(received.shape)


def attend_kernel(heads, head_size, q_ref, k_ref, v_ref, mask_ref, ctx_ref, peak_ref, tot_ref):
    vis = mask_ref[...] != 0
    for h in range(heads):
        cols = slice(h * head_size, (h + 1) * head_size)
        q_h = q_ref[:, cols]
        s = jnp.dot(q_h, k_ref[cols, :], preferred_element_type=jnp.float32)
        s = jnp.where(vis, s * (1.0 / math.sqrt(head_size)), NEG_FILL)
        m = jnp.max(s, axis=1, keepdims=True).astype(jnp.bfloat16).astype(jnp.float32)
        w = jnp.where(vis, jnp.exp(s - m), 0.0).astype(jnp.bfloat16)
        t = jnp.sum(w.astype(jnp.float32), axis=1, keepdims=True)
        c = jnp.dot(w, v_ref[:, cols], preferred_element_type=jnp.float32)
        ctx_ref[:, cols] = c
        peak_ref[:, h : h + 1] = m
        tot_ref[:, h : h + 1] = t

def attend(q, k, v, mask, heads):
    rows, width = q.shape
    head_size = width // heads
    return pl.pallas_call(
        functools.partial(attend_kernel, heads, head_size),
        out_shape=(
            jax.ShapeDtypeStruct((rows, width), jnp.float32),
            jax.ShapeDtypeStruct((rows, heads), jnp.float32),
            jax.ShapeDtypeStruct((rows, heads), jnp.float32),
        ),
        in_specs=[pl.BlockSpec(memory_space=pltpu.VMEM)] * 4,
        out_specs=[pl.BlockSpec(memory_space=pltpu.VMEM)] * 3,
    )(q, k, v, mask)


def gather_blocks(block, axis_name, count):
    spread = jnp.broadcast_to(block[None], (count,) + block.shape)
    return lax.all_to_all(spread, axis_name, 0, 0, tiled=False)


def on_device(
    query_stretch,
    resid_stretch,
    route_ids,
    route_probs,
    request_order,
    prior_pages,
    page_order,
    key_pool,
    value_pool,
    norm_gain,
    out_proj,
    gate_up,
    down_proj,
):
    members = prior_pages.shape[1]
    tokens_here = query_stretch.shape[1]
    width = query_stretch.shape[2]
    head_size = width // H
    group_index = lax.axis_index("req")
    exp_index = lax.axis_index("exp")
    shard_index = lax.axis_index("shard")
    shard_count = lax.axis_size("shard")
    experts_count = lax.axis_size("exp")
    extras = jnp.concatenate(
        [resid_stretch, route_probs, route_ids.astype(jnp.bfloat16)], axis=2
    )
    all_query = lax.all_gather(query_stretch, "req", axis=0, tiled=True)
    all_extras = lax.all_gather(extras, "req", axis=0, tiled=True)
    served = lax.dynamic_slice_in_dim(request_order, group_index * members, members)
    served_query = jnp.take(all_query, served, axis=0)
    served_extras = jnp.take(all_extras, served, axis=0)
    core_index = shard_index % 2
    own_member = lax.dynamic_slice_in_dim(served_query, core_index, 1, 0)
    own_query = gather_blocks(own_member, "exp", experts_count)
    partner_query = lax.ppermute(
        own_query, "shard", [(i, i ^ 1) for i in range(shard_count)]
    )
    group_query = jnp.where(
        core_index == 0,
        jnp.concatenate([own_query, partner_query], axis=1),
        jnp.concatenate([partner_query, own_query], axis=1),
    )
    group_query, served_extras = lax.optimization_barrier((group_query, served_extras))
    top_count = route_ids.shape[2]
    served_resid = served_extras[:, :, :width]
    served_probs = served_extras[:, :, width : width + top_count]
    served_ids = served_extras[:, :, width + top_count :].astype(jnp.int32)
    pages_here = key_pool.shape[1]
    page_size = key_pool.shape[2]
    keys_here = pages_here * page_size
    device_index = exp_index * shard_count + shard_index
    physical = device_index * pages_here + jnp.arange(pages_here, dtype=jnp.int32)
    page_row = page_order[0]
    pool_size = page_row.shape[0]
    matched = page_row[None, :] == physical[:, None]
    located = jnp.sum(
        jnp.where(matched, jnp.arange(pool_size, dtype=jnp.int32)[None, :], 0), axis=1
    )
    prior_row = prior_pages[0]
    page_counts = prior_row + experts_count * tokens_here // page_size
    page_ends = jnp.cumsum(page_counts)
    page_starts = page_ends - page_counts
    owner_slot = jnp.sum((located[:, None] >= page_ends[None, :]).astype(jnp.int32), axis=1)
    owner_hot = owner_slot[:, None] == jnp.arange(members, dtype=jnp.int32)[None, :]
    logical = located - jnp.sum(jnp.where(owner_hot, page_starts[None, :], 0), axis=1)
    key_place = (
        logical[:, None] * page_size + jnp.arange(page_size, dtype=jnp.int32)[None, :]
    ).reshape(keys_here)
    key_owner = jnp.repeat(owner_slot, page_size)
    query_place = (
        prior_row[None, :, None] * page_size
        + jnp.arange(experts_count, dtype=jnp.int32)[:, None, None] * tokens_here
        + jnp.arange(tokens_here, dtype=jnp.int32)[None, None, :]
    )
    visible = (key_owner[None, None, None, :] == jnp.arange(members, dtype=jnp.int32)[None, :, None, None]) & (
        key_place[None, None, None, :] <= query_place[..., None]
    )
    attend_rows = experts_count * members * tokens_here
    context, peak_rows, total_rows = attend(
        group_query.reshape(attend_rows, width),
        jnp.transpose(key_pool[0].reshape(keys_here, width)),
        value_pool[0].reshape(keys_here, width),
        visible.reshape(attend_rows, keys_here).astype(jnp.int32),
        H,
    )
    context = context.reshape(experts_count, members, tokens_here, width)
    half_width = width // 2
    half_heads = H // 2
    own_peak = peak_rows.reshape(experts_count, members, tokens_here, H)
    own_totals = lax.reduce_precision(
        total_rows.reshape(experts_count, members, tokens_here, H), 8, 7
    )
    head_of_column = jnp.arange(half_width, dtype=jnp.int32) // head_size
    widen_table = (
        jnp.arange(half_heads, dtype=jnp.int32)[:, None] == head_of_column[None, :]
    ).astype(jnp.float32)

    def widen(scale):
        return jnp.einsum(
            "...h,hc->...c", scale, widen_table, precision=lax.Precision.HIGHEST
        )

    keep_context = lax.dynamic_slice_in_dim(context, core_index * half_width, half_width, 3)
    give_context = lax.dynamic_slice_in_dim(
        context, (1 - core_index) * half_width, half_width, 3
    )
    message = jnp.concatenate(
        [
            give_context.astype(jnp.bfloat16),
            own_peak.astype(jnp.bfloat16),
            own_totals.astype(jnp.bfloat16),
        ],
        axis=3,
    )
    message = lax.ppermute(message, "shard", [(i, i ^ 1) for i in range(shard_count)])
    other_context = message[..., :half_width].astype(jnp.float32)
    other_peak = message[..., half_width : half_width + H].astype(jnp.float32)
    other_totals = message[..., half_width + H :].astype(jnp.float32)
    pair_peak = jnp.maximum(own_peak, other_peak)
    own_scale = jnp.exp(own_peak - pair_peak)
    other_scale = jnp.exp(other_peak - pair_peak)
    pair_totals = own_scale * own_totals + other_scale * other_totals

    def half_scale(scale):
        return widen(lax.dynamic_slice_in_dim(scale, core_index * half_heads, half_heads, 3))

    pair_context = half_scale(own_scale) * keep_context + half_scale(other_scale) * other_context
    packed = jnp.concatenate(
        [
            pair_context.astype(jnp.bfloat16),
            pair_peak.astype(jnp.bfloat16),
            pair_totals.astype(jnp.bfloat16),
        ],
        axis=3,
    )
    packed_width = packed.shape[3]
    rows_each = members * tokens_here // shard_count
    packed = packed.reshape(experts_count * shard_count, rows_each, packed_width)
    arrived = lax.all_to_all(packed, ("exp", "shard"), 0, 0, tiled=True)
    arrived = arrived.reshape(-1, 2, rows_each, packed_width)
    arrived_peak = arrived[:, 0, :, half_width : half_width + H].astype(jnp.float32)
    arrived_totals = arrived[:, 0, :, half_width + H :].astype(jnp.float32)
    row_peak = jnp.max(arrived_peak, axis=0)
    rescale = jnp.exp(arrived_peak - row_peak[None])
    row_totals = jnp.sum(rescale * arrived_totals, axis=0)
    row_halves = []
    for half in range(2):
        half_rescale = widen(rescale[:, :, half * half_heads : (half + 1) * half_heads])
        half_context = jnp.sum(
            half_rescale * arrived[:, half, :, :half_width].astype(jnp.float32), axis=0
        )
        half_totals = widen(row_totals[:, half * half_heads : (half + 1) * half_heads])
        row_halves.append(half_context / half_totals)
    row_attended = jnp.concatenate(row_halves, axis=1).astype(jnp.bfloat16)
    attended = gather_blocks(row_attended, "shard", shard_count).reshape(
        members, tokens_here, width
    )
    projected_part = lax.dot_general(
        attended, out_proj, (((2,), (1,)), ((), ())), preferred_element_type=jnp.float32
    ).astype(jnp.bfloat16)
    projected = jnp.transpose(
        gather_blocks(projected_part, "shard", shard_count), (1, 2, 0, 3)
    ).reshape(members, tokens_here, width)
    hidden_state = served_resid.astype(jnp.float32) + projected.astype(jnp.float32)
    mean_square = jnp.mean(hidden_state * hidden_state, axis=2, keepdims=True)
    normed = (hidden_state * lax.rsqrt(mean_square + EPSILON) * norm_gain).astype(jnp.bfloat16)
    capacity = min(tokens_here, max(2, 3 * tokens_here * top_count // (2 * experts_count)))
    flat_ids = served_ids.reshape(members, tokens_here * top_count)
    expert_hot = (
        flat_ids[:, :, None] == jnp.arange(experts_count, dtype=jnp.int32)[None, None, :]
    ).astype(jnp.int32)
    before = jnp.cumsum(expert_hot, axis=1) - expert_hot
    slot_place = jnp.sum(before * expert_hot, axis=2)
    slot_hot = (
        slot_place[:, :, None] == jnp.arange(capacity, dtype=jnp.int32)[None, None, :]
    ).astype(jnp.int32)
    place_table = (expert_hot[:, :, :, None] * slot_hot[:, :, None, :]).reshape(
        members, tokens_here, top_count, experts_count, capacity
    )
    pick_table = jnp.sum(place_table, axis=2).astype(jnp.bfloat16)
    sent_rows = jnp.einsum(
        "jtnc,jtd->njcd", pick_table, normed, preferred_element_type=jnp.float32
    ).astype(jnp.bfloat16)
    share_table = jnp.sum(
        place_table.astype(jnp.bfloat16) * served_probs[:, :, :, None, None], axis=2
    )
    own_rows = lax.all_to_all(
        lax.dynamic_slice_in_dim(sent_rows, core_index, 1, 1),
        "exp",
        split_axis=0,
        concat_axis=0,
        tiled=True,
    )
    partner_rows = lax.ppermute(own_rows, "shard", [(i, i ^ 1) for i in range(shard_count)])
    received_rows = jnp.where(
        core_index == 0,
        jnp.concatenate([own_rows, partner_rows], axis=1),
        jnp.concatenate([partner_rows, own_rows], axis=1),
    )
    partial_out = expert_rows(received_rows, gate_up, down_proj)
    feature_block = width // shard_count
    keep_rows = lax.dynamic_slice_in_dim(partial_out, core_index, 1, 1)
    give_rows = lax.dynamic_slice_in_dim(partial_out, 1 - core_index, 1, 1)
    pair_rows = keep_rows + lax.ppermute(
        give_rows, "shard", [(i, i ^ 1) for i in range(shard_count)]
    )
    pair_rows = pair_rows.astype(jnp.bfloat16).reshape(
        experts_count, 1, capacity, shard_count, feature_block
    )
    pair_rows = jnp.transpose(pair_rows, (0, 3, 1, 2, 4)).reshape(
        experts_count * shard_count, 1, capacity, feature_block
    )
    gathered_parts = lax.all_to_all(pair_rows, ("exp", "shard"), 0, 0, tiled=True)
    expert_out = (
        jnp.sum(
            gathered_parts.reshape(
                experts_count, shard_count // 2, 2, capacity, feature_block
            ).astype(jnp.float32),
            axis=1,
        )
        .astype(jnp.bfloat16)
    )
    moe_term = jnp.einsum(
        "jtnc,njcd->jtd", share_table, expert_out, preferred_element_type=jnp.float32
    )
    hidden_block = lax.dynamic_slice_in_dim(
        hidden_state, shard_index * feature_block, feature_block, 2
    )
    mixed_block = (hidden_block + moe_term).astype(jnp.bfloat16)
    mixed_out = jnp.transpose(
        gather_blocks(mixed_block, "shard", shard_count), (1, 2, 0, 3)
    ).reshape(members, tokens_here, width)
    return mixed_out


def solution(mesh):
    return jax.shard_map(
        on_device,
        mesh=mesh,
        in_specs=(
            P("req", "exp", None),
            P("req", "exp", None),
            P("req", "exp", None),
            P("req", "exp", None),
            P(),
            P("req", None),
            P("req", None),
            P("req", ("exp", "shard"), None, None),
            P("req", ("exp", "shard"), None, None),
            P(),
            P("shard", None),
            P("exp", None, "shard", None),
            P("exp", "shard", None),
        ),
        out_specs=P("req", "exp", None),
        check_vma=False,
    )
```

```python
import math

import jax
import jax.numpy as jnp
from jax import lax
from jax.experimental import pallas as pl
from jax.experimental.pallas import tpu as pltpu
from jax.sharding import PartitionSpec as P
import functools

H = 36


NEG_FILL = -1e30
EPSILON = 1e-06


def expert_rows(received, gate_up, down_proj):
    width = received.shape[-1]
    flat_rows = received.reshape(-1, width)
    both = lax.dot_general(
        flat_rows, gate_up[0], (((1,), (2,)), ((), ())), preferred_element_type=jnp.float32
    )
    active = (jax.nn.silu(both[:, 0]) * both[:, 1]).astype(jnp.bfloat16)
    partial_out = jnp.dot(active, down_proj[0], preferred_element_type=jnp.float32)
    return partial_out.reshape(received.shape)


def attend_kernel(heads, head_size, q_ref, k_ref, v_ref, mask_ref, ctx_ref, peak_ref, tot_ref):
    vis = mask_ref[...] != 0
    for h in range(heads):
        cols = slice(h * head_size, (h + 1) * head_size)
        q_h = q_ref[:, cols]
        k_h = k_ref[:, cols]
        s = lax.dot_general(q_h, k_h, (((1,), (1,)), ((), ())), preferred_element_type=jnp.float32)
        s = jnp.where(vis, s * (1.0 / math.sqrt(head_size)), NEG_FILL)
        m = jnp.max(s, axis=1, keepdims=True).astype(jnp.bfloat16).astype(jnp.float32)
        w = jnp.where(vis, jnp.exp(s - m), 0.0).astype(jnp.bfloat16)
        t = jnp.sum(w.astype(jnp.float32), axis=1, keepdims=True)
        c = jnp.dot(w, v_ref[:, cols], preferred_element_type=jnp.float32)
        ctx_ref[:, cols] = c
        peak_ref[:, h : h + 1] = m
        tot_ref[:, h : h + 1] = t

def attend(q, k, v, mask, heads):
    rows, width = q.shape
    head_size = width // heads
    return pl.pallas_call(
        functools.partial(attend_kernel, heads, head_size),
        out_shape=(
            jax.ShapeDtypeStruct((rows, width), jnp.float32),
            jax.ShapeDtypeStruct((rows, heads), jnp.float32),
            jax.ShapeDtypeStruct((rows, heads), jnp.float32),
        ),
        in_specs=[pl.BlockSpec(memory_space=pltpu.VMEM)] * 4,
        out_specs=[pl.BlockSpec(memory_space=pltpu.VMEM)] * 3,
    )(q, k, v, mask)


def gather_blocks(block, axis_name, count):
    spread = jnp.broadcast_to(block[None], (count,) + block.shape)
    return lax.all_to_all(spread, axis_name, 0, 0, tiled=False)


def on_device(
    query_stretch,
    resid_stretch,
    route_ids,
    route_probs,
    request_order,
    prior_pages,
    page_order,
    key_pool,
    value_pool,
    norm_gain,
    out_proj,
    gate_up,
    down_proj,
):
    members = prior_pages.shape[1]
    tokens_here = query_stretch.shape[1]
    width = query_stretch.shape[2]
    head_size = width // H
    group_index = lax.axis_index("req")
    exp_index = lax.axis_index("exp")
    shard_index = lax.axis_index("shard")
    shard_count = lax.axis_size("shard")
    experts_count = lax.axis_size("exp")
    extras = jnp.concatenate(
        [resid_stretch, route_probs, route_ids.astype(jnp.bfloat16)], axis=2
    )
    all_query = lax.all_gather(query_stretch, "req", axis=0, tiled=True)
    all_extras = lax.all_gather(extras, "req", axis=0, tiled=True)
    served = lax.dynamic_slice_in_dim(request_order, group_index * members, members)
    served_query = jnp.take(all_query, served, axis=0)
    served_extras = jnp.take(all_extras, served, axis=0)
    core_index = shard_index % 2
    own_member = lax.dynamic_slice_in_dim(served_query, core_index, 1, 0)
    own_query = gather_blocks(own_member, "exp", experts_count)
    partner_query = lax.ppermute(
        own_query, "shard", [(i, i ^ 1) for i in range(shard_count)]
    )
    group_query = jnp.where(
        core_index == 0,
        jnp.concatenate([own_query, partner_query], axis=1),
        jnp.concatenate([partner_query, own_query], axis=1),
    )
    top_count = route_ids.shape[2]
    served_resid = served_extras[:, :, :width]
    served_probs = served_extras[:, :, width : width + top_count]
    served_ids = served_extras[:, :, width + top_count :].astype(jnp.int32)
    pages_here = key_pool.shape[1]
    page_size = key_pool.shape[2]
    keys_here = pages_here * page_size
    device_index = exp_index * shard_count + shard_index
    physical = device_index * pages_here + jnp.arange(pages_here, dtype=jnp.int32)
    page_row = page_order[0]
    pool_size = page_row.shape[0]
    matched = page_row[None, :] == physical[:, None]
    located = jnp.sum(
        jnp.where(matched, jnp.arange(pool_size, dtype=jnp.int32)[None, :], 0), axis=1
    )
    prior_row = prior_pages[0]
    page_counts = prior_row + experts_count * tokens_here // page_size
    page_ends = jnp.cumsum(page_counts)
    page_starts = page_ends - page_counts
    owner_slot = jnp.sum((located[:, None] >= page_ends[None, :]).astype(jnp.int32), axis=1)
    owner_hot = owner_slot[:, None] == jnp.arange(members, dtype=jnp.int32)[None, :]
    logical = located - jnp.sum(jnp.where(owner_hot, page_starts[None, :], 0), axis=1)
    key_place = (
        logical[:, None] * page_size + jnp.arange(page_size, dtype=jnp.int32)[None, :]
    ).reshape(keys_here)
    key_owner = jnp.repeat(owner_slot, page_size)
    query_place = (
        prior_row[None, :, None] * page_size
        + jnp.arange(experts_count, dtype=jnp.int32)[:, None, None] * tokens_here
        + jnp.arange(tokens_here, dtype=jnp.int32)[None, None, :]
    )
    visible = (key_owner[None, None, None, :] == jnp.arange(members, dtype=jnp.int32)[None, :, None, None]) & (
        key_place[None, None, None, :] <= query_place[..., None]
    )
    attend_rows = experts_count * members * tokens_here
    context, peak_rows, total_rows = attend(
        group_query.reshape(attend_rows, width),
        key_pool[0].reshape(keys_here, width),
        value_pool[0].reshape(keys_here, width),
        visible.reshape(attend_rows, keys_here).astype(jnp.int32),
        H,
    )
    context = context.reshape(experts_count, members, tokens_here, width)
    half_width = width // 2
    half_heads = H // 2
    own_peak = peak_rows.reshape(experts_count, members, tokens_here, H)
    own_totals = lax.reduce_precision(
        total_rows.reshape(experts_count, members, tokens_here, H), 8, 7
    )
    head_of_column = jnp.arange(half_width, dtype=jnp.int32) // head_size
    widen_table = (
        jnp.arange(half_heads, dtype=jnp.int32)[:, None] == head_of_column[None, :]
    ).astype(jnp.float32)

    def widen(scale):
        return jnp.einsum(
            "...h,hc->...c", scale, widen_table, precision=lax.Precision.HIGHEST
        )

    keep_context = lax.dynamic_slice_in_dim(context, core_index * half_width, half_width, 3)
    give_context = lax.dynamic_slice_in_dim(
        context, (1 - core_index) * half_width, half_width, 3
    )
    message = jnp.concatenate(
        [
            give_context.astype(jnp.bfloat16),
            own_peak.astype(jnp.bfloat16),
            own_totals.astype(jnp.bfloat16),
        ],
        axis=3,
    )
    message = lax.ppermute(message, "shard", [(i, i ^ 1) for i in range(shard_count)])
    other_context = message[..., :half_width].astype(jnp.float32)
    other_peak = message[..., half_width : half_width + H].astype(jnp.float32)
    other_totals = message[..., half_width + H :].astype(jnp.float32)
    pair_peak = jnp.maximum(own_peak, other_peak)
    own_scale = jnp.exp(own_peak - pair_peak)
    other_scale = jnp.exp(other_peak - pair_peak)
    pair_totals = own_scale * own_totals + other_scale * other_totals

    def half_scale(scale):
        return widen(lax.dynamic_slice_in_dim(scale, core_index * half_heads, half_heads, 3))

    pair_context = half_scale(own_scale) * keep_context + half_scale(other_scale) * other_context
    packed = jnp.concatenate(
        [
            pair_context.astype(jnp.bfloat16),
            pair_peak.astype(jnp.bfloat16),
            pair_totals.astype(jnp.bfloat16),
        ],
        axis=3,
    )
    packed_width = packed.shape[3]
    rows_each = members * tokens_here // shard_count
    packed = packed.reshape(experts_count * shard_count, rows_each, packed_width)
    arrived = lax.all_to_all(packed, ("exp", "shard"), 0, 0, tiled=True)
    arrived = arrived.reshape(-1, 2, rows_each, packed_width)
    arrived_peak = arrived[:, 0, :, half_width : half_width + H].astype(jnp.float32)
    arrived_totals = arrived[:, 0, :, half_width + H :].astype(jnp.float32)
    row_peak = jnp.max(arrived_peak, axis=0)
    rescale = jnp.exp(arrived_peak - row_peak[None])
    row_totals = jnp.sum(rescale * arrived_totals, axis=0)
    row_halves = []
    for half in range(2):
        half_rescale = widen(rescale[:, :, half * half_heads : (half + 1) * half_heads])
        half_context = jnp.sum(
            half_rescale * arrived[:, half, :, :half_width].astype(jnp.float32), axis=0
        )
        half_totals = widen(row_totals[:, half * half_heads : (half + 1) * half_heads])
        row_halves.append(half_context / half_totals)
    row_attended = jnp.concatenate(row_halves, axis=1).astype(jnp.bfloat16)
    attended = gather_blocks(row_attended, "shard", shard_count).reshape(
        members, tokens_here, width
    )
    projected_part = lax.dot_general(
        attended, out_proj, (((2,), (1,)), ((), ())), preferred_element_type=jnp.float32
    ).astype(jnp.bfloat16)
    projected = jnp.transpose(
        gather_blocks(projected_part, "shard", shard_count), (1, 2, 0, 3)
    ).reshape(members, tokens_here, width)
    hidden_state = served_resid.astype(jnp.float32) + projected.astype(jnp.float32)
    mean_square = jnp.mean(hidden_state * hidden_state, axis=2, keepdims=True)
    normed = (hidden_state * lax.rsqrt(mean_square + EPSILON) * norm_gain).astype(jnp.bfloat16)
    capacity = min(tokens_here, max(2, 3 * tokens_here * top_count // (2 * experts_count)))
    flat_ids = served_ids.reshape(members, tokens_here * top_count)
    expert_hot = (
        flat_ids[:, :, None] == jnp.arange(experts_count, dtype=jnp.int32)[None, None, :]
    ).astype(jnp.int32)
    before = jnp.cumsum(expert_hot, axis=1) - expert_hot
    slot_place = jnp.sum(before * expert_hot, axis=2)
    slot_hot = (
        slot_place[:, :, None] == jnp.arange(capacity, dtype=jnp.int32)[None, None, :]
    ).astype(jnp.int32)
    place_table = (expert_hot[:, :, :, None] * slot_hot[:, :, None, :]).reshape(
        members, tokens_here, top_count, experts_count, capacity
    )
    pick_table = jnp.sum(place_table, axis=2).astype(jnp.bfloat16)
    sent_rows = jnp.einsum(
        "jtnc,jtd->njcd", pick_table, normed, preferred_element_type=jnp.float32
    ).astype(jnp.bfloat16)
    share_table = jnp.sum(
        place_table.astype(jnp.bfloat16) * served_probs[:, :, :, None, None], axis=2
    )
    own_rows = lax.all_to_all(
        lax.dynamic_slice_in_dim(sent_rows, core_index, 1, 1),
        "exp",
        split_axis=0,
        concat_axis=0,
        tiled=True,
    )
    partner_rows = lax.ppermute(own_rows, "shard", [(i, i ^ 1) for i in range(shard_count)])
    received_rows = jnp.where(
        core_index == 0,
        jnp.concatenate([own_rows, partner_rows], axis=1),
        jnp.concatenate([partner_rows, own_rows], axis=1),
    )
    partial_out = expert_rows(received_rows, gate_up, down_proj)
    feature_block = width // shard_count
    keep_rows = lax.dynamic_slice_in_dim(partial_out, core_index, 1, 1)
    give_rows = lax.dynamic_slice_in_dim(partial_out, 1 - core_index, 1, 1)
    pair_rows = keep_rows + lax.ppermute(
        give_rows, "shard", [(i, i ^ 1) for i in range(shard_count)]
    )
    pair_rows = pair_rows.astype(jnp.bfloat16).reshape(
        experts_count, 1, capacity, shard_count, feature_block
    )
    pair_rows = jnp.transpose(pair_rows, (0, 3, 1, 2, 4)).reshape(
        experts_count * shard_count, 1, capacity, feature_block
    )
    gathered_parts = lax.all_to_all(pair_rows, ("exp", "shard"), 0, 0, tiled=True)
    expert_out = (
        jnp.sum(
            gathered_parts.reshape(
                experts_count, shard_count // 2, 2, capacity, feature_block
            ).astype(jnp.float32),
            axis=1,
        )
        .astype(jnp.bfloat16)
    )
    moe_term = jnp.einsum(
        "jtnc,njcd->jtd", share_table, expert_out, preferred_element_type=jnp.float32
    )
    hidden_block = lax.dynamic_slice_in_dim(
        hidden_state, shard_index * feature_block, feature_block, 2
    )
    mixed_block = (hidden_block + moe_term).astype(jnp.bfloat16)
    mixed_out = jnp.transpose(
        gather_blocks(mixed_block, "shard", shard_count), (1, 2, 0, 3)
    ).reshape(members, tokens_here, width)
    return mixed_out


def solution(mesh):
    return jax.shard_map(
        on_device,
        mesh=mesh,
        in_specs=(
            P("req", "exp", None),
            P("req", "exp", None),
            P("req", "exp", None),
            P("req", "exp", None),
            P(),
            P("req", None),
            P("req", None),
            P("req", ("exp", "shard"), None, None),
            P("req", ("exp", "shard"), None, None),
            P(),
            P("shard", None),
            P("exp", None, "shard", None),
            P("exp", "shard", None),
        ),
        out_specs=P("req", "exp", None),
        check_vma=False,
    )
```
